512 devices in a mesh: spec: 32 (over x, y), tile: 16 (over z, core).
Axes of the slice: x: 4, y: 8, z: 8, core: 2. Of those that a mesh axis runs over, the one named last changes fastest.
Arguments:
- spectrum: float32 [1152, 64, 2048], P('spec', None, 'tile'), may hold values from 0.1 to 2
- depth_speed: float32 [64, 2048], P(None, 'tile'), may hold values from 0.5 to 1
- turning: float32 [64, 2048], P(None, 'tile'), may hold values from -0.5 to 0.5
- drift: float32 [1152], replicated, may hold values from -0.4 to 0.4
- partners: int32 [2, 1152], replicated, may hold values from 0 to 1151, as said below
- sea_slots: int32 [32, 16, 192], P(None, 'tile'), may hold values from 0 to 255, as said below
- sea_counts: int32 [32, 16], P(None, 'tile'), may hold values from 64 to 192
Outputs:
- new_spectrum: float32 [1152, 64, 2048], P(None, 'spec', 'tile')
The draws below stay inside these ranges and needn't reach their ends.
Inputs may be any that keep to these rules, and one draw needn't show every extreme that they name: partners[0, k] and partners[1, k] for k = f * 36 + d are components of frequency min(f + a_f, 31) and max(f - b_f, 0) and directions (d + c_f) and (d - e_f) modulo 36, with a_f, b_f, c_f, e_f between 1 and 3 and fixed for each frequency. sea_slots[j, t] names 192 distinct cells of block (j, t); its first sea_counts[j, t] entries are the block's sea cells, the others are land cells.
All inputs are finite; a program needn't handle non-finite values.
Results may differ from the reference program's by a relative error of at most 0.000075.
Values sent between devices are 32-bit elements; how exact they have to be, the bound alone decides.
No kernel may reach another device: no remote copies, remote signals or barrier semaphores. Data moves between devices by JAX's collectives and lax.ppermute only.
A program may use at most 64 MiB of HBM per device.

```python
import math
import jax
import jax.numpy as jnp
from jax import lax

ND = 36
NF = 32
X_DEV = 2
CY = 128
K = 1152
NX = 64
NY = 2048
ROW_BLOCKS = 32
TILES = 16
CAP = 192


def sea_layout(key):
    blocks = ROW_BLOCKS * TILES
    per_block = X_DEV * CY
    block_keys = jax.random.split(jax.random.fold_in(key, 11), blocks)
    shuffles = jax.vmap(lambda sub_key: jax.random.permutation(sub_key, per_block))(block_keys)
    sea_list = shuffles[:, :CAP].astype(jnp.int32)
    key_a, key_b, key_c = jax.random.split(jax.random.fold_in(key, 12), 3)
    sea_total = jax.random.randint(key_a, (blocks,), CAP // 3, CAP + 1)
    full_block = jax.random.randint(key_b, (), 0, blocks)
    thin_block = (full_block + 1 + jax.random.randint(key_c, (), 0, blocks - 1)) % blocks
    sea_total = sea_total.at[full_block].set(CAP).at[thin_block].set(CAP // 3)
    return (sea_list.reshape(ROW_BLOCKS, TILES, CAP), sea_total.reshape(ROW_BLOCKS, TILES).astype(jnp.int32))


def draw_sea_slots(key, part):
    return sea_layout(key)[0]


def draw_sea_counts(key, part):
    return sea_layout(key)[1]


def draw_partners(key, part):
    key_a, key_b, key_c, key_d = jax.random.split(jax.random.fold_in(key, 21), 4)
    freq_ids = jnp.arange(NF, dtype=jnp.int32)
    dir_ids = jnp.arange(ND, dtype=jnp.int32)
    upper_freq = jnp.minimum(freq_ids + jax.random.randint(key_a, (NF,), 1, 4), NF - 1)
    lower_freq = jnp.maximum(freq_ids - jax.random.randint(key_b, (NF,), 1, 4), 0)
    upper_turn = jax.random.randint(key_c, (NF,), 1, 4)
    lower_turn = jax.random.randint(key_d, (NF,), 1, 4)
    plus_ids = upper_freq[:, None] * ND + (dir_ids[None, :] + upper_turn[:, None]) % ND
    minus_ids = lower_freq[:, None] * ND + (dir_ids[None, :] - lower_turn[:, None]) % ND
    return jnp.stack([plus_ids.reshape(-1), minus_ids.reshape(-1)]).astype(jnp.int32)


def block_levels(key, dims, shards, low, high):
    gain, own = 1.0, jax.random.fold_in(key, 6)
    for position, parts in shards:
        draws = jnp.exp(jax.random.uniform(jax.random.fold_in(own, position), (parts,), jnp.float32, low / len(shards), high / len(shards)))
        gain = gain * jnp.repeat(draws, dims[position] // parts).reshape([-1 if axis == position else 1 for axis in range(len(dims))])
    return gain


def setup_inputs(seed: int = 0) -> dict:
    seeds = jax.random.split(jax.random.key(seed), 8)
    spectrum = jnp.clip(jnp.exp(math.log(2.0) - 2.9957323 * jax.random.uniform(seeds[0], (K, NX, NY), jnp.float32) ** block_levels(seeds[0], (K, NX, NY), ((0, 32), (2, 16)), -0.2, 0.2)), 0.1, 2.0)
    depth_speed = jnp.clip(0.5 + 0.5 * jax.random.uniform(seeds[1], (NX, NY), jnp.float32) ** block_levels(seeds[1], (NX, NY), ((1, 16),), -0.2, 0.2), 0.5, 1.0)
    turning = jnp.clip(jax.random.uniform(seeds[2], (NX, NY), jnp.float32, -0.5, 0.5) * block_levels(seeds[2], (NX, NY), ((1, 16),), -0.4, 0.0), -0.5, 0.5)
    drift = jnp.clip(jax.random.uniform(seeds[3], (K,), jnp.float32, -0.4, 0.4), -0.4, 0.4)
    partners = draw_partners(jax.random.fold_in(seeds[7], 71), 0)
    sea_slots = draw_sea_slots(jax.random.fold_in(seeds[7], 71), 0)
    sea_counts = draw_sea_counts(jax.random.fold_in(seeds[7], 71), 0)
    return dict(spectrum=spectrum, depth_speed=depth_speed, turning=turning, drift=drift, partners=partners, sea_slots=sea_slots, sea_counts=sea_counts)


speed_top = 0.6
decline = 0.0953102
dia_coeff = 0.25


def sea_cells(sea_list, sea_total, per_block):
    cell_ids = jnp.arange(per_block, dtype=jnp.int32)
    slot_rank = jnp.arange(sea_list.shape[1], dtype=jnp.int32)
    is_live = slot_rank[None, :] < sea_total[:, None]
    matches = (sea_list[:, :, None] == cell_ids[None, None, :]) & is_live[:, :, None]
    return jnp.any(matches, axis=1).astype(jnp.float32)


def advect_space(energy_ext, depth_ext, speeds, cosines, sine_part, sea_mask):
    east_rate = (speeds * cosines)[:, None, None] * depth_ext[None]
    north_rate = (speeds * sine_part)[:, None, None] * depth_ext[None, :, 1:-1]
    centre = energy_ext[:, :, 1:-1]
    east_mid = east_rate[:, :, 1:-1]
    inflow = jnp.maximum(east_rate[:, :, :-2], 0.0) * energy_ext[:, :, :-2] + jnp.maximum(-east_rate[:, :, 2:], 0.0) * energy_ext[:, :, 2:]
    empty_row = jnp.zeros_like(centre[:, :1])
    from_south = jnp.concatenate([empty_row, (jnp.maximum(north_rate, 0.0) * centre)[:, :-1]], axis=1)
    from_north = jnp.concatenate([(jnp.maximum(-north_rate, 0.0) * centre)[:, 1:], empty_row], axis=1)
    updated = centre - (jnp.abs(east_mid) + jnp.abs(north_rate)) * centre + inflow + from_south + from_north
    return updated * sea_mask


def advect_direction(energy, turning):
    turn_plus = jnp.maximum(turning, 0.0)
    behind = jnp.maximum(-turning, 0.0)
    return energy - jnp.abs(turning) * energy + turn_plus * jnp.roll(energy, 1, axis=1) + behind * jnp.roll(energy, -1, axis=1)


def advect_frequency(energy, drift, n_freq, n_dir):
    shaped = energy.reshape(n_freq, n_dir, -1)
    drift_rate = drift.reshape(n_freq, n_dir, 1)
    upward = jnp.maximum(drift_rate, 0.0) * shaped
    downward = jnp.maximum(-drift_rate, 0.0) * shaped
    empty_row = jnp.zeros_like(shaped[:1])
    from_below = jnp.concatenate([empty_row, upward[:-1]], axis=0)
    from_above = jnp.concatenate([downward[1:], empty_row], axis=0)
    return (shaped - jnp.abs(drift_rate) * shaped + from_below + from_above).reshape(energy.shape)


def settle_points(points, drift, partners):
    shifted = advect_frequency(points, drift, NF, ND)
    plus_values = jnp.take(shifted, partners[0], axis=0)
    minus_values = jnp.take(shifted, partners[1], axis=0)
    quartet = shifted * shifted * (plus_values + minus_values) - 2.0 * shifted * plus_values * minus_values
    source = jax.ops.segment_sum(quartet, partners[0], num_segments=K) + jax.ops.segment_sum(quartet, partners[1], num_segments=K) - 2.0 * quartet
    return shifted + dia_coeff * source


def reference(spectrum, depth_speed, turning, drift, partners, sea_slots, sea_counts):
    per_block = X_DEV * CY
    sea_mask = sea_cells(sea_slots.reshape(ROW_BLOCKS * TILES, CAP), sea_counts.reshape(ROW_BLOCKS * TILES), per_block)
    sea_mask = sea_mask.reshape(ROW_BLOCKS, TILES, X_DEV, CY).transpose(0, 2, 1, 3).reshape(NX, NY)
    depth_ext = jnp.concatenate([depth_speed[:, -1:], depth_speed, depth_speed[:, :1]], axis=1)
    angles = 2.0 * jnp.pi * jnp.arange(ND, dtype=jnp.float32) / ND
    cosines = jnp.cos(angles)
    sine_part = jnp.sin(angles)

    def one_freq(freq_id):
        block_rows = lax.dynamic_slice_in_dim(spectrum, freq_id * ND, ND, 0)
        energy = block_rows * sea_mask
        energy_ext = jnp.concatenate([energy[:, :, -1:], energy, energy[:, :, :1]], axis=2)
        speeds = jnp.repeat(speed_top * jnp.exp(-decline * freq_id.astype(jnp.float32)[None]), ND)
        spaced = advect_space(energy_ext, depth_ext, speeds, cosines, sine_part, sea_mask)
        return advect_direction(spaced[None], turning)[0]

    stepped = lax.map(one_freq, jnp.arange(NF, dtype=jnp.int32)).reshape(K, NX, NY)

    def one_row(row_id):
        points = lax.dynamic_index_in_dim(stepped, row_id, 1, keepdims=False)
        return settle_points(points, drift, partners)

    settled = lax.map(one_row, jnp.arange(NX, dtype=jnp.int32))
    return settled.transpose(1, 0, 2)
```

```python
import jax
import jax.numpy as jnp
from jax import lax
from jax.sharding import PartitionSpec as P

ND = 36
NF = 32


speed_top = 0.6
decline = 0.0953102
dia_coeff = 0.25


def extended(cells, sides, width):
    for axis, dim in sides:
        count = lax.axis_size(axis)
        head = lax.slice_in_dim(cells, 0, width, axis=dim)
        tail = lax.slice_in_dim(cells, cells.shape[dim] - width, cells.shape[dim], axis=dim)
        cells = jnp.concatenate(
            [
                lax.ppermute(tail, axis, [(i, (i + 1) % count) for i in range(count)]),
                cells,
                lax.ppermute(head, axis, [((i + 1) % count, i) for i in range(count)]),
            ],
            axis=dim,
        )
    return cells


def sea_cells(sea_list, sea_total, per_block):
    cell_ids = jnp.arange(per_block, dtype=jnp.int32)
    slot_rank = jnp.arange(sea_list.shape[1], dtype=jnp.int32)
    is_live = slot_rank[None, :] < sea_total[:, None]
    matches = (sea_list[:, :, None] == cell_ids[None, None, :]) & is_live[:, :, None]
    return jnp.any(matches, axis=1).astype(jnp.float32)


def advect_space(energy_ext, depth_ext, speeds, cosines, sine_part, sea_mask):
    east_rate = (speeds * cosines)[:, None, None] * depth_ext[None]
    north_rate = (speeds * sine_part)[:, None, None] * depth_ext[None, :, 1:-1]
    centre = energy_ext[:, :, 1:-1]
    east_mid = east_rate[:, :, 1:-1]
    inflow = (
        jnp.maximum(east_rate[:, :, :-2], 0.0) * energy_ext[:, :, :-2]
        + jnp.maximum(-east_rate[:, :, 2:], 0.0) * energy_ext[:, :, 2:]
    )
    empty_row = jnp.zeros_like(centre[:, :1])
    from_south = jnp.concatenate(
        [empty_row, (jnp.maximum(north_rate, 0.0) * centre)[:, :-1]], axis=1
    )
    from_north = jnp.concatenate(
        [(jnp.maximum(-north_rate, 0.0) * centre)[:, 1:], empty_row], axis=1
    )
    updated = (
        centre
        - (jnp.abs(east_mid) + jnp.abs(north_rate)) * centre
        + inflow
        + from_south
        + from_north
    )
    return updated * sea_mask


def advect_direction(energy, turning):
    turn_plus = jnp.maximum(turning, 0.0)
    behind = jnp.maximum(-turning, 0.0)
    return (
        energy
        - jnp.abs(turning) * energy
        + turn_plus * jnp.roll(energy, 1, axis=1)
        + behind * jnp.roll(energy, -1, axis=1)
    )


def advect_frequency(energy, drift, n_freq, n_dir):
    shaped = energy.reshape(n_freq, n_dir, -1)
    drift_rate = drift.reshape(n_freq, n_dir, 1)
    upward = jnp.maximum(drift_rate, 0.0) * shaped
    downward = jnp.maximum(-drift_rate, 0.0) * shaped
    empty_row = jnp.zeros_like(shaped[:1])
    from_below = jnp.concatenate([empty_row, upward[:-1]], axis=0)
    from_above = jnp.concatenate([downward[1:], empty_row], axis=0)
    return (shaped - jnp.abs(drift_rate) * shaped + from_below + from_above).reshape(energy.shape)


def shift_freq(x, s, up):
    if s == 0:
        return x
    n = x.shape[0]
    if up:
        return jnp.concatenate([x[s:], jnp.repeat(x[n - 1 :], s, axis=0)], axis=0)
    return jnp.concatenate([jnp.repeat(x[:1], s, axis=0), x[: n - s]], axis=0)


def pad_freq(x, s, up):
    if s == 0:
        return x
    n = x.shape[0]
    zeros = jnp.zeros_like(x[:s])
    if up:
        return jnp.concatenate([x[s:], zeros], axis=0)
    return jnp.concatenate([zeros, x[: n - s]], axis=0)


def pick_shift(choice, options):
    out = options[-1]
    for i in range(len(options) - 2, -1, -1):
        out = jnp.where(choice == i + 1, options[i], out)
    return out


def settle(points, drift, partners):
    n_freq = NF
    shape = points.shape
    grid = points.reshape(n_freq, ND, -1)
    shifted = advect_frequency(grid, drift, NF, ND).reshape(n_freq, ND, -1)
    freq_ids = jnp.arange(n_freq, dtype=jnp.int32)
    up_ids = partners[0].reshape(n_freq, ND)[:, 0]
    down_ids = partners[1].reshape(n_freq, ND)[:, 0]
    up_freq = up_ids // ND
    down_freq = down_ids // ND
    up_turn = (up_ids % ND)[:, None, None]
    down_turn = (ND - down_ids % ND)[:, None, None]
    up_step = (up_freq - freq_ids)[:, None, None]
    down_step = (freq_ids - down_freq)[:, None, None]

    def by_freq(step, up):
        out = shifted
        for s in (1, 2, 3):
            out = jnp.where(step == s, shift_freq(shifted, s, up), out)
        return out

    up_src = by_freq(up_step, True)
    down_src = by_freq(down_step, False)
    plus_values = pick_shift(up_turn, [jnp.roll(up_src, -r, axis=1) for r in (1, 2, 3)])
    minus_values = pick_shift(down_turn, [jnp.roll(down_src, r, axis=1) for r in (1, 2, 3)])
    quartet = (
        shifted * shifted * (plus_values + minus_values)
        - 2.0 * shifted * plus_values * minus_values
    )
    back_up = pick_shift(up_turn, [jnp.roll(quartet, r, axis=1) for r in (1, 2, 3)])
    back_down = pick_shift(down_turn, [jnp.roll(quartet, -r, axis=1) for r in (1, 2, 3)])
    to_up = jnp.zeros_like(quartet)
    to_down = jnp.zeros_like(quartet)
    for s in (0, 1, 2, 3):
        src_up = pad_freq(up_freq, s, False)
        hit_up = (src_up == freq_ids) & (freq_ids >= s)
        to_up = to_up + jnp.where(hit_up[:, None, None], pad_freq(back_up, s, False), 0.0)
        src_down = pad_freq(down_freq, s, True)
        hit_down = (src_down == freq_ids) & (freq_ids + s < n_freq)
        to_down = to_down + jnp.where(hit_down[:, None, None], pad_freq(back_down, s, True), 0.0)
    source = to_up + to_down - 2.0 * quartet
    return (shifted + dia_coeff * source).reshape(shape)


def shards(spectrum, depth_speed, turning, drift, partners, sea_slots, sea_counts):
    channels, grid_rows, grid_cols = spectrum.shape
    n_spec = lax.axis_size("spec")
    sub_rows = grid_rows // n_spec
    per_block = sub_rows * grid_cols
    sea_list = sea_slots[:, 0, :]
    sea_mask = sea_cells(sea_list, sea_counts[:, 0], per_block).reshape(grid_rows, grid_cols)
    energy = spectrum * sea_mask
    stacked = jnp.concatenate([energy, depth_speed[None]], axis=0)
    padded = extended(stacked, (("tile", 2),), 1)
    local_freq = channels // ND
    freq_ids = (
        lax.axis_index("spec") * local_freq + jnp.arange(local_freq, dtype=jnp.int32)
    ).astype(jnp.float32)
    speeds = jnp.repeat(speed_top * jnp.exp(-decline * freq_ids), ND)
    angles = 2.0 * jnp.pi * jnp.arange(ND, dtype=jnp.float32) / ND
    cosines = jnp.tile(jnp.cos(angles), local_freq)
    sine_part = jnp.tile(jnp.sin(angles), local_freq)
    spaced = advect_space(padded[:channels], padded[channels], speeds, cosines, sine_part, sea_mask)
    turned = advect_direction(spaced.reshape(local_freq, ND, grid_rows, grid_cols), turning)
    turned = turned.reshape(channels, grid_rows, grid_cols)
    points = lax.all_to_all(turned, "spec", split_axis=1, concat_axis=0, tiled=True)
    return settle(points, drift, partners)


def solution(mesh):
    return jax.shard_map(
        shards,
        mesh=mesh,
        in_specs=(
            P("spec", None, "tile"),
            P(None, "tile"),
            P(None, "tile"),
            P(),
            P(),
            P(None, "tile", None),
            P(None, "tile"),
        ),
        out_specs=P(None, "spec", "tile"),
        check_vma=False,
    )
```

```python
import jax
import jax.numpy as jnp
from jax import lax
from jax.sharding import PartitionSpec as P

ND = 36
NF = 32


speed_top = 0.6
decline = 0.0953102
dia_coeff = 0.25


def extended(cells, sides, width):
    for axis, dim in sides:
        count = lax.axis_size(axis)
        head = lax.slice_in_dim(cells, 0, width, axis=dim)
        tail = lax.slice_in_dim(cells, cells.shape[dim] - width, cells.shape[dim], axis=dim)
        cells = jnp.concatenate(
            [
                lax.ppermute(tail, axis, [(i, (i + 1) % count) for i in range(count)]),
                cells,
                lax.ppermute(head, axis, [((i + 1) % count, i) for i in range(count)]),
            ],
            axis=dim,
        )
    return cells


def sea_cells(sea_list, sea_total, per_block):
    cell_ids = jnp.arange(per_block, dtype=jnp.int32)
    slot_rank = jnp.arange(sea_list.shape[1], dtype=jnp.int32)
    is_live = slot_rank[None, :] < sea_total[:, None]
    matches = (sea_list[:, :, None] == cell_ids[None, None, :]) & is_live[:, :, None]
    return jnp.any(matches, axis=1).astype(jnp.float32)


def advect_space(energy_ext, depth_ext, speeds, cosines, sine_part, sea_mask):
    east_rate = (speeds * cosines)[:, None, None] * depth_ext[None]
    north_rate = (speeds * sine_part)[:, None, None] * depth_ext[None, :, 1:-1]
    centre = energy_ext[:, :, 1:-1]
    east_mid = east_rate[:, :, 1:-1]
    inflow = (
        jnp.maximum(east_rate[:, :, :-2], 0.0) * energy_ext[:, :, :-2]
        + jnp.maximum(-east_rate[:, :, 2:], 0.0) * energy_ext[:, :, 2:]
    )
    empty_row = jnp.zeros_like(centre[:, :1])
    from_south = jnp.concatenate(
        [empty_row, (jnp.maximum(north_rate, 0.0) * centre)[:, :-1]], axis=1
    )
    from_north = jnp.concatenate(
        [(jnp.maximum(-north_rate, 0.0) * centre)[:, 1:], empty_row], axis=1
    )
    updated = (
        centre
        - (jnp.abs(east_mid) + jnp.abs(north_rate)) * centre
        + inflow
        + from_south
        + from_north
    )
    return updated * sea_mask


def advect_direction(energy, turning):
    turn_plus = jnp.maximum(turning, 0.0)
    behind = jnp.maximum(-turning, 0.0)
    return (
        energy
        - jnp.abs(turning) * energy
        + turn_plus * jnp.roll(energy, 1, axis=1)
        + behind * jnp.roll(energy, -1, axis=1)
    )


def advect_frequency(energy, drift, n_freq, n_dir):
    shaped = energy.reshape(n_freq, n_dir, -1)
    drift_rate = drift.reshape(n_freq, n_dir, 1)
    upward = jnp.maximum(drift_rate, 0.0) * shaped
    downward = jnp.maximum(-drift_rate, 0.0) * shaped
    empty_row = jnp.zeros_like(shaped[:1])
    from_below = jnp.concatenate([empty_row, upward[:-1]], axis=0)
    from_above = jnp.concatenate([downward[1:], empty_row], axis=0)
    return (shaped - jnp.abs(drift_rate) * shaped + from_below + from_above).reshape(energy.shape)


def shift_freq(x, s, up):
    if s == 0:
        return x
    n = x.shape[0]
    if up:
        return jnp.concatenate([x[s:], jnp.repeat(x[n - 1 :], s, axis=0)], axis=0)
    return jnp.concatenate([jnp.repeat(x[:1], s, axis=0), x[: n - s]], axis=0)


def pad_freq(x, s, up):
    if s == 0:
        return x
    n = x.shape[0]
    zeros = jnp.zeros_like(x[:s])
    if up:
        return jnp.concatenate([x[s:], zeros], axis=0)
    return jnp.concatenate([zeros, x[: n - s]], axis=0)


def pick_shift(choice, options):
    out = options[-1]
    for i in range(len(options) - 2, -1, -1):
        out = jnp.where(choice == i + 1, options[i], out)
    return out


def settle(points, drift, partners):
    n_freq = NF
    shape = points.shape
    grid = points.reshape(n_freq, ND, -1)
    shifted = advect_frequency(grid, drift, NF, ND).reshape(n_freq, ND, -1)
    freq_ids = jnp.arange(n_freq, dtype=jnp.int32)
    up_ids = partners[0].reshape(n_freq, ND)[:, 0]
    down_ids = partners[1].reshape(n_freq, ND)[:, 0]
    up_freq = up_ids // ND
    down_freq = down_ids // ND
    up_turn = (up_ids % ND)[:, None, None]
    down_turn = (ND - down_ids % ND)[:, None, None]
    up_step = (up_freq - freq_ids)[:, None, None]
    down_step = (freq_ids - down_freq)[:, None, None]

    def by_freq(step, up):
        out = shifted
        for s in (1, 2, 3):
            out = jnp.where(step == s, shift_freq(shifted, s, up), out)
        return out

    up_src = by_freq(up_step, True)
    down_src = by_freq(down_step, False)
    plus_values = pick_shift(up_turn, [jnp.roll(up_src, -r, axis=1) for r in (1, 2, 3)])
    minus_values = pick_shift(down_turn, [jnp.roll(down_src, r, axis=1) for r in (1, 2, 3)])
    quartet = (
        shifted * shifted * (plus_values + minus_values)
        - 2.0 * shifted * plus_values * minus_values
    )
    back_up = pick_shift(up_turn, [jnp.roll(quartet, r, axis=1) for r in (1, 2, 3)])
    back_down = pick_shift(down_turn, [jnp.roll(quartet, -r, axis=1) for r in (1, 2, 3)])
    to_up = jnp.zeros_like(quartet)
    to_down = jnp.zeros_like(quartet)
    for s in (0, 1, 2, 3):
        src_up = pad_freq(up_freq, s, False)
        hit_up = (src_up == freq_ids) & (freq_ids >= s)
        to_up = to_up + jnp.where(hit_up[:, None, None], pad_freq(back_up, s, False), 0.0)
        src_down = pad_freq(down_freq, s, True)
        hit_down = (src_down == freq_ids) & (freq_ids + s < n_freq)
        to_down = to_down + jnp.where(hit_down[:, None, None], pad_freq(back_down, s, True), 0.0)
    source = to_up + to_down - 2.0 * quartet
    return (shifted + dia_coeff * source).reshape(shape)


def neighbours(edges_first, edges_last):
    count = lax.axis_size("tile")
    from_west = lax.ppermute(edges_last, "tile", [(i, (i + 1) % count) for i in range(count)])
    from_east = lax.ppermute(edges_first, "tile", [((i + 1) % count, i) for i in range(count)])
    return from_west, from_east


def propagate(energy, depth, sea_mask, turning, from_west, from_east, speeds, cosines, sine_part):
    channels, grid_rows, grid_cols = energy.shape
    col = lax.broadcasted_iota(jnp.int32, (grid_rows, grid_cols), 1)
    row = lax.broadcasted_iota(jnp.int32, (grid_rows, grid_cols), 0)
    first_col = col == 0
    last_col = col == grid_cols - 1
    west_energy = jnp.where(first_col, from_west[:channels, :, None], jnp.roll(energy, 1, axis=2))
    east_energy = jnp.where(last_col, from_east[:channels, :, None], jnp.roll(energy, -1, axis=2))
    west_depth = jnp.where(first_col, from_west[channels][:, None], jnp.roll(depth, 1, axis=1))
    east_depth = jnp.where(last_col, from_east[channels][:, None], jnp.roll(depth, -1, axis=1))
    east_coef = (speeds * cosines)[:, None, None]
    north_coef = (speeds * sine_part)[:, None, None]
    east_mid = east_coef * depth[None]
    north_rate = north_coef * depth[None]
    inflow = (
        jnp.maximum(east_coef * west_depth[None], 0.0) * west_energy
        + jnp.maximum(-(east_coef * east_depth[None]), 0.0) * east_energy
    )
    south_flux = jnp.maximum(north_rate, 0.0) * energy
    north_flux = jnp.maximum(-north_rate, 0.0) * energy
    from_south = jnp.where(row == 0, 0.0, jnp.roll(south_flux, 1, axis=1))
    from_north = jnp.where(row == grid_rows - 1, 0.0, jnp.roll(north_flux, -1, axis=1))
    updated = (
        energy
        - (jnp.abs(east_mid) + jnp.abs(north_rate)) * energy
        + inflow
        + from_south
        + from_north
    )
    spaced = updated * sea_mask
    return advect_direction(spaced[None], turning)[0]


def shards(spectrum, depth_speed, turning, drift, partners, sea_slots, sea_counts):
    channels, grid_rows, grid_cols = spectrum.shape
    n_spec = lax.axis_size("spec")
    sub_rows = grid_rows // n_spec
    per_block = sub_rows * grid_cols
    sea_list = sea_slots[:, 0, :]
    sea_mask = sea_cells(sea_list, sea_counts[:, 0], per_block).reshape(grid_rows, grid_cols)
    energy = spectrum * sea_mask
    edges_first = jnp.concatenate([energy[:, :, 0], depth_speed[None, :, 0]], axis=0)
    edges_last = jnp.concatenate([energy[:, :, -1], depth_speed[None, :, -1]], axis=0)
    from_west, from_east = neighbours(edges_first, edges_last)
    local_freq = channels // ND
    freq_ids = (
        lax.axis_index("spec") * local_freq + jnp.arange(local_freq, dtype=jnp.int32)
    ).astype(jnp.float32)
    speeds = jnp.repeat(speed_top * jnp.exp(-decline * freq_ids), ND)
    angles = 2.0 * jnp.pi * jnp.arange(ND, dtype=jnp.float32) / ND
    cosines = jnp.tile(jnp.cos(angles), local_freq)
    sine_part = jnp.tile(jnp.sin(angles), local_freq)
    turned = propagate(
        energy, depth_speed, sea_mask, turning, from_west, from_east, speeds, cosines, sine_part
    )
    points = lax.all_to_all(turned, "spec", split_axis=1, concat_axis=0, tiled=True)
    return settle(points, drift, partners)


def solution(mesh):
    return jax.shard_map(
        shards,
        mesh=mesh,
        in_specs=(
            P("spec", None, "tile"),
            P(None, "tile"),
            P(None, "tile"),
            P(),
            P(),
            P(None, "tile", None),
            P(None, "tile"),
        ),
        out_specs=P(None, "spec", "tile"),
        check_vma=False,
    )
```

```python
import jax
import jax.numpy as jnp
from jax import lax
from jax.sharding import PartitionSpec as P
from jax.experimental import pallas as pl
from jax.experimental.pallas import tpu as pltpu

ND = 36
NF = 32


speed_top = 0.6
decline = 0.0953102
dia_coeff = 0.25


def extended(cells, sides, width):
    for axis, dim in sides:
        count = lax.axis_size(axis)
        head = lax.slice_in_dim(cells, 0, width, axis=dim)
        tail = lax.slice_in_dim(cells, cells.shape[dim] - width, cells.shape[dim], axis=dim)
        cells = jnp.concatenate(
            [
                lax.ppermute(tail, axis, [(i, (i + 1) % count) for i in range(count)]),
                cells,
                lax.ppermute(head, axis, [((i + 1) % count, i) for i in range(count)]),
            ],
            axis=dim,
        )
    return cells


def sea_cells(sea_list, sea_total, per_block):
    cell_ids = jnp.arange(per_block, dtype=jnp.int32)
    slot_rank = jnp.arange(sea_list.shape[1], dtype=jnp.int32)
    is_live = slot_rank[None, :] < sea_total[:, None]
    matches = (sea_list[:, :, None] == cell_ids[None, None, :]) & is_live[:, :, None]
    return jnp.any(matches, axis=1).astype(jnp.float32)


def advect_space(energy_ext, depth_ext, speeds, cosines, sine_part, sea_mask):
    east_rate = (speeds * cosines)[:, None, None] * depth_ext[None]
    north_rate = (speeds * sine_part)[:, None, None] * depth_ext[None, :, 1:-1]
    centre = energy_ext[:, :, 1:-1]
    east_mid = east_rate[:, :, 1:-1]
    inflow = (
        jnp.maximum(east_rate[:, :, :-2], 0.0) * energy_ext[:, :, :-2]
        + jnp.maximum(-east_rate[:, :, 2:], 0.0) * energy_ext[:, :, 2:]
    )
    empty_row = jnp.zeros_like(centre[:, :1])
    from_south = jnp.concatenate(
        [empty_row, (jnp.maximum(north_rate, 0.0) * centre)[:, :-1]], axis=1
    )
    from_north = jnp.concatenate(
        [(jnp.maximum(-north_rate, 0.0) * centre)[:, 1:], empty_row], axis=1
    )
    updated = (
        centre
        - (jnp.abs(east_mid) + jnp.abs(north_rate)) * centre
        + inflow
        + from_south
        + from_north
    )
    return updated * sea_mask


def advect_direction(energy, turning):
    turn_plus = jnp.maximum(turning, 0.0)
    behind = jnp.maximum(-turning, 0.0)
    return (
        energy
        - jnp.abs(turning) * energy
        + turn_plus * jnp.roll(energy, 1, axis=1)
        + behind * jnp.roll(energy, -1, axis=1)
    )


def advect_frequency(energy, drift, n_freq, n_dir):
    shaped = energy.reshape(n_freq, n_dir, -1)
    drift_rate = drift.reshape(n_freq, n_dir, 1)
    upward = jnp.maximum(drift_rate, 0.0) * shaped
    downward = jnp.maximum(-drift_rate, 0.0) * shaped
    empty_row = jnp.zeros_like(shaped[:1])
    from_below = jnp.concatenate([empty_row, upward[:-1]], axis=0)
    from_above = jnp.concatenate([downward[1:], empty_row], axis=0)
    return (shaped - jnp.abs(drift_rate) * shaped + from_below + from_above).reshape(energy.shape)


def shift_freq(x, s, up):
    if s == 0:
        return x
    n = x.shape[0]
    if up:
        return jnp.concatenate([x[s:], jnp.repeat(x[n - 1 :], s, axis=0)], axis=0)
    return jnp.concatenate([jnp.repeat(x[:1], s, axis=0), x[: n - s]], axis=0)


def pad_freq(x, s, up):
    if s == 0:
        return x
    n = x.shape[0]
    zeros = jnp.zeros_like(x[:s])
    if up:
        return jnp.concatenate([x[s:], zeros], axis=0)
    return jnp.concatenate([zeros, x[: n - s]], axis=0)


def pick_shift(choice, options):
    out = options[-1]
    for i in range(len(options) - 2, -1, -1):
        out = jnp.where(choice == i + 1, options[i], out)
    return out


def settle(points, drift, partners):
    n_freq = NF
    shape = points.shape
    grid = points.reshape(n_freq, ND, -1)
    shifted = advect_frequency(grid, drift, NF, ND).reshape(n_freq, ND, -1)
    freq_ids = jnp.arange(n_freq, dtype=jnp.int32)
    up_ids = partners[0].reshape(n_freq, ND)[:, 0]
    down_ids = partners[1].reshape(n_freq, ND)[:, 0]
    up_freq = up_ids // ND
    down_freq = down_ids // ND
    up_turn = (up_ids % ND)[:, None, None]
    down_turn = (ND - down_ids % ND)[:, None, None]
    up_step = (up_freq - freq_ids)[:, None, None]
    down_step = (freq_ids - down_freq)[:, None, None]

    def by_freq(step, up):
        out = shifted
        for s in (1, 2, 3):
            out = jnp.where(step == s, shift_freq(shifted, s, up), out)
        return out

    up_src = by_freq(up_step, True)
    down_src = by_freq(down_step, False)
    plus_values = pick_shift(up_turn, [jnp.roll(up_src, -r, axis=1) for r in (1, 2, 3)])
    minus_values = pick_shift(down_turn, [jnp.roll(down_src, r, axis=1) for r in (1, 2, 3)])
    quartet = (
        shifted * shifted * (plus_values + minus_values)
        - 2.0 * shifted * plus_values * minus_values
    )
    back_up = pick_shift(up_turn, [jnp.roll(quartet, r, axis=1) for r in (1, 2, 3)])
    back_down = pick_shift(down_turn, [jnp.roll(quartet, -r, axis=1) for r in (1, 2, 3)])
    to_up = jnp.zeros_like(quartet)
    to_down = jnp.zeros_like(quartet)
    for s in (0, 1, 2, 3):
        src_up = pad_freq(up_freq, s, False)
        hit_up = (src_up == freq_ids) & (freq_ids >= s)
        to_up = to_up + jnp.where(hit_up[:, None, None], pad_freq(back_up, s, False), 0.0)
        src_down = pad_freq(down_freq, s, True)
        hit_down = (src_down == freq_ids) & (freq_ids + s < n_freq)
        to_down = to_down + jnp.where(hit_down[:, None, None], pad_freq(back_down, s, True), 0.0)
    source = to_up + to_down - 2.0 * quartet
    return (shifted + dia_coeff * source).reshape(shape)


def neighbours(edges_first, edges_last):
    count = lax.axis_size("tile")
    from_west = lax.ppermute(edges_last, "tile", [(i, (i + 1) % count) for i in range(count)])
    from_east = lax.ppermute(edges_first, "tile", [((i + 1) % count, i) for i in range(count)])
    return from_west, from_east


def propagate_kernel(coef_ref, spec_ref, mask_ref, depth_ref, turn_ref, west_ref, east_ref, out_ref, spaced_ref):
    channels, grid_rows, grid_cols = spec_ref.shape
    mask = mask_ref[...]
    depth = depth_ref[...]
    west = west_ref[...]
    east = east_ref[...]
    col = lax.broadcasted_iota(jnp.int32, (grid_rows, grid_cols), 1)
    row = lax.broadcasted_iota(jnp.int32, (grid_rows, grid_cols), 0)
    first_col = col == 0
    last_col = col == grid_cols - 1
    first_row = row == 0
    last_row = row == grid_rows - 1
    west_depth = jnp.where(first_col, west[:, channels : channels + 1], pltpu.roll(depth, 1, 1))
    east_depth = jnp.where(last_col, east[:, channels : channels + 1], pltpu.roll(depth, grid_cols - 1, 1))
    for d in range(channels):
        energy = spec_ref[d] * mask
        west_energy = jnp.where(first_col, west[:, d : d + 1], pltpu.roll(energy, 1, 1))
        east_energy = jnp.where(last_col, east[:, d : d + 1], pltpu.roll(energy, grid_cols - 1, 1))
        east_coef = coef_ref[0, d]
        north_coef = coef_ref[1, d]
        east_mid = east_coef * depth
        north_rate = north_coef * depth
        inflow = (
            jnp.maximum(east_coef * west_depth, 0.0) * west_energy
            + jnp.maximum(-(east_coef * east_depth), 0.0) * east_energy
        )
        south_flux = jnp.maximum(north_rate, 0.0) * energy
        north_flux = jnp.maximum(-north_rate, 0.0) * energy
        from_south = jnp.where(first_row, 0.0, pltpu.roll(south_flux, 1, 0))
        from_north = jnp.where(last_row, 0.0, pltpu.roll(north_flux, grid_rows - 1, 0))
        updated = (
            energy
            - (jnp.abs(east_mid) + jnp.abs(north_rate)) * energy
            + inflow
            + from_south
            + from_north
        )
        spaced_ref[d] = updated * mask
    turning = turn_ref[...]
    turn_plus = jnp.maximum(turning, 0.0)
    behind = jnp.maximum(-turning, 0.0)
    turn_abs = jnp.abs(turning)
    for d in range(channels):
        here = spaced_ref[d]
        out_ref[d] = (
            here
            - turn_abs * here
            + turn_plus * spaced_ref[(d - 1) % channels]
            + behind * spaced_ref[(d + 1) % channels]
        )


def propagate(spectrum, depth, sea_mask, turning, from_west, from_east, coef):
    vmem = pl.BlockSpec(memory_space=pltpu.VMEM)
    return pl.pallas_call(
        propagate_kernel,
        out_shape=jax.ShapeDtypeStruct(spectrum.shape, jnp.float32),
        in_specs=[pl.BlockSpec(memory_space=pltpu.SMEM)] + [vmem] * 6,
        out_specs=vmem,
        scratch_shapes=[pltpu.VMEM(spectrum.shape, jnp.float32)],
    )(coef, spectrum, sea_mask, depth, turning, from_west, from_east)


def shards(spectrum, depth_speed, turning, drift, partners, sea_slots, sea_counts):
    channels, grid_rows, grid_cols = spectrum.shape
    n_spec = lax.axis_size("spec")
    sub_rows = grid_rows // n_spec
    per_block = sub_rows * grid_cols
    sea_list = sea_slots[:, 0, :]
    sea_mask = sea_cells(sea_list, sea_counts[:, 0], per_block).reshape(grid_rows, grid_cols)
    edge_mask = sea_mask[:, ::grid_cols - 1]
    edges_first = jnp.concatenate(
        [(spectrum[:, :, 0] * edge_mask[None, :, 0]).T, depth_speed[:, :1]], axis=1
    )
    edges_last = jnp.concatenate(
        [(spectrum[:, :, -1] * edge_mask[None, :, 1]).T, depth_speed[:, -1:]], axis=1
    )
    from_west, from_east = neighbours(edges_first, edges_last)
    local_freq = channels // ND
    freq_ids = (
        lax.axis_index("spec") * local_freq + jnp.arange(local_freq, dtype=jnp.int32)
    ).astype(jnp.float32)
    speeds = jnp.repeat(speed_top * jnp.exp(-decline * freq_ids), ND)
    angles = 2.0 * jnp.pi * jnp.arange(ND, dtype=jnp.float32) / ND
    cosines = jnp.tile(jnp.cos(angles), local_freq)
    sine_part = jnp.tile(jnp.sin(angles), local_freq)
    coef = jnp.stack([speeds * cosines, speeds * sine_part])
    turned = propagate(spectrum, depth_speed, sea_mask, turning, from_west, from_east, coef)
    points = lax.all_to_all(turned, "spec", split_axis=1, concat_axis=0, tiled=True)
    return settle(points, drift, partners)


def solution(mesh):
    return jax.shard_map(
        shards,
        mesh=mesh,
        in_specs=(
            P("spec", None, "tile"),
            P(None, "tile"),
            P(None, "tile"),
            P(),
            P(),
            P(None, "tile", None),
            P(None, "tile"),
        ),
        out_specs=P(None, "spec", "tile"),
        check_vma=False,
    )
```

```python
import jax
import jax.numpy as jnp
from jax import lax
from jax.sharding import PartitionSpec as P
from jax.experimental import pallas as pl
from jax.experimental.pallas import tpu as pltpu

ND = 36
NF = 32


speed_top = 0.6
decline = 0.0953102
dia_coeff = 0.25


def extended(cells, sides, width):
    for axis, dim in sides:
        count = lax.axis_size(axis)
        head = lax.slice_in_dim(cells, 0, width, axis=dim)
        tail = lax.slice_in_dim(cells, cells.shape[dim] - width, cells.shape[dim], axis=dim)
        cells = jnp.concatenate(
            [
                lax.ppermute(tail, axis, [(i, (i + 1) % count) for i in range(count)]),
                cells,
                lax.ppermute(head, axis, [((i + 1) % count, i) for i in range(count)]),
            ],
            axis=dim,
        )
    return cells


def sea_cells(sea_list, sea_total, per_block):
    cell_ids = jnp.arange(per_block, dtype=jnp.int32)
    slot_rank = jnp.arange(sea_list.shape[1], dtype=jnp.int32)
    is_live = slot_rank[None, :] < sea_total[:, None]
    matches = (sea_list[:, :, None] == cell_ids[None, None, :]) & is_live[:, :, None]
    return jnp.any(matches, axis=1).astype(jnp.float32)


def advect_space(energy_ext, depth_ext, speeds, cosines, sine_part, sea_mask):
    east_rate = (speeds * cosines)[:, None, None] * depth_ext[None]
    north_rate = (speeds * sine_part)[:, None, None] * depth_ext[None, :, 1:-1]
    centre = energy_ext[:, :, 1:-1]
    east_mid = east_rate[:, :, 1:-1]
    inflow = (
        jnp.maximum(east_rate[:, :, :-2], 0.0) * energy_ext[:, :, :-2]
        + jnp.maximum(-east_rate[:, :, 2:], 0.0) * energy_ext[:, :, 2:]
    )
    empty_row = jnp.zeros_like(centre[:, :1])
    from_south = jnp.concatenate(
        [empty_row, (jnp.maximum(north_rate, 0.0) * centre)[:, :-1]], axis=1
    )
    from_north = jnp.concatenate(
        [(jnp.maximum(-north_rate, 0.0) * centre)[:, 1:], empty_row], axis=1
    )
    updated = (
        centre
        - (jnp.abs(east_mid) + jnp.abs(north_rate)) * centre
        + inflow
        + from_south
        + from_north
    )
    return updated * sea_mask


def advect_direction(energy, turning):
    turn_plus = jnp.maximum(turning, 0.0)
    behind = jnp.maximum(-turning, 0.0)
    return (
        energy
        - jnp.abs(turning) * energy
        + turn_plus * jnp.roll(energy, 1, axis=1)
        + behind * jnp.roll(energy, -1, axis=1)
    )


def advect_frequency(energy, drift, n_freq, n_dir):
    shaped = energy.reshape(n_freq, n_dir, -1)
    drift_rate = drift.reshape(n_freq, n_dir, 1)
    upward = jnp.maximum(drift_rate, 0.0) * shaped
    downward = jnp.maximum(-drift_rate, 0.0) * shaped
    empty_row = jnp.zeros_like(shaped[:1])
    from_below = jnp.concatenate([empty_row, upward[:-1]], axis=0)
    from_above = jnp.concatenate([downward[1:], empty_row], axis=0)
    return (shaped - jnp.abs(drift_rate) * shaped + from_below + from_above).reshape(energy.shape)


def shift_freq(x, s, up):
    if s == 0:
        return x
    n = x.shape[0]
    if up:
        return jnp.concatenate([x[s:], jnp.repeat(x[n - 1 :], s, axis=0)], axis=0)
    return jnp.concatenate([jnp.repeat(x[:1], s, axis=0), x[: n - s]], axis=0)


def pad_freq(x, s, up):
    if s == 0:
        return x
    n = x.shape[0]
    zeros = jnp.zeros_like(x[:s])
    if up:
        return jnp.concatenate([x[s:], zeros], axis=0)
    return jnp.concatenate([zeros, x[: n - s]], axis=0)


def pick_shift(choice, options):
    out = options[-1]
    for i in range(len(options) - 2, -1, -1):
        out = jnp.where(choice == i + 1, options[i], out)
    return out


def settle(grid, drift, partners):
    n_freq = grid.shape[0]
    drift_rate = drift.reshape(n_freq, 1, ND, 1)
    upward = jnp.maximum(drift_rate, 0.0) * grid
    downward = jnp.maximum(-drift_rate, 0.0) * grid
    empty_row = jnp.zeros_like(grid[:1])
    from_below = jnp.concatenate([empty_row, upward[:-1]], axis=0)
    from_above = jnp.concatenate([downward[1:], empty_row], axis=0)
    shifted = grid - jnp.abs(drift_rate) * grid + from_below + from_above
    freq_ids = jnp.arange(n_freq, dtype=jnp.int32)
    up_ids = partners[0].reshape(n_freq, ND)[:, 0]
    down_ids = partners[1].reshape(n_freq, ND)[:, 0]
    up_freq = up_ids // ND
    down_freq = down_ids // ND
    per_freq = (n_freq, 1, 1, 1)
    up_turn = (up_ids % ND).reshape(per_freq)
    down_turn = (ND - down_ids % ND).reshape(per_freq)
    up_step = (up_freq - freq_ids).reshape(per_freq)
    down_step = (freq_ids - down_freq).reshape(per_freq)

    def by_freq(step, up):
        out = shifted
        for s in (1, 2, 3):
            out = jnp.where(step == s, shift_freq(shifted, s, up), out)
        return out

    up_src = by_freq(up_step, True)
    down_src = by_freq(down_step, False)
    plus_values = pick_shift(up_turn, [jnp.roll(up_src, -r, axis=2) for r in (1, 2, 3)])
    minus_values = pick_shift(down_turn, [jnp.roll(down_src, r, axis=2) for r in (1, 2, 3)])
    quartet = (
        shifted * shifted * (plus_values + minus_values)
        - 2.0 * shifted * plus_values * minus_values
    )
    back_up = pick_shift(up_turn, [jnp.roll(quartet, r, axis=2) for r in (1, 2, 3)])
    back_down = pick_shift(down_turn, [jnp.roll(quartet, -r, axis=2) for r in (1, 2, 3)])
    to_up = jnp.zeros_like(quartet)
    to_down = jnp.zeros_like(quartet)
    for s in (0, 1, 2, 3):
        src_up = pad_freq(up_freq, s, False)
        hit_up = ((src_up == freq_ids) & (freq_ids >= s)).reshape(per_freq)
        to_up = to_up + jnp.where(hit_up, pad_freq(back_up, s, False), 0.0)
        src_down = pad_freq(down_freq, s, True)
        hit_down = ((src_down == freq_ids) & (freq_ids + s < n_freq)).reshape(per_freq)
        to_down = to_down + jnp.where(hit_down, pad_freq(back_down, s, True), 0.0)
    source = to_up + to_down - 2.0 * quartet
    return shifted + dia_coeff * source


def neighbours(edges_first, edges_last):
    count = lax.axis_size("tile")
    from_west = lax.ppermute(edges_last, "tile", [(i, (i + 1) % count) for i in range(count)])
    from_east = lax.ppermute(edges_first, "tile", [((i + 1) % count, i) for i in range(count)])
    return from_west, from_east


def propagate_kernel(coef_ref, spec_ref, mask_ref, depth_ref, turn_ref, west_ref, east_ref, out_ref, spaced_ref):
    channels, grid_rows, grid_cols = spec_ref.shape
    mask = mask_ref[...]
    depth = depth_ref[...]
    west = west_ref[...]
    east = east_ref[...]
    col = lax.broadcasted_iota(jnp.int32, (grid_rows, grid_cols), 1)
    row = lax.broadcasted_iota(jnp.int32, (grid_rows, grid_cols), 0)
    first_col = col == 0
    last_col = col == grid_cols - 1
    first_row = row == 0
    last_row = row == grid_rows - 1
    west_depth = jnp.where(first_col, west[:, channels : channels + 1], pltpu.roll(depth, 1, 1))
    east_depth = jnp.where(last_col, east[:, channels : channels + 1], pltpu.roll(depth, grid_cols - 1, 1))
    for d in range(channels):
        energy = spec_ref[d] * mask
        west_energy = jnp.where(first_col, west[:, d : d + 1], pltpu.roll(energy, 1, 1))
        east_energy = jnp.where(last_col, east[:, d : d + 1], pltpu.roll(energy, grid_cols - 1, 1))
        east_coef = coef_ref[0, d]
        north_coef = coef_ref[1, d]
        east_mid = east_coef * depth
        north_rate = north_coef * depth
        inflow = (
            jnp.maximum(east_coef * west_depth, 0.0) * west_energy
            + jnp.maximum(-(east_coef * east_depth), 0.0) * east_energy
        )
        south_flux = jnp.maximum(north_rate, 0.0) * energy
        north_flux = jnp.maximum(-north_rate, 0.0) * energy
        from_south = jnp.where(first_row, 0.0, pltpu.roll(south_flux, 1, 0))
        from_north = jnp.where(last_row, 0.0, pltpu.roll(north_flux, grid_rows - 1, 0))
        updated = (
            energy
            - (jnp.abs(east_mid) + jnp.abs(north_rate)) * energy
            + inflow
            + from_south
            + from_north
        )
        spaced_ref[d] = updated * mask
    turning = turn_ref[...]
    turn_plus = jnp.maximum(turning, 0.0)
    behind = jnp.maximum(-turning, 0.0)
    turn_abs = jnp.abs(turning)
    for d in range(channels):
        here = spaced_ref[d]
        out_ref[d] = (
            here
            - turn_abs * here
            + turn_plus * spaced_ref[(d - 1) % channels]
            + behind * spaced_ref[(d + 1) % channels]
        )


def propagate(spectrum, depth, sea_mask, turning, from_west, from_east, coef):
    vmem = pl.BlockSpec(memory_space=pltpu.VMEM)
    return pl.pallas_call(
        propagate_kernel,
        out_shape=jax.ShapeDtypeStruct(spectrum.shape, jnp.float32),
        in_specs=[pl.BlockSpec(memory_space=pltpu.SMEM)] + [vmem] * 6,
        out_specs=vmem,
        scratch_shapes=[pltpu.VMEM(spectrum.shape, jnp.float32)],
    )(coef, spectrum, sea_mask, depth, turning, from_west, from_east)


def shards(spectrum, depth_speed, turning, drift, partners, sea_slots, sea_counts):
    channels, grid_rows, grid_cols = spectrum.shape
    n_spec = lax.axis_size("spec")
    sub_rows = grid_rows // n_spec
    per_block = sub_rows * grid_cols
    sea_list = sea_slots[:, 0, :]
    sea_mask = sea_cells(sea_list, sea_counts[:, 0], per_block).reshape(grid_rows, grid_cols)
    edge_mask = sea_mask[:, ::grid_cols - 1]
    edges_first = jnp.concatenate(
        [(spectrum[:, :, 0] * edge_mask[None, :, 0]).T, depth_speed[:, :1]], axis=1
    )
    edges_last = jnp.concatenate(
        [(spectrum[:, :, -1] * edge_mask[None, :, 1]).T, depth_speed[:, -1:]], axis=1
    )
    from_west, from_east = neighbours(edges_first, edges_last)
    local_freq = channels // ND
    freq_ids = (
        lax.axis_index("spec") * local_freq + jnp.arange(local_freq, dtype=jnp.int32)
    ).astype(jnp.float32)
    speeds = jnp.repeat(speed_top * jnp.exp(-decline * freq_ids), ND)
    angles = 2.0 * jnp.pi * jnp.arange(ND, dtype=jnp.float32) / ND
    cosines = jnp.tile(jnp.cos(angles), local_freq)
    sine_part = jnp.tile(jnp.sin(angles), local_freq)
    coef = jnp.stack([speeds * cosines, speeds * sine_part])
    turned = propagate(spectrum, depth_speed, sea_mask, turning, from_west, from_east, coef)
    by_row = jnp.transpose(turned, (1, 0, 2))
    points = lax.all_to_all(by_row, "spec", split_axis=0, concat_axis=0, tiled=True)
    grid = points.reshape(NF, sub_rows, ND, grid_cols)
    settled = settle(grid, drift, partners)
    return jnp.transpose(settled, (0, 2, 1, 3)).reshape(NF * ND, sub_rows, grid_cols)


def solution(mesh):
    return jax.shard_map(
        shards,
        mesh=mesh,
        in_specs=(
            P("spec", None, "tile"),
            P(None, "tile"),
            P(None, "tile"),
            P(),
            P(),
            P(None, "tile", None),
            P(None, "tile"),
        ),
        out_specs=P(None, "spec", "tile"),
        check_vma=False,
    )
```

```python
import jax
import jax.numpy as jnp
from jax import lax
from jax.sharding import PartitionSpec as P
from jax.experimental import pallas as pl
from jax.experimental.pallas import tpu as pltpu

ND = 36
NF = 32


speed_top = 0.6
decline = 0.0953102
dia_coeff = 0.25


def extended(cells, sides, width):
    for axis, dim in sides:
        count = lax.axis_size(axis)
        head = lax.slice_in_dim(cells, 0, width, axis=dim)
        tail = lax.slice_in_dim(cells, cells.shape[dim] - width, cells.shape[dim], axis=dim)
        cells = jnp.concatenate(
            [
                lax.ppermute(tail, axis, [(i, (i + 1) % count) for i in range(count)]),
                cells,
                lax.ppermute(head, axis, [((i + 1) % count, i) for i in range(count)]),
            ],
            axis=dim,
        )
    return cells


def sea_cells(sea_list, sea_total, per_block):
    cell_ids = jnp.arange(per_block, dtype=jnp.int32)
    slot_rank = jnp.arange(sea_list.shape[1], dtype=jnp.int32)
    is_live = slot_rank[None, :] < sea_total[:, None]
    matches = (sea_list[:, :, None] == cell_ids[None, None, :]) & is_live[:, :, None]
    return jnp.any(matches, axis=1).astype(jnp.float32)


def advect_space(energy_ext, depth_ext, speeds, cosines, sine_part, sea_mask):
    east_rate = (speeds * cosines)[:, None, None] * depth_ext[None]
    north_rate = (speeds * sine_part)[:, None, None] * depth_ext[None, :, 1:-1]
    centre = energy_ext[:, :, 1:-1]
    east_mid = east_rate[:, :, 1:-1]
    inflow = (
        jnp.maximum(east_rate[:, :, :-2], 0.0) * energy_ext[:, :, :-2]
        + jnp.maximum(-east_rate[:, :, 2:], 0.0) * energy_ext[:, :, 2:]
    )
    empty_row = jnp.zeros_like(centre[:, :1])
    from_south = jnp.concatenate(
        [empty_row, (jnp.maximum(north_rate, 0.0) * centre)[:, :-1]], axis=1
    )
    from_north = jnp.concatenate(
        [(jnp.maximum(-north_rate, 0.0) * centre)[:, 1:], empty_row], axis=1
    )
    updated = (
        centre
        - (jnp.abs(east_mid) + jnp.abs(north_rate)) * centre
        + inflow
        + from_south
        + from_north
    )
    return updated * sea_mask


def advect_direction(energy, turning):
    turn_plus = jnp.maximum(turning, 0.0)
    behind = jnp.maximum(-turning, 0.0)
    return (
        energy
        - jnp.abs(turning) * energy
        + turn_plus * jnp.roll(energy, 1, axis=1)
        + behind * jnp.roll(energy, -1, axis=1)
    )


def advect_frequency(energy, drift, n_freq, n_dir):
    shaped = energy.reshape(n_freq, n_dir, -1)
    drift_rate = drift.reshape(n_freq, n_dir, 1)
    upward = jnp.maximum(drift_rate, 0.0) * shaped
    downward = jnp.maximum(-drift_rate, 0.0) * shaped
    empty_row = jnp.zeros_like(shaped[:1])
    from_below = jnp.concatenate([empty_row, upward[:-1]], axis=0)
    from_above = jnp.concatenate([downward[1:], empty_row], axis=0)
    return (shaped - jnp.abs(drift_rate) * shaped + from_below + from_above).reshape(energy.shape)


def shift_freq(x, s, up):
    if s == 0:
        return x
    n = x.shape[0]
    if up:
        return jnp.concatenate([x[s:], jnp.repeat(x[n - 1 :], s, axis=0)], axis=0)
    return jnp.concatenate([jnp.repeat(x[:1], s, axis=0), x[: n - s]], axis=0)


def pad_freq(x, s, up):
    if s == 0:
        return x
    n = x.shape[0]
    zeros = jnp.zeros_like(x[:s])
    if up:
        return jnp.concatenate([x[s:], zeros], axis=0)
    return jnp.concatenate([zeros, x[: n - s]], axis=0)


def pick_shift(choice, options):
    out = options[-1]
    for i in range(len(options) - 2, -1, -1):
        out = jnp.where(choice == i + 1, options[i], out)
    return out


def settle(grid, drift, partners):
    n_freq = grid.shape[0]
    drift_rate = drift.reshape(n_freq, 1, ND, 1)
    upward = jnp.maximum(drift_rate, 0.0) * grid
    downward = jnp.maximum(-drift_rate, 0.0) * grid
    empty_row = jnp.zeros_like(grid[:1])
    from_below = jnp.concatenate([empty_row, upward[:-1]], axis=0)
    from_above = jnp.concatenate([downward[1:], empty_row], axis=0)
    shifted = grid - jnp.abs(drift_rate) * grid + from_below + from_above
    freq_ids = jnp.arange(n_freq, dtype=jnp.int32)
    up_ids = partners[0].reshape(n_freq, ND)[:, 0]
    down_ids = partners[1].reshape(n_freq, ND)[:, 0]
    up_freq = up_ids // ND
    down_freq = down_ids // ND
    per_freq = (n_freq, 1, 1, 1)
    up_turn = (up_ids % ND).reshape(per_freq)
    down_turn = (ND - down_ids % ND).reshape(per_freq)
    up_step = (up_freq - freq_ids).reshape(per_freq)
    down_step = (freq_ids - down_freq).reshape(per_freq)

    def by_freq(step, up):
        out = shifted
        for s in (1, 2, 3):
            out = jnp.where(step == s, shift_freq(shifted, s, up), out)
        return out

    up_src = by_freq(up_step, True)
    down_src = by_freq(down_step, False)
    plus_values = pick_shift(up_turn, [jnp.roll(up_src, -r, axis=2) for r in (1, 2, 3)])
    minus_values = pick_shift(down_turn, [jnp.roll(down_src, r, axis=2) for r in (1, 2, 3)])
    quartet = (
        shifted * shifted * (plus_values + minus_values)
        - 2.0 * shifted * plus_values * minus_values
    )
    back_up = pick_shift(up_turn, [jnp.roll(quartet, r, axis=2) for r in (1, 2, 3)])
    back_down = pick_shift(down_turn, [jnp.roll(quartet, -r, axis=2) for r in (1, 2, 3)])
    to_up = jnp.zeros_like(quartet)
    to_down = jnp.zeros_like(quartet)
    for s in (0, 1, 2, 3):
        src_up = pad_freq(up_freq, s, False)
        hit_up = ((src_up == freq_ids) & (freq_ids >= s)).reshape(per_freq)
        to_up = to_up + jnp.where(hit_up, pad_freq(back_up, s, False), 0.0)
        src_down = pad_freq(down_freq, s, True)
        hit_down = ((src_down == freq_ids) & (freq_ids + s < n_freq)).reshape(per_freq)
        to_down = to_down + jnp.where(hit_down, pad_freq(back_down, s, True), 0.0)
    source = to_up + to_down - 2.0 * quartet
    return shifted + dia_coeff * source


def neighbours(edges_first, edges_last):
    count = lax.axis_size("tile")
    from_west = lax.ppermute(edges_last, "tile", [(i, (i + 1) % count) for i in range(count)])
    from_east = lax.ppermute(edges_first, "tile", [((i + 1) % count, i) for i in range(count)])
    return from_west, from_east


def propagate_kernel(coef_ref, spec_ref, mask_ref, depth_ref, turn_ref, west_ref, east_ref, out_ref, spaced_ref):
    channels, grid_rows, grid_cols = spec_ref.shape
    mask = mask_ref[...]
    depth = depth_ref[...]
    west = west_ref[...]
    east = east_ref[...]
    col = lax.broadcasted_iota(jnp.int32, (grid_rows, grid_cols), 1)
    row = lax.broadcasted_iota(jnp.int32, (grid_rows, grid_cols), 0)
    first_col = col == 0
    last_col = col == grid_cols - 1
    first_row = row == 0
    last_row = row == grid_rows - 1
    west_depth = jnp.where(first_col, west[:, channels : channels + 1], pltpu.roll(depth, 1, 1))
    east_depth = jnp.where(last_col, east[:, channels : channels + 1], pltpu.roll(depth, grid_cols - 1, 1))
    for d in range(channels):
        energy = spec_ref[d] * mask
        west_energy = jnp.where(first_col, west[:, d : d + 1], pltpu.roll(energy, 1, 1))
        east_energy = jnp.where(last_col, east[:, d : d + 1], pltpu.roll(energy, grid_cols - 1, 1))
        east_coef = coef_ref[0, d]
        north_coef = coef_ref[1, d]
        east_mid = east_coef * depth
        north_rate = north_coef * depth
        inflow = (
            jnp.maximum(east_coef * west_depth, 0.0) * west_energy
            + jnp.maximum(-(east_coef * east_depth), 0.0) * east_energy
        )
        south_flux = jnp.maximum(north_rate, 0.0) * energy
        north_flux = jnp.maximum(-north_rate, 0.0) * energy
        from_south = jnp.where(first_row, 0.0, pltpu.roll(south_flux, 1, 0))
        from_north = jnp.where(last_row, 0.0, pltpu.roll(north_flux, grid_rows - 1, 0))
        updated = (
            energy
            - (jnp.abs(east_mid) + jnp.abs(north_rate)) * energy
            + inflow
            + from_south
            + from_north
        )
        spaced_ref[d] = updated * mask
    turning = turn_ref[...]
    turn_plus = jnp.maximum(turning, 0.0)
    behind = jnp.maximum(-turning, 0.0)
    turn_abs = jnp.abs(turning)
    for d in range(channels):
        here = spaced_ref[d]
        out_ref[:, d, :] = (
            here
            - turn_abs * here
            + turn_plus * spaced_ref[(d - 1) % channels]
            + behind * spaced_ref[(d + 1) % channels]
        )


def edges_kernel(spec_ref, mask_ref, depth_ref, first_ref, last_ref):
    channels, grid_rows, grid_cols = spec_ref.shape
    mask = mask_ref[...]
    depth = depth_ref[...]
    lane = lax.broadcasted_iota(jnp.int32, (grid_rows, grid_cols), 1)
    first = jnp.where(lane == channels, depth[:, :1], 0.0)
    last = jnp.where(lane == channels, depth[:, grid_cols - 1 :], 0.0)
    for d in range(channels):
        energy = spec_ref[d] * mask
        first = jnp.where(lane == d, energy[:, :1], first)
        last = jnp.where(lane == d, energy[:, grid_cols - 1 :], last)
    first_ref[...] = first
    last_ref[...] = last


def edges(spectrum, sea_mask, depth):
    vmem = pl.BlockSpec(memory_space=pltpu.VMEM)
    plane = jax.ShapeDtypeStruct(depth.shape, jnp.float32)
    return pl.pallas_call(
        edges_kernel,
        out_shape=(plane, plane),
        in_specs=[vmem] * 3,
        out_specs=(vmem, vmem),
    )(spectrum, sea_mask, depth)


def propagate(spectrum, depth, sea_mask, turning, from_west, from_east, coef):
    channels, grid_rows, grid_cols = spectrum.shape
    vmem = pl.BlockSpec(memory_space=pltpu.VMEM)
    return pl.pallas_call(
        propagate_kernel,
        out_shape=jax.ShapeDtypeStruct((grid_rows, channels, grid_cols), jnp.float32),
        in_specs=[pl.BlockSpec(memory_space=pltpu.SMEM)] + [vmem] * 6,
        out_specs=vmem,
        scratch_shapes=[pltpu.VMEM(spectrum.shape, jnp.float32)],
    )(coef, spectrum, sea_mask, depth, turning, from_west, from_east)


def shards(spectrum, depth_speed, turning, drift, partners, sea_slots, sea_counts):
    channels, grid_rows, grid_cols = spectrum.shape
    n_spec = lax.axis_size("spec")
    sub_rows = grid_rows // n_spec
    per_block = sub_rows * grid_cols
    sea_list = sea_slots[:, 0, :]
    sea_mask = sea_cells(sea_list, sea_counts[:, 0], per_block).reshape(grid_rows, grid_cols)
    edges_first, edges_last = edges(spectrum, sea_mask, depth_speed)
    from_west, from_east = neighbours(edges_first, edges_last)
    local_freq = channels // ND
    freq_ids = (
        lax.axis_index("spec") * local_freq + jnp.arange(local_freq, dtype=jnp.int32)
    ).astype(jnp.float32)
    speeds = jnp.repeat(speed_top * jnp.exp(-decline * freq_ids), ND)
    angles = 2.0 * jnp.pi * jnp.arange(ND, dtype=jnp.float32) / ND
    cosines = jnp.tile(jnp.cos(angles), local_freq)
    sine_part = jnp.tile(jnp.sin(angles), local_freq)
    coef = jnp.stack([speeds * cosines, speeds * sine_part])
    turned = propagate(spectrum, depth_speed, sea_mask, turning, from_west, from_east, coef)
    points = lax.all_to_all(turned, "spec", split_axis=0, concat_axis=0, tiled=True)
    grid = points.reshape(NF, sub_rows, ND, grid_cols)
    settled = settle(grid, drift, partners)
    return jnp.transpose(settled, (0, 2, 1, 3)).reshape(NF * ND, sub_rows, grid_cols)


def solution(mesh):
    return jax.shard_map(
        shards,
        mesh=mesh,
        in_specs=(
            P("spec", None, "tile"),
            P(None, "tile"),
            P(None, "tile"),
            P(),
            P(),
            P(None, "tile", None),
            P(None, "tile"),
        ),
        out_specs=P(None, "spec", "tile"),
        check_vma=False,
    )
```

```python
import jax
import jax.numpy as jnp
from jax import lax
from jax.sharding import PartitionSpec as P
from jax.experimental import pallas as pl
from jax.experimental.pallas import tpu as pltpu

ND = 36
NF = 32
PAD_DIR = 40


speed_top = 0.6
decline = 0.0953102
dia_coeff = 0.25


def extended(cells, sides, width):
    for axis, dim in sides:
        count = lax.axis_size(axis)
        head = lax.slice_in_dim(cells, 0, width, axis=dim)
        tail = lax.slice_in_dim(cells, cells.shape[dim] - width, cells.shape[dim], axis=dim)
        cells = jnp.concatenate(
            [
                lax.ppermute(tail, axis, [(i, (i + 1) % count) for i in range(count)]),
                cells,
                lax.ppermute(head, axis, [((i + 1) % count, i) for i in range(count)]),
            ],
            axis=dim,
        )
    return cells


def sea_cells(sea_list, sea_total, per_block):
    cell_ids = jnp.arange(per_block, dtype=jnp.int32)
    slot_rank = jnp.arange(sea_list.shape[1], dtype=jnp.int32)
    is_live = slot_rank[None, :] < sea_total[:, None]
    matches = (sea_list[:, :, None] == cell_ids[None, None, :]) & is_live[:, :, None]
    return jnp.any(matches, axis=1).astype(jnp.float32)


def advect_space(energy_ext, depth_ext, speeds, cosines, sine_part, sea_mask):
    east_rate = (speeds * cosines)[:, None, None] * depth_ext[None]
    north_rate = (speeds * sine_part)[:, None, None] * depth_ext[None, :, 1:-1]
    centre = energy_ext[:, :, 1:-1]
    east_mid = east_rate[:, :, 1:-1]
    inflow = (
        jnp.maximum(east_rate[:, :, :-2], 0.0) * energy_ext[:, :, :-2]
        + jnp.maximum(-east_rate[:, :, 2:], 0.0) * energy_ext[:, :, 2:]
    )
    empty_row = jnp.zeros_like(centre[:, :1])
    from_south = jnp.concatenate(
        [empty_row, (jnp.maximum(north_rate, 0.0) * centre)[:, :-1]], axis=1
    )
    from_north = jnp.concatenate(
        [(jnp.maximum(-north_rate, 0.0) * centre)[:, 1:], empty_row], axis=1
    )
    updated = (
        centre
        - (jnp.abs(east_mid) + jnp.abs(north_rate)) * centre
        + inflow
        + from_south
        + from_north
    )
    return updated * sea_mask


def advect_direction(energy, turning):
    turn_plus = jnp.maximum(turning, 0.0)
    behind = jnp.maximum(-turning, 0.0)
    return (
        energy
        - jnp.abs(turning) * energy
        + turn_plus * jnp.roll(energy, 1, axis=1)
        + behind * jnp.roll(energy, -1, axis=1)
    )


def advect_frequency(energy, drift, n_freq, n_dir):
    shaped = energy.reshape(n_freq, n_dir, -1)
    drift_rate = drift.reshape(n_freq, n_dir, 1)
    upward = jnp.maximum(drift_rate, 0.0) * shaped
    downward = jnp.maximum(-drift_rate, 0.0) * shaped
    empty_row = jnp.zeros_like(shaped[:1])
    from_below = jnp.concatenate([empty_row, upward[:-1]], axis=0)
    from_above = jnp.concatenate([downward[1:], empty_row], axis=0)
    return (shaped - jnp.abs(drift_rate) * shaped + from_below + from_above).reshape(energy.shape)


def shift_freq(x, s, up):
    if s == 0:
        return x
    n = x.shape[0]
    if up:
        return jnp.concatenate([x[s:], jnp.repeat(x[n - 1 :], s, axis=0)], axis=0)
    return jnp.concatenate([jnp.repeat(x[:1], s, axis=0), x[: n - s]], axis=0)


def pad_freq(x, s, up):
    if s == 0:
        return x
    n = x.shape[0]
    zeros = jnp.zeros_like(x[:s])
    if up:
        return jnp.concatenate([x[s:], zeros], axis=0)
    return jnp.concatenate([zeros, x[: n - s]], axis=0)


def pick_shift(choice, options):
    out = options[-1]
    for i in range(len(options) - 2, -1, -1):
        out = jnp.where(choice == i + 1, options[i], out)
    return out


def turn_rows(x, k):
    d = lax.broadcasted_iota(jnp.int32, x.shape, 0)
    ahead = pltpu.roll(x, PAD_DIR - k, 0)
    wrapped = pltpu.roll(x, ND - k, 0)
    return jnp.where(d + k < ND, ahead, wrapped)


def settle_kernel(table_ref, points_ref, drift_ref, out_ref, shifted_ref, quartet_ref, source_ref):
    n_freq = drift_ref.shape[0]
    sub_rows = points_ref.shape[0] // n_freq
    grid_cols = points_ref.shape[2]
    for r in range(sub_rows):

        def advect(f, carry):
            here = points_ref[f * sub_rows + r]
            rate = drift_ref[f]
            below = jnp.maximum(f - 1, 0)
            above = jnp.minimum(f + 1, n_freq - 1)
            from_below = jnp.where(
                f > 0, jnp.maximum(drift_ref[below], 0.0) * points_ref[below * sub_rows + r], 0.0
            )
            from_above = jnp.where(
                f < n_freq - 1,
                jnp.maximum(-drift_ref[above], 0.0) * points_ref[above * sub_rows + r],
                0.0,
            )
            shifted_ref[f] = here - jnp.abs(rate) * here + from_below + from_above
            source_ref[f] = jnp.zeros_like(here)
            return carry

        lax.fori_loop(0, n_freq, advect, 0)

        def interact(f, carry):
            up_freq = table_ref[0, f]
            down_freq = table_ref[1, f]
            up_turn = table_ref[2, f]
            down_turn = table_ref[3, f]
            here = shifted_ref[f]
            plus_values = turn_rows(shifted_ref[up_freq], up_turn)
            minus_values = turn_rows(shifted_ref[down_freq], ND - down_turn)
            quartet = (
                here * here * (plus_values + minus_values)
                - 2.0 * here * plus_values * minus_values
            )
            quartet_ref[f] = quartet
            source_ref[up_freq] = source_ref[up_freq] + turn_rows(quartet, ND - up_turn)
            source_ref[down_freq] = source_ref[down_freq] + turn_rows(quartet, down_turn)
            return carry

        lax.fori_loop(0, n_freq, interact, 0)

        def finish(f, carry):
            source = source_ref[f] - 2.0 * quartet_ref[f]
            value = shifted_ref[f] + dia_coeff * source
            out_ref[f, :, pl.ds(r * grid_cols, grid_cols)] = value[:ND]
            return carry

        lax.fori_loop(0, n_freq, finish, 0)


def settle(points, drift, partners):
    n_rows, _, grid_cols = points.shape
    sub_rows = n_rows // NF
    up_ids = partners[0].reshape(NF, ND)[:, 0]
    down_ids = partners[1].reshape(NF, ND)[:, 0]
    table = jnp.stack([up_ids // ND, down_ids // ND, up_ids % ND, ND - down_ids % ND])
    rates = jnp.pad(drift.reshape(NF, ND), ((0, 0), (0, PAD_DIR - ND)))
    rates = jnp.broadcast_to(rates[:, :, None], (NF, PAD_DIR, grid_cols))
    vmem = pl.BlockSpec(memory_space=pltpu.VMEM)
    block = pltpu.VMEM((NF, PAD_DIR, grid_cols), jnp.float32)
    out = pl.pallas_call(
        settle_kernel,
        out_shape=jax.ShapeDtypeStruct((NF, ND, sub_rows * grid_cols), jnp.float32),
        in_specs=[pl.BlockSpec(memory_space=pltpu.SMEM), vmem, vmem],
        out_specs=vmem,
        scratch_shapes=[block, block, block],
    )(table, points, rates)
    return out.reshape(NF * ND, sub_rows, grid_cols)


def neighbours(edges_first, edges_last):
    count = lax.axis_size("tile")
    from_west = lax.ppermute(edges_last, "tile", [(i, (i + 1) % count) for i in range(count)])
    from_east = lax.ppermute(edges_first, "tile", [((i + 1) % count, i) for i in range(count)])
    return from_west, from_east


def propagate_kernel(coef_ref, spec_ref, mask_ref, depth_ref, turn_ref, west_ref, east_ref, out_ref, spaced_ref):
    channels, grid_rows, grid_cols = spec_ref.shape
    mask = mask_ref[...]
    depth = depth_ref[...]
    west = west_ref[...]
    east = east_ref[...]
    col = lax.broadcasted_iota(jnp.int32, (grid_rows, grid_cols), 1)
    row = lax.broadcasted_iota(jnp.int32, (grid_rows, grid_cols), 0)
    first_col = col == 0
    last_col = col == grid_cols - 1
    first_row = row == 0
    last_row = row == grid_rows - 1
    west_depth = jnp.where(first_col, west[:, channels : channels + 1], pltpu.roll(depth, 1, 1))
    east_depth = jnp.where(last_col, east[:, channels : channels + 1], pltpu.roll(depth, grid_cols - 1, 1))
    for d in range(channels):
        energy = spec_ref[d] * mask
        west_energy = jnp.where(first_col, west[:, d : d + 1], pltpu.roll(energy, 1, 1))
        east_energy = jnp.where(last_col, east[:, d : d + 1], pltpu.roll(energy, grid_cols - 1, 1))
        east_coef = coef_ref[0, d]
        north_coef = coef_ref[1, d]
        east_mid = east_coef * depth
        north_rate = north_coef * depth
        inflow = (
            jnp.maximum(east_coef * west_depth, 0.0) * west_energy
            + jnp.maximum(-(east_coef * east_depth), 0.0) * east_energy
        )
        south_flux = jnp.maximum(north_rate, 0.0) * energy
        north_flux = jnp.maximum(-north_rate, 0.0) * energy
        from_south = jnp.where(first_row, 0.0, pltpu.roll(south_flux, 1, 0))
        from_north = jnp.where(last_row, 0.0, pltpu.roll(north_flux, grid_rows - 1, 0))
        updated = (
            energy
            - (jnp.abs(east_mid) + jnp.abs(north_rate)) * energy
            + inflow
            + from_south
            + from_north
        )
        spaced_ref[d] = updated * mask
    out_ref[:, channels:, :] = jnp.zeros((grid_rows, PAD_DIR - channels, grid_cols), jnp.float32)
    turning = turn_ref[...]
    turn_plus = jnp.maximum(turning, 0.0)
    behind = jnp.maximum(-turning, 0.0)
    turn_abs = jnp.abs(turning)
    for d in range(channels):
        here = spaced_ref[d]
        out_ref[:, d, :] = (
            here
            - turn_abs * here
            + turn_plus * spaced_ref[(d - 1) % channels]
            + behind * spaced_ref[(d + 1) % channels]
        )


def edges_kernel(spec_ref, mask_ref, depth_ref, first_ref, last_ref):
    channels, grid_rows, grid_cols = spec_ref.shape
    mask = mask_ref[...]
    depth = depth_ref[...]
    lane = lax.broadcasted_iota(jnp.int32, (grid_rows, grid_cols), 1)
    first = jnp.where(lane == channels, depth[:, :1], 0.0)
    last = jnp.where(lane == channels, depth[:, grid_cols - 1 :], 0.0)
    for d in range(channels):
        energy = spec_ref[d] * mask
        first = jnp.where(lane == d, energy[:, :1], first)
        last = jnp.where(lane == d, energy[:, grid_cols - 1 :], last)
    first_ref[...] = first
    last_ref[...] = last


def edges(spectrum, sea_mask, depth):
    vmem = pl.BlockSpec(memory_space=pltpu.VMEM)
    plane = jax.ShapeDtypeStruct(depth.shape, jnp.float32)
    return pl.pallas_call(
        edges_kernel,
        out_shape=(plane, plane),
        in_specs=[vmem] * 3,
        out_specs=(vmem, vmem),
    )(spectrum, sea_mask, depth)


def propagate(spectrum, depth, sea_mask, turning, from_west, from_east, coef):
    channels, grid_rows, grid_cols = spectrum.shape
    vmem = pl.BlockSpec(memory_space=pltpu.VMEM)
    return pl.pallas_call(
        propagate_kernel,
        out_shape=jax.ShapeDtypeStruct((grid_rows, PAD_DIR, grid_cols), jnp.float32),
        in_specs=[pl.BlockSpec(memory_space=pltpu.SMEM)] + [vmem] * 6,
        out_specs=vmem,
        scratch_shapes=[pltpu.VMEM(spectrum.shape, jnp.float32)],
    )(coef, spectrum, sea_mask, depth, turning, from_west, from_east)


def shards(spectrum, depth_speed, turning, drift, partners, sea_slots, sea_counts):
    channels, grid_rows, grid_cols = spectrum.shape
    n_spec = lax.axis_size("spec")
    sub_rows = grid_rows // n_spec
    per_block = sub_rows * grid_cols
    sea_list = sea_slots[:, 0, :]
    sea_mask = sea_cells(sea_list, sea_counts[:, 0], per_block).reshape(grid_rows, grid_cols)
    edges_first, edges_last = edges(spectrum, sea_mask, depth_speed)
    from_west, from_east = neighbours(edges_first, edges_last)
    local_freq = channels // ND
    freq_ids = (
        lax.axis_index("spec") * local_freq + jnp.arange(local_freq, dtype=jnp.int32)
    ).astype(jnp.float32)
    speeds = jnp.repeat(speed_top * jnp.exp(-decline * freq_ids), ND)
    angles = 2.0 * jnp.pi * jnp.arange(ND, dtype=jnp.float32) / ND
    cosines = jnp.tile(jnp.cos(angles), local_freq)
    sine_part = jnp.tile(jnp.sin(angles), local_freq)
    coef = jnp.stack([speeds * cosines, speeds * sine_part])
    turned = propagate(spectrum, depth_speed, sea_mask, turning, from_west, from_east, coef)
    points = lax.all_to_all(turned, "spec", split_axis=0, concat_axis=0, tiled=True)
    return settle(points, drift, partners)


def solution(mesh):
    return jax.shard_map(
        shards,
        mesh=mesh,
        in_specs=(
            P("spec", None, "tile"),
            P(None, "tile"),
            P(None, "tile"),
            P(),
            P(),
            P(None, "tile", None),
            P(None, "tile"),
        ),
        out_specs=P(None, "spec", "tile"),
        check_vma=False,
    )
```

```python
import jax
import jax.numpy as jnp
from jax import lax
from jax.sharding import PartitionSpec as P
from jax.experimental import pallas as pl
from jax.experimental.pallas import tpu as pltpu

ND = 36
NF = 32
PAD_DIR = 40


speed_top = 0.6
decline = 0.0953102
dia_coeff = 0.25


def extended(cells, sides, width):
    for axis, dim in sides:
        count = lax.axis_size(axis)
        head = lax.slice_in_dim(cells, 0, width, axis=dim)
        tail = lax.slice_in_dim(cells, cells.shape[dim] - width, cells.shape[dim], axis=dim)
        cells = jnp.concatenate(
            [
                lax.ppermute(tail, axis, [(i, (i + 1) % count) for i in range(count)]),
                cells,
                lax.ppermute(head, axis, [((i + 1) % count, i) for i in range(count)]),
            ],
            axis=dim,
        )
    return cells


def sea_cells(sea_list, sea_total, per_block):
    cell_ids = jnp.arange(per_block, dtype=jnp.int32)
    slot_rank = jnp.arange(sea_list.shape[1], dtype=jnp.int32)
    is_live = slot_rank[None, :] < sea_total[:, None]
    matches = (sea_list[:, :, None] == cell_ids[None, None, :]) & is_live[:, :, None]
    return jnp.any(matches, axis=1).astype(jnp.float32)


def advect_space(energy_ext, depth_ext, speeds, cosines, sine_part, sea_mask):
    east_rate = (speeds * cosines)[:, None, None] * depth_ext[None]
    north_rate = (speeds * sine_part)[:, None, None] * depth_ext[None, :, 1:-1]
    centre = energy_ext[:, :, 1:-1]
    east_mid = east_rate[:, :, 1:-1]
    inflow = (
        jnp.maximum(east_rate[:, :, :-2], 0.0) * energy_ext[:, :, :-2]
        + jnp.maximum(-east_rate[:, :, 2:], 0.0) * energy_ext[:, :, 2:]
    )
    empty_row = jnp.zeros_like(centre[:, :1])
    from_south = jnp.concatenate(
        [empty_row, (jnp.maximum(north_rate, 0.0) * centre)[:, :-1]], axis=1
    )
    from_north = jnp.concatenate(
        [(jnp.maximum(-north_rate, 0.0) * centre)[:, 1:], empty_row], axis=1
    )
    updated = (
        centre
        - (jnp.abs(east_mid) + jnp.abs(north_rate)) * centre
        + inflow
        + from_south
        + from_north
    )
    return updated * sea_mask


def advect_direction(energy, turning):
    turn_plus = jnp.maximum(turning, 0.0)
    behind = jnp.maximum(-turning, 0.0)
    return (
        energy
        - jnp.abs(turning) * energy
        + turn_plus * jnp.roll(energy, 1, axis=1)
        + behind * jnp.roll(energy, -1, axis=1)
    )


def advect_frequency(energy, drift, n_freq, n_dir):
    shaped = energy.reshape(n_freq, n_dir, -1)
    drift_rate = drift.reshape(n_freq, n_dir, 1)
    upward = jnp.maximum(drift_rate, 0.0) * shaped
    downward = jnp.maximum(-drift_rate, 0.0) * shaped
    empty_row = jnp.zeros_like(shaped[:1])
    from_below = jnp.concatenate([empty_row, upward[:-1]], axis=0)
    from_above = jnp.concatenate([downward[1:], empty_row], axis=0)
    return (shaped - jnp.abs(drift_rate) * shaped + from_below + from_above).reshape(energy.shape)


def shift_freq(x, s, up):
    if s == 0:
        return x
    n = x.shape[0]
    if up:
        return jnp.concatenate([x[s:], jnp.repeat(x[n - 1 :], s, axis=0)], axis=0)
    return jnp.concatenate([jnp.repeat(x[:1], s, axis=0), x[: n - s]], axis=0)


def pad_freq(x, s, up):
    if s == 0:
        return x
    n = x.shape[0]
    zeros = jnp.zeros_like(x[:s])
    if up:
        return jnp.concatenate([x[s:], zeros], axis=0)
    return jnp.concatenate([zeros, x[: n - s]], axis=0)


def pick_shift(choice, options):
    out = options[-1]
    for i in range(len(options) - 2, -1, -1):
        out = jnp.where(choice == i + 1, options[i], out)
    return out


def turn_rows(x, k):
    d = lax.broadcasted_iota(jnp.int32, x.shape, 0)
    ahead = pltpu.roll(x, PAD_DIR - k, 0)
    wrapped = pltpu.roll(x, ND - k, 0)
    return jnp.where(d + k < ND, ahead, wrapped)


def settle_kernel(table_ref, points_ref, drift_ref, out_ref, shifted_ref, quartet_ref, source_ref):
    n_freq = drift_ref.shape[0]
    sub_rows = points_ref.shape[0] // n_freq
    for r in range(sub_rows):

        def advect(f, carry):
            here = points_ref[f * sub_rows + r]
            rate = drift_ref[f]
            below = jnp.maximum(f - 1, 0)
            above = jnp.minimum(f + 1, n_freq - 1)
            from_below = jnp.where(
                f > 0, jnp.maximum(drift_ref[below], 0.0) * points_ref[below * sub_rows + r], 0.0
            )
            from_above = jnp.where(
                f < n_freq - 1,
                jnp.maximum(-drift_ref[above], 0.0) * points_ref[above * sub_rows + r],
                0.0,
            )
            shifted_ref[f] = here - jnp.abs(rate) * here + from_below + from_above
            source_ref[f] = jnp.zeros_like(here)
            return carry

        lax.fori_loop(0, n_freq, advect, 0, unroll=True)

        def interact(f, carry):
            up_freq = table_ref[0, f]
            down_freq = table_ref[1, f]
            up_turn = table_ref[2, f]
            down_turn = table_ref[3, f]
            here = shifted_ref[f]
            plus_values = turn_rows(shifted_ref[up_freq], up_turn)
            minus_values = turn_rows(shifted_ref[down_freq], ND - down_turn)
            quartet = (
                here * here * (plus_values + minus_values)
                - 2.0 * here * plus_values * minus_values
            )
            quartet_ref[f] = quartet
            source_ref[up_freq] = source_ref[up_freq] + turn_rows(quartet, ND - up_turn)
            source_ref[down_freq] = source_ref[down_freq] + turn_rows(quartet, down_turn)
            return carry

        lax.fori_loop(0, n_freq, interact, 0, unroll=True)

        def finish(f, carry):
            source = source_ref[f] - 2.0 * quartet_ref[f]
            value = shifted_ref[f] + dia_coeff * source
            out_ref[pl.ds(f * ND, ND), r, :] = value[:ND]
            return carry

        lax.fori_loop(0, n_freq, finish, 0, unroll=True)


def settle(points, drift, partners):
    n_rows, _, grid_cols = points.shape
    sub_rows = n_rows // NF
    up_ids = partners[0].reshape(NF, ND)[:, 0]
    down_ids = partners[1].reshape(NF, ND)[:, 0]
    table = jnp.stack([up_ids // ND, down_ids // ND, up_ids % ND, ND - down_ids % ND])
    rates = jnp.pad(drift.reshape(NF, ND), ((0, 0), (0, PAD_DIR - ND)))
    rates = jnp.broadcast_to(rates[:, :, None], (NF, PAD_DIR, grid_cols))
    vmem = pl.BlockSpec(memory_space=pltpu.VMEM)
    block = pltpu.VMEM((NF, PAD_DIR, grid_cols), jnp.float32)
    out = pl.pallas_call(
        settle_kernel,
        out_shape=jax.ShapeDtypeStruct((NF * ND, sub_rows, grid_cols), jnp.float32),
        in_specs=[pl.BlockSpec(memory_space=pltpu.SMEM), vmem, vmem],
        out_specs=vmem,
        scratch_shapes=[block, block, block],
    )(table, points, rates)
    return out


def neighbours(edges_first, edges_last):
    count = lax.axis_size("tile")
    from_west = lax.ppermute(edges_last, "tile", [(i, (i + 1) % count) for i in range(count)])
    from_east = lax.ppermute(edges_first, "tile", [((i + 1) % count, i) for i in range(count)])
    return from_west, from_east


def propagate_kernel(coef_ref, spec_ref, mask_ref, depth_ref, turn_ref, west_ref, east_ref, out_ref, spaced_ref):
    channels, grid_rows, grid_cols = spec_ref.shape
    mask = mask_ref[...]
    depth = depth_ref[...]
    west = west_ref[...]
    east = east_ref[...]
    col = lax.broadcasted_iota(jnp.int32, (grid_rows, grid_cols), 1)
    row = lax.broadcasted_iota(jnp.int32, (grid_rows, grid_cols), 0)
    first_col = col == 0
    last_col = col == grid_cols - 1
    first_row = row == 0
    last_row = row == grid_rows - 1
    west_depth = jnp.where(first_col, west[:, channels : channels + 1], pltpu.roll(depth, 1, 1))
    east_depth = jnp.where(last_col, east[:, channels : channels + 1], pltpu.roll(depth, grid_cols - 1, 1))
    for d in range(channels):
        energy = spec_ref[d] * mask
        west_energy = jnp.where(first_col, west[:, d : d + 1], pltpu.roll(energy, 1, 1))
        east_energy = jnp.where(last_col, east[:, d : d + 1], pltpu.roll(energy, grid_cols - 1, 1))
        east_coef = coef_ref[0, d]
        north_coef = coef_ref[1, d]
        east_mid = east_coef * depth
        north_rate = north_coef * depth
        inflow = (
            jnp.maximum(east_coef * west_depth, 0.0) * west_energy
            + jnp.maximum(-(east_coef * east_depth), 0.0) * east_energy
        )
        south_flux = jnp.maximum(north_rate, 0.0) * energy
        north_flux = jnp.maximum(-north_rate, 0.0) * energy
        from_south = jnp.where(first_row, 0.0, pltpu.roll(south_flux, 1, 0))
        from_north = jnp.where(last_row, 0.0, pltpu.roll(north_flux, grid_rows - 1, 0))
        updated = (
            energy
            - (jnp.abs(east_mid) + jnp.abs(north_rate)) * energy
            + inflow
            + from_south
            + from_north
        )
        spaced_ref[d] = updated * mask
    out_ref[:, channels:, :] = jnp.zeros((grid_rows, PAD_DIR - channels, grid_cols), jnp.float32)
    turning = turn_ref[...]
    turn_plus = jnp.maximum(turning, 0.0)
    behind = jnp.maximum(-turning, 0.0)
    turn_abs = jnp.abs(turning)
    for d in range(channels):
        here = spaced_ref[d]
        out_ref[:, d, :] = (
            here
            - turn_abs * here
            + turn_plus * spaced_ref[(d - 1) % channels]
            + behind * spaced_ref[(d + 1) % channels]
        )


def edges_kernel(spec_ref, mask_ref, depth_ref, first_ref, last_ref):
    channels, grid_rows, grid_cols = spec_ref.shape
    mask = mask_ref[...]
    depth = depth_ref[...]
    lane = lax.broadcasted_iota(jnp.int32, (grid_rows, grid_cols), 1)
    first = jnp.where(lane == channels, depth[:, :1], 0.0)
    last = jnp.where(lane == channels, depth[:, grid_cols - 1 :], 0.0)
    for d in range(channels):
        energy = spec_ref[d] * mask
        first = jnp.where(lane == d, energy[:, :1], first)
        last = jnp.where(lane == d, energy[:, grid_cols - 1 :], last)
    first_ref[...] = first
    last_ref[...] = last


def edges(spectrum, sea_mask, depth):
    vmem = pl.BlockSpec(memory_space=pltpu.VMEM)
    plane = jax.ShapeDtypeStruct(depth.shape, jnp.float32)
    return pl.pallas_call(
        edges_kernel,
        out_shape=(plane, plane),
        in_specs=[vmem] * 3,
        out_specs=(vmem, vmem),
    )(spectrum, sea_mask, depth)


def propagate(spectrum, depth, sea_mask, turning, from_west, from_east, coef):
    channels, grid_rows, grid_cols = spectrum.shape
    vmem = pl.BlockSpec(memory_space=pltpu.VMEM)
    return pl.pallas_call(
        propagate_kernel,
        out_shape=jax.ShapeDtypeStruct((grid_rows, PAD_DIR, grid_cols), jnp.float32),
        in_specs=[pl.BlockSpec(memory_space=pltpu.SMEM)] + [vmem] * 6,
        out_specs=vmem,
        scratch_shapes=[pltpu.VMEM(spectrum.shape, jnp.float32)],
    )(coef, spectrum, sea_mask, depth, turning, from_west, from_east)


def shards(spectrum, depth_speed, turning, drift, partners, sea_slots, sea_counts):
    channels, grid_rows, grid_cols = spectrum.shape
    n_spec = lax.axis_size("spec")
    sub_rows = grid_rows // n_spec
    per_block = sub_rows * grid_cols
    sea_list = sea_slots[:, 0, :]
    sea_mask = sea_cells(sea_list, sea_counts[:, 0], per_block).reshape(grid_rows, grid_cols)
    edges_first, edges_last = edges(spectrum, sea_mask, depth_speed)
    from_west, from_east = neighbours(edges_first, edges_last)
    local_freq = channels // ND
    freq_ids = (
        lax.axis_index("spec") * local_freq + jnp.arange(local_freq, dtype=jnp.int32)
    ).astype(jnp.float32)
    speeds = jnp.repeat(speed_top * jnp.exp(-decline * freq_ids), ND)
    angles = 2.0 * jnp.pi * jnp.arange(ND, dtype=jnp.float32) / ND
    cosines = jnp.tile(jnp.cos(angles), local_freq)
    sine_part = jnp.tile(jnp.sin(angles), local_freq)
    coef = jnp.stack([speeds * cosines, speeds * sine_part])
    turned = propagate(spectrum, depth_speed, sea_mask, turning, from_west, from_east, coef)
    points = lax.all_to_all(turned, "spec", split_axis=0, concat_axis=0, tiled=True)
    return settle(points, drift, partners)


def solution(mesh):
    return jax.shard_map(
        shards,
        mesh=mesh,
        in_specs=(
            P("spec", None, "tile"),
            P(None, "tile"),
            P(None, "tile"),
            P(),
            P(),
            P(None, "tile", None),
            P(None, "tile"),
        ),
        out_specs=P(None, "spec", "tile"),
        check_vma=False,
    )
```

```python
import jax
import jax.numpy as jnp
from jax import lax
from jax.sharding import PartitionSpec as P
from jax.experimental import pallas as pl
from jax.experimental.pallas import tpu as pltpu

ND = 36
NF = 32
PAD_DIR = 40


speed_top = 0.6
decline = 0.0953102
dia_coeff = 0.25


def extended(cells, sides, width):
    for axis, dim in sides:
        count = lax.axis_size(axis)
        head = lax.slice_in_dim(cells, 0, width, axis=dim)
        tail = lax.slice_in_dim(cells, cells.shape[dim] - width, cells.shape[dim], axis=dim)
        cells = jnp.concatenate(
            [
                lax.ppermute(tail, axis, [(i, (i + 1) % count) for i in range(count)]),
                cells,
                lax.ppermute(head, axis, [((i + 1) % count, i) for i in range(count)]),
            ],
            axis=dim,
        )
    return cells


def edge_cells(sea_list, sea_total, sub_rows, grid_cols):
    slot_rank = jnp.arange(sea_list.shape[1], dtype=jnp.int32)
    is_live = slot_rank[None, :] < sea_total[:, None]
    rows = jnp.arange(sub_rows, dtype=jnp.int32)[:, None] * grid_cols
    cells = rows + jnp.array([0, grid_cols - 1], dtype=jnp.int32)[None, :]
    matches = (sea_list[:, None, None, :] == cells[None, :, :, None]) & is_live[:, None, None, :]
    return jnp.any(matches, axis=3).astype(jnp.float32).reshape(-1, 2)


def sea_cells(sea_list, sea_total, per_block):
    cell_ids = jnp.arange(per_block, dtype=jnp.int32)
    slot_rank = jnp.arange(sea_list.shape[1], dtype=jnp.int32)
    is_live = slot_rank[None, :] < sea_total[:, None]
    matches = (sea_list[:, :, None] == cell_ids[None, None, :]) & is_live[:, :, None]
    return jnp.any(matches, axis=1).astype(jnp.float32)


def advect_space(energy_ext, depth_ext, speeds, cosines, sine_part, sea_mask):
    east_rate = (speeds * cosines)[:, None, None] * depth_ext[None]
    north_rate = (speeds * sine_part)[:, None, None] * depth_ext[None, :, 1:-1]
    centre = energy_ext[:, :, 1:-1]
    east_mid = east_rate[:, :, 1:-1]
    inflow = (
        jnp.maximum(east_rate[:, :, :-2], 0.0) * energy_ext[:, :, :-2]
        + jnp.maximum(-east_rate[:, :, 2:], 0.0) * energy_ext[:, :, 2:]
    )
    empty_row = jnp.zeros_like(centre[:, :1])
    from_south = jnp.concatenate(
        [empty_row, (jnp.maximum(north_rate, 0.0) * centre)[:, :-1]], axis=1
    )
    from_north = jnp.concatenate(
        [(jnp.maximum(-north_rate, 0.0) * centre)[:, 1:], empty_row], axis=1
    )
    updated = (
        centre
        - (jnp.abs(east_mid) + jnp.abs(north_rate)) * centre
        + inflow
        + from_south
        + from_north
    )
    return updated * sea_mask


def advect_direction(energy, turning):
    turn_plus = jnp.maximum(turning, 0.0)
    behind = jnp.maximum(-turning, 0.0)
    return (
        energy
        - jnp.abs(turning) * energy
        + turn_plus * jnp.roll(energy, 1, axis=1)
        + behind * jnp.roll(energy, -1, axis=1)
    )


def advect_frequency(energy, drift, n_freq, n_dir):
    shaped = energy.reshape(n_freq, n_dir, -1)
    drift_rate = drift.reshape(n_freq, n_dir, 1)
    upward = jnp.maximum(drift_rate, 0.0) * shaped
    downward = jnp.maximum(-drift_rate, 0.0) * shaped
    empty_row = jnp.zeros_like(shaped[:1])
    from_below = jnp.concatenate([empty_row, upward[:-1]], axis=0)
    from_above = jnp.concatenate([downward[1:], empty_row], axis=0)
    return (shaped - jnp.abs(drift_rate) * shaped + from_below + from_above).reshape(energy.shape)


def shift_freq(x, s, up):
    if s == 0:
        return x
    n = x.shape[0]
    if up:
        return jnp.concatenate([x[s:], jnp.repeat(x[n - 1 :], s, axis=0)], axis=0)
    return jnp.concatenate([jnp.repeat(x[:1], s, axis=0), x[: n - s]], axis=0)


def pad_freq(x, s, up):
    if s == 0:
        return x
    n = x.shape[0]
    zeros = jnp.zeros_like(x[:s])
    if up:
        return jnp.concatenate([x[s:], zeros], axis=0)
    return jnp.concatenate([zeros, x[: n - s]], axis=0)


def pick_shift(choice, options):
    out = options[-1]
    for i in range(len(options) - 2, -1, -1):
        out = jnp.where(choice == i + 1, options[i], out)
    return out


def turn_rows(x, k):
    d = lax.broadcasted_iota(jnp.int32, x.shape, 0)
    ahead = pltpu.roll(x, PAD_DIR - k, 0)
    wrapped = pltpu.roll(x, ND - k, 0)
    return jnp.where(d + k < ND, ahead, wrapped)


def settle_kernel(table_ref, points_ref, drift_ref, out_ref, shifted_ref, quartet_ref, source_ref):
    n_freq = drift_ref.shape[0]
    sub_rows = points_ref.shape[0] // n_freq
    for r in range(sub_rows):

        def advect(f, carry):
            here = points_ref[f * sub_rows + r]
            rate = drift_ref[f]
            below = jnp.maximum(f - 1, 0)
            above = jnp.minimum(f + 1, n_freq - 1)
            from_below = jnp.where(
                f > 0, jnp.maximum(drift_ref[below], 0.0) * points_ref[below * sub_rows + r], 0.0
            )
            from_above = jnp.where(
                f < n_freq - 1,
                jnp.maximum(-drift_ref[above], 0.0) * points_ref[above * sub_rows + r],
                0.0,
            )
            shifted_ref[f] = here - jnp.abs(rate) * here + from_below + from_above
            source_ref[f] = jnp.zeros_like(here)
            return carry

        lax.fori_loop(0, n_freq, advect, 0, unroll=True)

        def interact(f, carry):
            up_freq = table_ref[0, f]
            down_freq = table_ref[1, f]
            up_turn = table_ref[2, f]
            down_turn = table_ref[3, f]
            here = shifted_ref[f]
            plus_values = turn_rows(shifted_ref[up_freq], up_turn)
            minus_values = turn_rows(shifted_ref[down_freq], ND - down_turn)
            quartet = (
                here * here * (plus_values + minus_values)
                - 2.0 * here * plus_values * minus_values
            )
            quartet_ref[f] = quartet
            source_ref[up_freq] = source_ref[up_freq] + turn_rows(quartet, ND - up_turn)
            source_ref[down_freq] = source_ref[down_freq] + turn_rows(quartet, down_turn)
            return carry

        lax.fori_loop(0, n_freq, interact, 0, unroll=True)

        def finish(f, carry):
            source = source_ref[f] - 2.0 * quartet_ref[f]
            value = shifted_ref[f] + dia_coeff * source
            out_ref[pl.ds(f * ND, ND), r, :] = value[:ND]
            return carry

        lax.fori_loop(0, n_freq, finish, 0, unroll=True)


def settle(points, drift, partners):
    n_rows, _, grid_cols = points.shape
    sub_rows = n_rows // NF
    up_ids = partners[0].reshape(NF, ND)[:, 0]
    down_ids = partners[1].reshape(NF, ND)[:, 0]
    table = jnp.stack([up_ids // ND, down_ids // ND, up_ids % ND, ND - down_ids % ND])
    rates = jnp.pad(drift.reshape(NF, ND), ((0, 0), (0, PAD_DIR - ND)))
    rates = jnp.broadcast_to(rates[:, :, None], (NF, PAD_DIR, grid_cols))
    vmem = pl.BlockSpec(memory_space=pltpu.VMEM)
    block = pltpu.VMEM((NF, PAD_DIR, grid_cols), jnp.float32)
    out = pl.pallas_call(
        settle_kernel,
        out_shape=jax.ShapeDtypeStruct((NF * ND, sub_rows, grid_cols), jnp.float32),
        in_specs=[pl.BlockSpec(memory_space=pltpu.SMEM), vmem, vmem],
        out_specs=vmem,
        scratch_shapes=[block, block, block],
    )(table, points, rates)
    return out


def neighbours(edges_first, edges_last):
    count = lax.axis_size("tile")
    from_west = lax.ppermute(edges_last, "tile", [(i, (i + 1) % count) for i in range(count)])
    from_east = lax.ppermute(edges_first, "tile", [((i + 1) % count, i) for i in range(count)])
    return from_west, from_east


def propagate_kernel(coef_ref, spec_ref, mask_ref, depth_ref, turn_ref, west_ref, east_ref, out_ref, spaced_ref):
    channels, grid_rows, grid_cols = spec_ref.shape
    mask = mask_ref[...]
    depth = depth_ref[...]
    west = west_ref[...]
    east = east_ref[...]
    col = lax.broadcasted_iota(jnp.int32, (grid_rows, grid_cols), 1)
    row = lax.broadcasted_iota(jnp.int32, (grid_rows, grid_cols), 0)
    first_col = col == 0
    last_col = col == grid_cols - 1
    first_row = row == 0
    last_row = row == grid_rows - 1
    west_depth = jnp.where(first_col, west[:, channels : channels + 1], pltpu.roll(depth, 1, 1))
    east_depth = jnp.where(last_col, east[:, channels : channels + 1], pltpu.roll(depth, grid_cols - 1, 1))
    for d in range(channels):
        energy = spec_ref[d] * mask
        west_energy = jnp.where(first_col, west[:, d : d + 1], pltpu.roll(energy, 1, 1))
        east_energy = jnp.where(last_col, east[:, d : d + 1], pltpu.roll(energy, grid_cols - 1, 1))
        east_coef = coef_ref[0, d]
        north_coef = coef_ref[1, d]
        east_mid = east_coef * depth
        north_rate = north_coef * depth
        inflow = (
            jnp.maximum(east_coef * west_depth, 0.0) * west_energy
            + jnp.maximum(-(east_coef * east_depth), 0.0) * east_energy
        )
        south_flux = jnp.maximum(north_rate, 0.0) * energy
        north_flux = jnp.maximum(-north_rate, 0.0) * energy
        from_south = jnp.where(first_row, 0.0, pltpu.roll(south_flux, 1, 0))
        from_north = jnp.where(last_row, 0.0, pltpu.roll(north_flux, grid_rows - 1, 0))
        updated = (
            energy
            - (jnp.abs(east_mid) + jnp.abs(north_rate)) * energy
            + inflow
            + from_south
            + from_north
        )
        spaced_ref[d] = updated * mask
    out_ref[:, channels:, :] = jnp.zeros((grid_rows, PAD_DIR - channels, grid_cols), jnp.float32)
    turning = turn_ref[...]
    turn_plus = jnp.maximum(turning, 0.0)
    behind = jnp.maximum(-turning, 0.0)
    turn_abs = jnp.abs(turning)
    for d in range(channels):
        here = spaced_ref[d]
        out_ref[:, d, :] = (
            here
            - turn_abs * here
            + turn_plus * spaced_ref[(d - 1) % channels]
            + behind * spaced_ref[(d + 1) % channels]
        )


def edges_kernel(spec_ref, mask_ref, depth_ref, first_ref, last_ref):
    channels, grid_rows, grid_cols = spec_ref.shape
    edge_mask = mask_ref[...]
    depth = depth_ref[...]
    lane = lax.broadcasted_iota(jnp.int32, (grid_rows, grid_cols), 1)
    first = jnp.where(lane == channels, depth[:, :1], 0.0)
    last = jnp.where(lane == channels, depth[:, grid_cols - 1 :], 0.0)
    for d in range(channels):
        plane = spec_ref[d]
        first = jnp.where(lane == d, plane[:, :1] * edge_mask[:, :1], first)
        last = jnp.where(lane == d, plane[:, grid_cols - 1 :] * edge_mask[:, 1:], last)
    first_ref[...] = first
    last_ref[...] = last


def edges(spectrum, edge_mask, depth):
    vmem = pl.BlockSpec(memory_space=pltpu.VMEM)
    plane = jax.ShapeDtypeStruct(depth.shape, jnp.float32)
    return pl.pallas_call(
        edges_kernel,
        out_shape=(plane, plane),
        in_specs=[vmem] * 3,
        out_specs=(vmem, vmem),
    )(spectrum, edge_mask, depth)


def propagate(spectrum, depth, sea_mask, turning, from_west, from_east, coef):
    channels, grid_rows, grid_cols = spectrum.shape
    vmem = pl.BlockSpec(memory_space=pltpu.VMEM)
    return pl.pallas_call(
        propagate_kernel,
        out_shape=jax.ShapeDtypeStruct((grid_rows, PAD_DIR, grid_cols), jnp.float32),
        in_specs=[pl.BlockSpec(memory_space=pltpu.SMEM)] + [vmem] * 6,
        out_specs=vmem,
        scratch_shapes=[pltpu.VMEM(spectrum.shape, jnp.float32)],
    )(coef, spectrum, sea_mask, depth, turning, from_west, from_east)


def shards(spectrum, depth_speed, turning, drift, partners, sea_slots, sea_counts):
    channels, grid_rows, grid_cols = spectrum.shape
    n_spec = lax.axis_size("spec")
    sub_rows = grid_rows // n_spec
    per_block = sub_rows * grid_cols
    sea_list = sea_slots[:, 0, :]
    sea_mask = sea_cells(sea_list, sea_counts[:, 0], per_block).reshape(grid_rows, grid_cols)
    edge_mask = edge_cells(sea_list, sea_counts[:, 0], sub_rows, grid_cols)
    edges_first, edges_last = edges(spectrum, edge_mask, depth_speed)
    from_west, from_east = neighbours(edges_first, edges_last)
    local_freq = channels // ND
    freq_ids = (
        lax.axis_index("spec") * local_freq + jnp.arange(local_freq, dtype=jnp.int32)
    ).astype(jnp.float32)
    speeds = jnp.repeat(speed_top * jnp.exp(-decline * freq_ids), ND)
    angles = 2.0 * jnp.pi * jnp.arange(ND, dtype=jnp.float32) / ND
    cosines = jnp.tile(jnp.cos(angles), local_freq)
    sine_part = jnp.tile(jnp.sin(angles), local_freq)
    coef = jnp.stack([speeds * cosines, speeds * sine_part])
    turned = propagate(spectrum, depth_speed, sea_mask, turning, from_west, from_east, coef)
    points = lax.all_to_all(turned, "spec", split_axis=0, concat_axis=0, tiled=True)
    return settle(points, drift, partners)


def solution(mesh):
    return jax.shard_map(
        shards,
        mesh=mesh,
        in_specs=(
            P("spec", None, "tile"),
            P(None, "tile"),
            P(None, "tile"),
            P(),
            P(),
            P(None, "tile", None),
            P(None, "tile"),
        ),
        out_specs=P(None, "spec", "tile"),
        check_vma=False,
    )
```

```python
import jax
import jax.numpy as jnp
from jax import lax
from jax.sharding import PartitionSpec as P
from jax.experimental import pallas as pl
from jax.experimental.pallas import tpu as pltpu

ND = 36
NF = 32
PAD_DIR = 40


speed_top = 0.6
decline = 0.0953102
dia_coeff = 0.25


def extended(cells, sides, width):
    for axis, dim in sides:
        count = lax.axis_size(axis)
        head = lax.slice_in_dim(cells, 0, width, axis=dim)
        tail = lax.slice_in_dim(cells, cells.shape[dim] - width, cells.shape[dim], axis=dim)
        cells = jnp.concatenate(
            [
                lax.ppermute(tail, axis, [(i, (i + 1) % count) for i in range(count)]),
                cells,
                lax.ppermute(head, axis, [((i + 1) % count, i) for i in range(count)]),
            ],
            axis=dim,
        )
    return cells


def edge_cells(sea_list, sea_total, sub_rows, grid_cols):
    slot_rank = jnp.arange(sea_list.shape[1], dtype=jnp.int32)
    is_live = slot_rank[None, :] < sea_total[:, None]
    rows = jnp.arange(sub_rows, dtype=jnp.int32)[:, None] * grid_cols
    cells = rows + jnp.array([0, grid_cols - 1], dtype=jnp.int32)[None, :]
    matches = (sea_list[:, None, None, :] == cells[None, :, :, None]) & is_live[:, None, None, :]
    return jnp.any(matches, axis=3).astype(jnp.float32).reshape(-1, 2)


def sea_cells(sea_list, sea_total, per_block):
    cell_ids = jnp.arange(per_block, dtype=jnp.int32)
    slot_rank = jnp.arange(sea_list.shape[1], dtype=jnp.int32)
    is_live = slot_rank[None, :] < sea_total[:, None]
    matches = (sea_list[:, :, None] == cell_ids[None, None, :]) & is_live[:, :, None]
    return jnp.any(matches, axis=1).astype(jnp.float32)


def advect_space(energy_ext, depth_ext, speeds, cosines, sine_part, sea_mask):
    east_rate = (speeds * cosines)[:, None, None] * depth_ext[None]
    north_rate = (speeds * sine_part)[:, None, None] * depth_ext[None, :, 1:-1]
    centre = energy_ext[:, :, 1:-1]
    east_mid = east_rate[:, :, 1:-1]
    inflow = (
        jnp.maximum(east_rate[:, :, :-2], 0.0) * energy_ext[:, :, :-2]
        + jnp.maximum(-east_rate[:, :, 2:], 0.0) * energy_ext[:, :, 2:]
    )
    empty_row = jnp.zeros_like(centre[:, :1])
    from_south = jnp.concatenate(
        [empty_row, (jnp.maximum(north_rate, 0.0) * centre)[:, :-1]], axis=1
    )
    from_north = jnp.concatenate(
        [(jnp.maximum(-north_rate, 0.0) * centre)[:, 1:], empty_row], axis=1
    )
    updated = (
        centre
        - (jnp.abs(east_mid) + jnp.abs(north_rate)) * centre
        + inflow
        + from_south
        + from_north
    )
    return updated * sea_mask


def advect_direction(energy, turning):
    turn_plus = jnp.maximum(turning, 0.0)
    behind = jnp.maximum(-turning, 0.0)
    return (
        energy
        - jnp.abs(turning) * energy
        + turn_plus * jnp.roll(energy, 1, axis=1)
        + behind * jnp.roll(energy, -1, axis=1)
    )


def advect_frequency(energy, drift, n_freq, n_dir):
    shaped = energy.reshape(n_freq, n_dir, -1)
    drift_rate = drift.reshape(n_freq, n_dir, 1)
    upward = jnp.maximum(drift_rate, 0.0) * shaped
    downward = jnp.maximum(-drift_rate, 0.0) * shaped
    empty_row = jnp.zeros_like(shaped[:1])
    from_below = jnp.concatenate([empty_row, upward[:-1]], axis=0)
    from_above = jnp.concatenate([downward[1:], empty_row], axis=0)
    return (shaped - jnp.abs(drift_rate) * shaped + from_below + from_above).reshape(energy.shape)


def shift_freq(x, s, up):
    if s == 0:
        return x
    n = x.shape[0]
    if up:
        return jnp.concatenate([x[s:], jnp.repeat(x[n - 1 :], s, axis=0)], axis=0)
    return jnp.concatenate([jnp.repeat(x[:1], s, axis=0), x[: n - s]], axis=0)


def pad_freq(x, s, up):
    if s == 0:
        return x
    n = x.shape[0]
    zeros = jnp.zeros_like(x[:s])
    if up:
        return jnp.concatenate([x[s:], zeros], axis=0)
    return jnp.concatenate([zeros, x[: n - s]], axis=0)


def pick_shift(choice, options):
    out = options[-1]
    for i in range(len(options) - 2, -1, -1):
        out = jnp.where(choice == i + 1, options[i], out)
    return out


def turn_rows(x, k):
    d = lax.broadcasted_iota(jnp.int32, x.shape, 0)
    ahead = pltpu.roll(x, PAD_DIR - k, 0)
    wrapped = pltpu.roll(x, ND - k, 0)
    return jnp.where(d + k < ND, ahead, wrapped)


def settle_kernel(
    table_ref, blocks_ref, drift_ref, out_ref, points_ref, shifted_ref, quartet_ref, source_ref
):
    n_freq = drift_ref.shape[0]
    sub_rows = blocks_ref.shape[1] // ND
    for r in range(sub_rows):
        start = r * ND // 8 * 8
        offset = r * ND - start

        def align(f, carry):
            block = blocks_ref[f, pl.ds(start, PAD_DIR), :]
            if offset:
                block = pltpu.roll(block, PAD_DIR - offset, 0)
            points_ref[f * sub_rows + r] = block
            return carry

        lax.fori_loop(0, n_freq, align, 0, unroll=True)

    for r in range(sub_rows):

        def advect(f, carry):
            here = points_ref[f * sub_rows + r]
            rate = drift_ref[f]
            below = jnp.maximum(f - 1, 0)
            above = jnp.minimum(f + 1, n_freq - 1)
            from_below = jnp.where(
                f > 0, jnp.maximum(drift_ref[below], 0.0) * points_ref[below * sub_rows + r], 0.0
            )
            from_above = jnp.where(
                f < n_freq - 1,
                jnp.maximum(-drift_ref[above], 0.0) * points_ref[above * sub_rows + r],
                0.0,
            )
            shifted_ref[f] = here - jnp.abs(rate) * here + from_below + from_above
            source_ref[f] = jnp.zeros_like(here)
            return carry

        lax.fori_loop(0, n_freq, advect, 0, unroll=True)

        def interact(f, carry):
            up_freq = table_ref[0, f]
            down_freq = table_ref[1, f]
            up_turn = table_ref[2, f]
            down_turn = table_ref[3, f]
            here = shifted_ref[f]
            plus_values = turn_rows(shifted_ref[up_freq], up_turn)
            minus_values = turn_rows(shifted_ref[down_freq], ND - down_turn)
            quartet = (
                here * here * (plus_values + minus_values)
                - 2.0 * here * plus_values * minus_values
            )
            quartet_ref[f] = quartet
            source_ref[up_freq] = source_ref[up_freq] + turn_rows(quartet, ND - up_turn)
            source_ref[down_freq] = source_ref[down_freq] + turn_rows(quartet, down_turn)
            return carry

        lax.fori_loop(0, n_freq, interact, 0, unroll=True)

        def finish(f, carry):
            source = source_ref[f] - 2.0 * quartet_ref[f]
            value = shifted_ref[f] + dia_coeff * source
            out_ref[pl.ds(f * ND, ND), r, :] = value[:ND]
            return carry

        lax.fori_loop(0, n_freq, finish, 0, unroll=True)


def settle(points, drift, partners):
    _, block_rows, grid_cols = points.shape
    sub_rows = block_rows // ND
    up_ids = partners[0].reshape(NF, ND)[:, 0]
    down_ids = partners[1].reshape(NF, ND)[:, 0]
    table = jnp.stack([up_ids // ND, down_ids // ND, up_ids % ND, ND - down_ids % ND])
    rates = jnp.pad(drift.reshape(NF, ND), ((0, 0), (0, PAD_DIR - ND)))
    rates = jnp.broadcast_to(rates[:, :, None], (NF, PAD_DIR, grid_cols))
    vmem = pl.BlockSpec(memory_space=pltpu.VMEM)
    block = pltpu.VMEM((NF, PAD_DIR, grid_cols), jnp.float32)
    out = pl.pallas_call(
        settle_kernel,
        out_shape=jax.ShapeDtypeStruct((NF * ND, sub_rows, grid_cols), jnp.float32),
        in_specs=[pl.BlockSpec(memory_space=pltpu.SMEM), vmem, vmem],
        out_specs=vmem,
        scratch_shapes=[pltpu.VMEM((NF * sub_rows, PAD_DIR, grid_cols), jnp.float32), block, block, block],
    )(table, points, rates)
    return out


def neighbours(edges_first, edges_last):
    count = lax.axis_size("tile")
    from_west = lax.ppermute(edges_last, "tile", [(i, (i + 1) % count) for i in range(count)])
    from_east = lax.ppermute(edges_first, "tile", [((i + 1) % count, i) for i in range(count)])
    return from_west, from_east


def propagate_kernel(
    coef_ref, spec_ref, mask_ref, depth_ref, turn_ref, west_ref, east_ref, out_ref, spaced_ref, plane_ref
):
    channels, grid_rows, grid_cols = spec_ref.shape
    mask = mask_ref[...]
    depth = depth_ref[...]
    west = west_ref[...]
    east = east_ref[...]
    col = lax.broadcasted_iota(jnp.int32, (grid_rows, grid_cols), 1)
    row = lax.broadcasted_iota(jnp.int32, (grid_rows, grid_cols), 0)
    first_col = col == 0
    last_col = col == grid_cols - 1
    first_row = row == 0
    last_row = row == grid_rows - 1
    west_depth = jnp.where(first_col, west[:, channels : channels + 1], pltpu.roll(depth, 1, 1))
    east_depth = jnp.where(last_col, east[:, channels : channels + 1], pltpu.roll(depth, grid_cols - 1, 1))
    for d in range(channels):
        energy = spec_ref[d] * mask
        west_energy = jnp.where(first_col, west[:, d : d + 1], pltpu.roll(energy, 1, 1))
        east_energy = jnp.where(last_col, east[:, d : d + 1], pltpu.roll(energy, grid_cols - 1, 1))
        east_coef = coef_ref[0, d]
        north_coef = coef_ref[1, d]
        east_mid = east_coef * depth
        north_rate = north_coef * depth
        inflow = (
            jnp.maximum(east_coef * west_depth, 0.0) * west_energy
            + jnp.maximum(-(east_coef * east_depth), 0.0) * east_energy
        )
        south_flux = jnp.maximum(north_rate, 0.0) * energy
        north_flux = jnp.maximum(-north_rate, 0.0) * energy
        from_south = jnp.where(first_row, 0.0, pltpu.roll(south_flux, 1, 0))
        from_north = jnp.where(last_row, 0.0, pltpu.roll(north_flux, grid_rows - 1, 0))
        updated = (
            energy
            - (jnp.abs(east_mid) + jnp.abs(north_rate)) * energy
            + inflow
            + from_south
            + from_north
        )
        spaced_ref[d] = updated * mask
    blocks = out_ref.shape[0]
    sub_rows = out_ref.shape[1] // channels
    turning = turn_ref[...]
    turn_plus = jnp.maximum(turning, 0.0)
    behind = jnp.maximum(-turning, 0.0)
    turn_abs = jnp.abs(turning)
    for d in range(channels):
        here = spaced_ref[d]
        plane_ref[...] = (
            here
            - turn_abs * here
            + turn_plus * spaced_ref[(d - 1) % channels]
            + behind * spaced_ref[(d + 1) % channels]
        )
        for r in range(sub_rows):
            out_ref[:, r * channels + d, :] = plane_ref[pl.ds(r, blocks, stride=sub_rows), :]


def edges_kernel(spec_ref, mask_ref, depth_ref, first_ref, last_ref):
    channels, grid_rows, grid_cols = spec_ref.shape
    edge_mask = mask_ref[...]
    depth = depth_ref[...]
    lane = lax.broadcasted_iota(jnp.int32, (grid_rows, grid_cols), 1)
    first = jnp.where(lane == channels, depth[:, :1], 0.0)
    last = jnp.where(lane == channels, depth[:, grid_cols - 1 :], 0.0)
    for d in range(channels):
        plane = spec_ref[d]
        first = jnp.where(lane == d, plane[:, :1] * edge_mask[:, :1], first)
        last = jnp.where(lane == d, plane[:, grid_cols - 1 :] * edge_mask[:, 1:], last)
    first_ref[...] = first
    last_ref[...] = last


def edges(spectrum, edge_mask, depth):
    vmem = pl.BlockSpec(memory_space=pltpu.VMEM)
    plane = jax.ShapeDtypeStruct(depth.shape, jnp.float32)
    return pl.pallas_call(
        edges_kernel,
        out_shape=(plane, plane),
        in_specs=[vmem] * 3,
        out_specs=(vmem, vmem),
    )(spectrum, edge_mask, depth)


def propagate(spectrum, depth, sea_mask, turning, from_west, from_east, coef, blocks):
    channels, grid_rows, grid_cols = spectrum.shape
    vmem = pl.BlockSpec(memory_space=pltpu.VMEM)
    return pl.pallas_call(
        propagate_kernel,
        out_shape=jax.ShapeDtypeStruct((blocks, grid_rows // blocks * channels, grid_cols), jnp.float32),
        in_specs=[pl.BlockSpec(memory_space=pltpu.SMEM)] + [vmem] * 6,
        out_specs=vmem,
        scratch_shapes=[
            pltpu.VMEM(spectrum.shape, jnp.float32),
            pltpu.VMEM((grid_rows, grid_cols), jnp.float32),
        ],
    )(coef, spectrum, sea_mask, depth, turning, from_west, from_east)


def shards(spectrum, depth_speed, turning, drift, partners, sea_slots, sea_counts):
    channels, grid_rows, grid_cols = spectrum.shape
    n_spec = lax.axis_size("spec")
    sub_rows = grid_rows // n_spec
    per_block = sub_rows * grid_cols
    sea_list = sea_slots[:, 0, :]
    sea_mask = sea_cells(sea_list, sea_counts[:, 0], per_block).reshape(grid_rows, grid_cols)
    edge_mask = edge_cells(sea_list, sea_counts[:, 0], sub_rows, grid_cols)
    edges_first, edges_last = edges(spectrum, edge_mask, depth_speed)
    from_west, from_east = neighbours(edges_first, edges_last)
    local_freq = channels // ND
    freq_ids = (
        lax.axis_index("spec") * local_freq + jnp.arange(local_freq, dtype=jnp.int32)
    ).astype(jnp.float32)
    speeds = jnp.repeat(speed_top * jnp.exp(-decline * freq_ids), ND)
    angles = 2.0 * jnp.pi * jnp.arange(ND, dtype=jnp.float32) / ND
    cosines = jnp.tile(jnp.cos(angles), local_freq)
    sine_part = jnp.tile(jnp.sin(angles), local_freq)
    coef = jnp.stack([speeds * cosines, speeds * sine_part])
    turned = propagate(
        spectrum, depth_speed, sea_mask, turning, from_west, from_east, coef, n_spec
    )
    points = lax.all_to_all(turned, "spec", split_axis=0, concat_axis=0, tiled=True)
    return settle(points, drift, partners)


def solution(mesh):
    return jax.shard_map(
        shards,
        mesh=mesh,
        in_specs=(
            P("spec", None, "tile"),
            P(None, "tile"),
            P(None, "tile"),
            P(),
            P(),
            P(None, "tile", None),
            P(None, "tile"),
        ),
        out_specs=P(None, "spec", "tile"),
        check_vma=False,
    )
```

```python
import jax
import jax.numpy as jnp
from jax import lax
from jax.sharding import PartitionSpec as P
from jax.experimental import pallas as pl
from jax.experimental.pallas import tpu as pltpu

ND = 36
NF = 32
PAD_DIR = 40


speed_top = 0.6
decline = 0.0953102
dia_coeff = 0.25


def extended(cells, sides, width):
    for axis, dim in sides:
        count = lax.axis_size(axis)
        head = lax.slice_in_dim(cells, 0, width, axis=dim)
        tail = lax.slice_in_dim(cells, cells.shape[dim] - width, cells.shape[dim], axis=dim)
        cells = jnp.concatenate(
            [
                lax.ppermute(tail, axis, [(i, (i + 1) % count) for i in range(count)]),
                cells,
                lax.ppermute(head, axis, [((i + 1) % count, i) for i in range(count)]),
            ],
            axis=dim,
        )
    return cells


def edge_cells(sea_list, sea_total, sub_rows, grid_cols):
    slot_rank = jnp.arange(sea_list.shape[1], dtype=jnp.int32)
    is_live = slot_rank[None, :] < sea_total[:, None]
    rows = jnp.arange(sub_rows, dtype=jnp.int32)[:, None] * grid_cols
    cells = rows + jnp.array([0, grid_cols - 1], dtype=jnp.int32)[None, :]
    matches = (sea_list[:, None, None, :] == cells[None, :, :, None]) & is_live[:, None, None, :]
    return jnp.any(matches, axis=3).astype(jnp.float32).reshape(-1, 2)


def sea_cells(sea_list, sea_total, per_block):
    cell_ids = jnp.arange(per_block, dtype=jnp.int32)
    slot_rank = jnp.arange(sea_list.shape[1], dtype=jnp.int32)
    is_live = slot_rank[None, :] < sea_total[:, None]
    matches = (sea_list[:, :, None] == cell_ids[None, None, :]) & is_live[:, :, None]
    return jnp.any(matches, axis=1).astype(jnp.float32)


def advect_space(energy_ext, depth_ext, speeds, cosines, sine_part, sea_mask):
    east_rate = (speeds * cosines)[:, None, None] * depth_ext[None]
    north_rate = (speeds * sine_part)[:, None, None] * depth_ext[None, :, 1:-1]
    centre = energy_ext[:, :, 1:-1]
    east_mid = east_rate[:, :, 1:-1]
    inflow = (
        jnp.maximum(east_rate[:, :, :-2], 0.0) * energy_ext[:, :, :-2]
        + jnp.maximum(-east_rate[:, :, 2:], 0.0) * energy_ext[:, :, 2:]
    )
    empty_row = jnp.zeros_like(centre[:, :1])
    from_south = jnp.concatenate(
        [empty_row, (jnp.maximum(north_rate, 0.0) * centre)[:, :-1]], axis=1
    )
    from_north = jnp.concatenate(
        [(jnp.maximum(-north_rate, 0.0) * centre)[:, 1:], empty_row], axis=1
    )
    updated = (
        centre
        - (jnp.abs(east_mid) + jnp.abs(north_rate)) * centre
        + inflow
        + from_south
        + from_north
    )
    return updated * sea_mask


def advect_direction(energy, turning):
    turn_plus = jnp.maximum(turning, 0.0)
    behind = jnp.maximum(-turning, 0.0)
    return (
        energy
        - jnp.abs(turning) * energy
        + turn_plus * jnp.roll(energy, 1, axis=1)
        + behind * jnp.roll(energy, -1, axis=1)
    )


def advect_frequency(energy, drift, n_freq, n_dir):
    shaped = energy.reshape(n_freq, n_dir, -1)
    drift_rate = drift.reshape(n_freq, n_dir, 1)
    upward = jnp.maximum(drift_rate, 0.0) * shaped
    downward = jnp.maximum(-drift_rate, 0.0) * shaped
    empty_row = jnp.zeros_like(shaped[:1])
    from_below = jnp.concatenate([empty_row, upward[:-1]], axis=0)
    from_above = jnp.concatenate([downward[1:], empty_row], axis=0)
    return (shaped - jnp.abs(drift_rate) * shaped + from_below + from_above).reshape(energy.shape)


def shift_freq(x, s, up):
    if s == 0:
        return x
    n = x.shape[0]
    if up:
        return jnp.concatenate([x[s:], jnp.repeat(x[n - 1 :], s, axis=0)], axis=0)
    return jnp.concatenate([jnp.repeat(x[:1], s, axis=0), x[: n - s]], axis=0)


def pad_freq(x, s, up):
    if s == 0:
        return x
    n = x.shape[0]
    zeros = jnp.zeros_like(x[:s])
    if up:
        return jnp.concatenate([x[s:], zeros], axis=0)
    return jnp.concatenate([zeros, x[: n - s]], axis=0)


def pick_shift(choice, options):
    out = options[-1]
    for i in range(len(options) - 2, -1, -1):
        out = jnp.where(choice == i + 1, options[i], out)
    return out


def turn_rows(x, k):
    d = lax.broadcasted_iota(jnp.int32, x.shape, 0)
    ahead = pltpu.roll(x, PAD_DIR - k, 0)
    wrapped = pltpu.roll(x, ND - k, 0)
    return jnp.where(d + k < ND, ahead, wrapped)


def settle_kernel(
    table_ref, blocks_ref, drift_ref, out_ref, points_ref, shifted_ref, quartet_ref, source_ref
):
    n_freq = blocks_ref.shape[0]
    sub_rows = blocks_ref.shape[1] // ND
    for r in range(sub_rows):
        start = r * ND // 8 * 8
        offset = r * ND - start

        def align(f, carry):
            block = blocks_ref[f, pl.ds(start, PAD_DIR), :]
            if offset:
                block = pltpu.roll(block, PAD_DIR - offset, 0)
            points_ref[f * sub_rows + r] = block
            return carry

        lax.fori_loop(0, n_freq, align, 0, unroll=True)

    for r in range(sub_rows):

        for f in range(n_freq):
            here = points_ref[f * sub_rows + r]
            rate = drift_ref[:, f : f + 1]
            shifted = here - jnp.abs(rate) * here
            if f > 0:
                below = points_ref[(f - 1) * sub_rows + r]
                shifted = shifted + jnp.maximum(drift_ref[:, f - 1 : f], 0.0) * below
            if f < n_freq - 1:
                above = points_ref[(f + 1) * sub_rows + r]
                shifted = shifted + jnp.maximum(-drift_ref[:, f + 1 : f + 2], 0.0) * above
            shifted_ref[f] = shifted
            source_ref[f] = jnp.zeros_like(here)

        def interact(f, carry):
            up_freq = table_ref[0, f]
            down_freq = table_ref[1, f]
            up_turn = table_ref[2, f]
            down_turn = table_ref[3, f]
            here = shifted_ref[f]
            plus_values = turn_rows(shifted_ref[up_freq], up_turn)
            minus_values = turn_rows(shifted_ref[down_freq], ND - down_turn)
            quartet = (
                here * here * (plus_values + minus_values)
                - 2.0 * here * plus_values * minus_values
            )
            quartet_ref[f] = quartet
            source_ref[up_freq] = source_ref[up_freq] + turn_rows(quartet, ND - up_turn)
            source_ref[down_freq] = source_ref[down_freq] + turn_rows(quartet, down_turn)
            return carry

        lax.fori_loop(0, n_freq, interact, 0, unroll=True)

        def finish(f, carry):
            source = source_ref[f] - 2.0 * quartet_ref[f]
            value = shifted_ref[f] + dia_coeff * source
            out_ref[pl.ds(f * ND, ND), r, :] = value[:ND]
            return carry

        lax.fori_loop(0, n_freq, finish, 0, unroll=True)


def settle(points, drift, partners):
    _, block_rows, grid_cols = points.shape
    sub_rows = block_rows // ND
    up_ids = partners[0].reshape(NF, ND)[:, 0]
    down_ids = partners[1].reshape(NF, ND)[:, 0]
    table = jnp.stack([up_ids // ND, down_ids // ND, up_ids % ND, ND - down_ids % ND])
    rates = jnp.pad(drift.reshape(NF, ND).T, ((0, PAD_DIR - ND), (0, grid_cols - NF)))
    vmem = pl.BlockSpec(memory_space=pltpu.VMEM)
    block = pltpu.VMEM((NF, PAD_DIR, grid_cols), jnp.float32)
    out = pl.pallas_call(
        settle_kernel,
        out_shape=jax.ShapeDtypeStruct((NF * ND, sub_rows, grid_cols), jnp.float32),
        in_specs=[pl.BlockSpec(memory_space=pltpu.SMEM), vmem, vmem],
        out_specs=vmem,
        scratch_shapes=[pltpu.VMEM((NF * sub_rows, PAD_DIR, grid_cols), jnp.float32), block, block, block],
    )(table, points, rates)
    return out


def neighbours(edges_first, edges_last):
    count = lax.axis_size("tile")
    from_west = lax.ppermute(edges_last, "tile", [(i, (i + 1) % count) for i in range(count)])
    from_east = lax.ppermute(edges_first, "tile", [((i + 1) % count, i) for i in range(count)])
    return from_west, from_east


def propagate_kernel(
    coef_ref, spec_ref, mask_ref, depth_ref, turn_ref, west_ref, east_ref, out_ref, spaced_ref, plane_ref
):
    channels, grid_rows, grid_cols = spec_ref.shape
    mask = mask_ref[...]
    depth = depth_ref[...]
    west = west_ref[...]
    east = east_ref[...]
    col = lax.broadcasted_iota(jnp.int32, (grid_rows, grid_cols), 1)
    row = lax.broadcasted_iota(jnp.int32, (grid_rows, grid_cols), 0)
    first_col = col == 0
    last_col = col == grid_cols - 1
    first_row = row == 0
    last_row = row == grid_rows - 1
    west_depth = jnp.where(first_col, west[:, channels : channels + 1], pltpu.roll(depth, 1, 1))
    east_depth = jnp.where(last_col, east[:, channels : channels + 1], pltpu.roll(depth, grid_cols - 1, 1))
    for d in range(channels):
        energy = spec_ref[d] * mask
        west_energy = jnp.where(first_col, west[:, d : d + 1], pltpu.roll(energy, 1, 1))
        east_energy = jnp.where(last_col, east[:, d : d + 1], pltpu.roll(energy, grid_cols - 1, 1))
        east_coef = coef_ref[0, d]
        north_coef = coef_ref[1, d]
        east_mid = east_coef * depth
        north_rate = north_coef * depth
        inflow = (
            jnp.maximum(east_coef * west_depth, 0.0) * west_energy
            + jnp.maximum(-(east_coef * east_depth), 0.0) * east_energy
        )
        south_flux = jnp.maximum(north_rate, 0.0) * energy
        north_flux = jnp.maximum(-north_rate, 0.0) * energy
        from_south = jnp.where(first_row, 0.0, pltpu.roll(south_flux, 1, 0))
        from_north = jnp.where(last_row, 0.0, pltpu.roll(north_flux, grid_rows - 1, 0))
        updated = (
            energy
            - (jnp.abs(east_mid) + jnp.abs(north_rate)) * energy
            + inflow
            + from_south
            + from_north
        )
        spaced_ref[d] = updated * mask
    blocks = out_ref.shape[0]
    sub_rows = out_ref.shape[1] // channels
    turning = turn_ref[...]
    turn_plus = jnp.maximum(turning, 0.0)
    behind = jnp.maximum(-turning, 0.0)
    turn_abs = jnp.abs(turning)
    for d in range(channels):
        here = spaced_ref[d]
        plane_ref[...] = (
            here
            - turn_abs * here
            + turn_plus * spaced_ref[(d - 1) % channels]
            + behind * spaced_ref[(d + 1) % channels]
        )
        for r in range(sub_rows):
            out_ref[:, r * channels + d, :] = plane_ref[pl.ds(r, blocks, stride=sub_rows), :]


def edges_kernel(spec_ref, mask_ref, depth_ref, first_ref, last_ref):
    channels, grid_rows, grid_cols = spec_ref.shape
    edge_mask = mask_ref[...]
    depth = depth_ref[...]
    lane = lax.broadcasted_iota(jnp.int32, (grid_rows, grid_cols), 1)
    first = jnp.where(lane == channels, depth[:, :1], 0.0)
    last = jnp.where(lane == channels, depth[:, grid_cols - 1 :], 0.0)
    for d in range(channels):
        plane = spec_ref[d]
        first = jnp.where(lane == d, plane[:, :1] * edge_mask[:, :1], first)
        last = jnp.where(lane == d, plane[:, grid_cols - 1 :] * edge_mask[:, 1:], last)
    first_ref[...] = first
    last_ref[...] = last


def edges(spectrum, edge_mask, depth):
    vmem = pl.BlockSpec(memory_space=pltpu.VMEM)
    plane = jax.ShapeDtypeStruct(depth.shape, jnp.float32)
    return pl.pallas_call(
        edges_kernel,
        out_shape=(plane, plane),
        in_specs=[vmem] * 3,
        out_specs=(vmem, vmem),
    )(spectrum, edge_mask, depth)


def propagate(spectrum, depth, sea_mask, turning, from_west, from_east, coef, blocks):
    channels, grid_rows, grid_cols = spectrum.shape
    vmem = pl.BlockSpec(memory_space=pltpu.VMEM)
    return pl.pallas_call(
        propagate_kernel,
        out_shape=jax.ShapeDtypeStruct((blocks, grid_rows // blocks * channels, grid_cols), jnp.float32),
        in_specs=[pl.BlockSpec(memory_space=pltpu.SMEM)] + [vmem] * 6,
        out_specs=vmem,
        scratch_shapes=[
            pltpu.VMEM(spectrum.shape, jnp.float32),
            pltpu.VMEM((grid_rows, grid_cols), jnp.float32),
        ],
    )(coef, spectrum, sea_mask, depth, turning, from_west, from_east)


def shards(spectrum, depth_speed, turning, drift, partners, sea_slots, sea_counts):
    channels, grid_rows, grid_cols = spectrum.shape
    n_spec = lax.axis_size("spec")
    sub_rows = grid_rows // n_spec
    per_block = sub_rows * grid_cols
    sea_list = sea_slots[:, 0, :]
    sea_mask = sea_cells(sea_list, sea_counts[:, 0], per_block).reshape(grid_rows, grid_cols)
    edge_mask = edge_cells(sea_list, sea_counts[:, 0], sub_rows, grid_cols)
    edges_first, edges_last = edges(spectrum, edge_mask, depth_speed)
    from_west, from_east = neighbours(edges_first, edges_last)
    local_freq = channels // ND
    freq_ids = (
        lax.axis_index("spec") * local_freq + jnp.arange(local_freq, dtype=jnp.int32)
    ).astype(jnp.float32)
    speeds = jnp.repeat(speed_top * jnp.exp(-decline * freq_ids), ND)
    angles = 2.0 * jnp.pi * jnp.arange(ND, dtype=jnp.float32) / ND
    cosines = jnp.tile(jnp.cos(angles), local_freq)
    sine_part = jnp.tile(jnp.sin(angles), local_freq)
    coef = jnp.stack([speeds * cosines, speeds * sine_part])
    turned = propagate(
        spectrum, depth_speed, sea_mask, turning, from_west, from_east, coef, n_spec
    )
    points = lax.all_to_all(turned, "spec", split_axis=0, concat_axis=0, tiled=True)
    return settle(points, drift, partners)


def solution(mesh):
    return jax.shard_map(
        shards,
        mesh=mesh,
        in_specs=(
            P("spec", None, "tile"),
            P(None, "tile"),
            P(None, "tile"),
            P(),
            P(),
            P(None, "tile", None),
            P(None, "tile"),
        ),
        out_specs=P(None, "spec", "tile"),
        check_vma=False,
    )
```

```python
import jax
import jax.numpy as jnp
from jax import lax
from jax.sharding import PartitionSpec as P
from jax.experimental import pallas as pl
from jax.experimental.pallas import tpu as pltpu

ND = 36
NF = 32
PAD_DIR = 40


speed_top = 0.6
decline = 0.0953102
dia_coeff = 0.25


def extended(cells, sides, width):
    for axis, dim in sides:
        count = lax.axis_size(axis)
        head = lax.slice_in_dim(cells, 0, width, axis=dim)
        tail = lax.slice_in_dim(cells, cells.shape[dim] - width, cells.shape[dim], axis=dim)
        cells = jnp.concatenate(
            [
                lax.ppermute(tail, axis, [(i, (i + 1) % count) for i in range(count)]),
                cells,
                lax.ppermute(head, axis, [((i + 1) % count, i) for i in range(count)]),
            ],
            axis=dim,
        )
    return cells


def edge_cells(sea_list, sea_total, sub_rows, grid_cols):
    slot_rank = jnp.arange(sea_list.shape[1], dtype=jnp.int32)
    is_live = slot_rank[None, :] < sea_total[:, None]
    rows = jnp.arange(sub_rows, dtype=jnp.int32)[:, None] * grid_cols
    cells = rows + jnp.array([0, grid_cols - 1], dtype=jnp.int32)[None, :]
    matches = (sea_list[:, None, None, :] == cells[None, :, :, None]) & is_live[:, None, None, :]
    return jnp.any(matches, axis=3).astype(jnp.float32).reshape(-1, 2)


def sea_cells(sea_list, sea_total, per_block):
    cell_ids = jnp.arange(per_block, dtype=jnp.int32)
    slot_rank = jnp.arange(sea_list.shape[1], dtype=jnp.int32)
    is_live = slot_rank[None, :] < sea_total[:, None]
    matches = (sea_list[:, :, None] == cell_ids[None, None, :]) & is_live[:, :, None]
    return jnp.any(matches, axis=1).astype(jnp.float32)


def advect_space(energy_ext, depth_ext, speeds, cosines, sine_part, sea_mask):
    east_rate = (speeds * cosines)[:, None, None] * depth_ext[None]
    north_rate = (speeds * sine_part)[:, None, None] * depth_ext[None, :, 1:-1]
    centre = energy_ext[:, :, 1:-1]
    east_mid = east_rate[:, :, 1:-1]
    inflow = (
        jnp.maximum(east_rate[:, :, :-2], 0.0) * energy_ext[:, :, :-2]
        + jnp.maximum(-east_rate[:, :, 2:], 0.0) * energy_ext[:, :, 2:]
    )
    empty_row = jnp.zeros_like(centre[:, :1])
    from_south = jnp.concatenate(
        [empty_row, (jnp.maximum(north_rate, 0.0) * centre)[:, :-1]], axis=1
    )
    from_north = jnp.concatenate(
        [(jnp.maximum(-north_rate, 0.0) * centre)[:, 1:], empty_row], axis=1
    )
    updated = (
        centre
        - (jnp.abs(east_mid) + jnp.abs(north_rate)) * centre
        + inflow
        + from_south
        + from_north
    )
    return updated * sea_mask


def advect_direction(energy, turning):
    turn_plus = jnp.maximum(turning, 0.0)
    behind = jnp.maximum(-turning, 0.0)
    return (
        energy
        - jnp.abs(turning) * energy
        + turn_plus * jnp.roll(energy, 1, axis=1)
        + behind * jnp.roll(energy, -1, axis=1)
    )


def advect_frequency(energy, drift, n_freq, n_dir):
    shaped = energy.reshape(n_freq, n_dir, -1)
    drift_rate = drift.reshape(n_freq, n_dir, 1)
    upward = jnp.maximum(drift_rate, 0.0) * shaped
    downward = jnp.maximum(-drift_rate, 0.0) * shaped
    empty_row = jnp.zeros_like(shaped[:1])
    from_below = jnp.concatenate([empty_row, upward[:-1]], axis=0)
    from_above = jnp.concatenate([downward[1:], empty_row], axis=0)
    return (shaped - jnp.abs(drift_rate) * shaped + from_below + from_above).reshape(energy.shape)


def shift_freq(x, s, up):
    if s == 0:
        return x
    n = x.shape[0]
    if up:
        return jnp.concatenate([x[s:], jnp.repeat(x[n - 1 :], s, axis=0)], axis=0)
    return jnp.concatenate([jnp.repeat(x[:1], s, axis=0), x[: n - s]], axis=0)


def pad_freq(x, s, up):
    if s == 0:
        return x
    n = x.shape[0]
    zeros = jnp.zeros_like(x[:s])
    if up:
        return jnp.concatenate([x[s:], zeros], axis=0)
    return jnp.concatenate([zeros, x[: n - s]], axis=0)


def pick_shift(choice, options):
    out = options[-1]
    for i in range(len(options) - 2, -1, -1):
        out = jnp.where(choice == i + 1, options[i], out)
    return out


def turn_rows(x, k):
    d = lax.broadcasted_iota(jnp.int32, x.shape, 0)
    ahead = pltpu.roll(x, PAD_DIR - k, 0)
    wrapped = pltpu.roll(x, ND - k, 0)
    return jnp.where(d + k < ND, ahead, wrapped)


def settle_kernel(
    table_ref, blocks_ref, drift_ref, out_ref, points_ref, shifted_ref, quartet_ref, source_ref
):
    n_freq = blocks_ref.shape[0]
    sub_rows = blocks_ref.shape[1] // ND
    for r in range(sub_rows):
        start = r * ND // 8 * 8
        offset = r * ND - start

        def align(f, carry):
            block = blocks_ref[f, pl.ds(start, PAD_DIR), :]
            if offset:
                block = pltpu.roll(block, PAD_DIR - offset, 0)
            points_ref[f * sub_rows + r] = block
            return carry

        lax.fori_loop(0, n_freq, align, 0, unroll=True)

    for r in range(sub_rows):

        for f in range(n_freq):
            here = points_ref[f * sub_rows + r]
            rate = drift_ref[:, f : f + 1]
            shifted = here - jnp.abs(rate) * here
            if f > 0:
                below = points_ref[(f - 1) * sub_rows + r]
                shifted = shifted + jnp.maximum(drift_ref[:, f - 1 : f], 0.0) * below
            if f < n_freq - 1:
                above = points_ref[(f + 1) * sub_rows + r]
                shifted = shifted + jnp.maximum(-drift_ref[:, f + 1 : f + 2], 0.0) * above
            shifted_ref[f * sub_rows + r] = shifted
            source_ref[f * sub_rows + r] = jnp.zeros_like(here)

        def interact(f, carry):
            up_freq = table_ref[0, f]
            down_freq = table_ref[1, f]
            up_turn = table_ref[2, f]
            down_turn = table_ref[3, f]
            here = shifted_ref[f * sub_rows + r]
            plus_values = turn_rows(shifted_ref[up_freq * sub_rows + r], up_turn)
            minus_values = turn_rows(shifted_ref[down_freq * sub_rows + r], ND - down_turn)
            quartet = (
                here * here * (plus_values + minus_values)
                - 2.0 * here * plus_values * minus_values
            )
            quartet_ref[f * sub_rows + r] = quartet
            up_at = up_freq * sub_rows + r
            down_at = down_freq * sub_rows + r
            source_ref[up_at] = source_ref[up_at] + turn_rows(quartet, ND - up_turn)
            source_ref[down_at] = source_ref[down_at] + turn_rows(quartet, down_turn)
            return carry

        lax.fori_loop(0, n_freq, interact, 0, unroll=True)

    def finish(f, carry):
        values = []
        for r in range(sub_rows):
            at = f * sub_rows + r
            source = source_ref[at] - 2.0 * quartet_ref[at]
            values.append((shifted_ref[at] + dia_coeff * source)[:ND])
        out_ref[pl.ds(f * ND, ND), :, :] = jnp.stack(values, axis=1)
        return carry

    lax.fori_loop(0, n_freq, finish, 0, unroll=True)


def settle(points, drift, partners):
    _, block_rows, grid_cols = points.shape
    sub_rows = block_rows // ND
    up_ids = partners[0].reshape(NF, ND)[:, 0]
    down_ids = partners[1].reshape(NF, ND)[:, 0]
    table = jnp.stack([up_ids // ND, down_ids // ND, up_ids % ND, ND - down_ids % ND])
    rates = jnp.pad(drift.reshape(NF, ND).T, ((0, PAD_DIR - ND), (0, grid_cols - NF)))
    vmem = pl.BlockSpec(memory_space=pltpu.VMEM)
    block = pltpu.VMEM((NF * sub_rows, PAD_DIR, grid_cols), jnp.float32)
    out = pl.pallas_call(
        settle_kernel,
        out_shape=jax.ShapeDtypeStruct((NF * ND, sub_rows, grid_cols), jnp.float32),
        in_specs=[pl.BlockSpec(memory_space=pltpu.SMEM), vmem, vmem],
        out_specs=vmem,
        scratch_shapes=[block, block, block, block],
    )(table, points, rates)
    return out


def neighbours(edges_first, edges_last):
    count = lax.axis_size("tile")
    from_west = lax.ppermute(edges_last, "tile", [(i, (i + 1) % count) for i in range(count)])
    from_east = lax.ppermute(edges_first, "tile", [((i + 1) % count, i) for i in range(count)])
    return from_west, from_east


def propagate_kernel(
    coef_ref, spec_ref, mask_ref, depth_ref, turn_ref, west_ref, east_ref, out_ref, spaced_ref, plane_ref
):
    channels, grid_rows, grid_cols = spec_ref.shape
    mask = mask_ref[...]
    depth = depth_ref[...]
    west = west_ref[...]
    east = east_ref[...]
    col = lax.broadcasted_iota(jnp.int32, (grid_rows, grid_cols), 1)
    row = lax.broadcasted_iota(jnp.int32, (grid_rows, grid_cols), 0)
    first_col = col == 0
    last_col = col == grid_cols - 1
    first_row = row == 0
    last_row = row == grid_rows - 1
    west_depth = jnp.where(first_col, west[:, channels : channels + 1], pltpu.roll(depth, 1, 1))
    east_depth = jnp.where(last_col, east[:, channels : channels + 1], pltpu.roll(depth, grid_cols - 1, 1))
    for d in range(channels):
        energy = spec_ref[d] * mask
        west_energy = jnp.where(first_col, west[:, d : d + 1], pltpu.roll(energy, 1, 1))
        east_energy = jnp.where(last_col, east[:, d : d + 1], pltpu.roll(energy, grid_cols - 1, 1))
        east_coef = coef_ref[0, d]
        north_coef = coef_ref[1, d]
        east_mid = east_coef * depth
        north_rate = north_coef * depth
        inflow = (
            jnp.maximum(east_coef * west_depth, 0.0) * west_energy
            + jnp.maximum(-(east_coef * east_depth), 0.0) * east_energy
        )
        south_flux = jnp.maximum(north_rate, 0.0) * energy
        north_flux = jnp.maximum(-north_rate, 0.0) * energy
        from_south = jnp.where(first_row, 0.0, pltpu.roll(south_flux, 1, 0))
        from_north = jnp.where(last_row, 0.0, pltpu.roll(north_flux, grid_rows - 1, 0))
        updated = (
            energy
            - (jnp.abs(east_mid) + jnp.abs(north_rate)) * energy
            + inflow
            + from_south
            + from_north
        )
        spaced_ref[d] = updated * mask
    blocks = out_ref.shape[0]
    sub_rows = out_ref.shape[1] // channels
    turning = turn_ref[...]
    turn_plus = jnp.maximum(turning, 0.0)
    behind = jnp.maximum(-turning, 0.0)
    turn_abs = jnp.abs(turning)
    for d in range(channels):
        here = spaced_ref[d]
        plane_ref[...] = (
            here
            - turn_abs * here
            + turn_plus * spaced_ref[(d - 1) % channels]
            + behind * spaced_ref[(d + 1) % channels]
        )
        for r in range(sub_rows):
            out_ref[:, r * channels + d, :] = plane_ref[pl.ds(r, blocks, stride=sub_rows), :]


def edges_kernel(spec_ref, mask_ref, depth_ref, first_ref, last_ref):
    channels, grid_rows, grid_cols = spec_ref.shape
    edge_mask = mask_ref[...]
    depth = depth_ref[...]
    lane = lax.broadcasted_iota(jnp.int32, (grid_rows, grid_cols), 1)
    first = jnp.where(lane == channels, depth[:, :1], 0.0)
    last = jnp.where(lane == channels, depth[:, grid_cols - 1 :], 0.0)
    for d in range(channels):
        plane = spec_ref[d]
        first = jnp.where(lane == d, plane[:, :1] * edge_mask[:, :1], first)
        last = jnp.where(lane == d, plane[:, grid_cols - 1 :] * edge_mask[:, 1:], last)
    first_ref[...] = first
    last_ref[...] = last


def edges(spectrum, edge_mask, depth):
    vmem = pl.BlockSpec(memory_space=pltpu.VMEM)
    plane = jax.ShapeDtypeStruct(depth.shape, jnp.float32)
    return pl.pallas_call(
        edges_kernel,
        out_shape=(plane, plane),
        in_specs=[vmem] * 3,
        out_specs=(vmem, vmem),
    )(spectrum, edge_mask, depth)


def propagate(spectrum, depth, sea_mask, turning, from_west, from_east, coef, blocks):
    channels, grid_rows, grid_cols = spectrum.shape
    vmem = pl.BlockSpec(memory_space=pltpu.VMEM)
    return pl.pallas_call(
        propagate_kernel,
        out_shape=jax.ShapeDtypeStruct((blocks, grid_rows // blocks * channels, grid_cols), jnp.float32),
        in_specs=[pl.BlockSpec(memory_space=pltpu.SMEM)] + [vmem] * 6,
        out_specs=vmem,
        scratch_shapes=[
            pltpu.VMEM(spectrum.shape, jnp.float32),
            pltpu.VMEM((grid_rows, grid_cols), jnp.float32),
        ],
    )(coef, spectrum, sea_mask, depth, turning, from_west, from_east)


def shards(spectrum, depth_speed, turning, drift, partners, sea_slots, sea_counts):
    channels, grid_rows, grid_cols = spectrum.shape
    n_spec = lax.axis_size("spec")
    sub_rows = grid_rows // n_spec
    per_block = sub_rows * grid_cols
    sea_list = sea_slots[:, 0, :]
    sea_mask = sea_cells(sea_list, sea_counts[:, 0], per_block).reshape(grid_rows, grid_cols)
    edge_mask = edge_cells(sea_list, sea_counts[:, 0], sub_rows, grid_cols)
    edges_first, edges_last = edges(spectrum, edge_mask, depth_speed)
    from_west, from_east = neighbours(edges_first, edges_last)
    local_freq = channels // ND
    freq_ids = (
        lax.axis_index("spec") * local_freq + jnp.arange(local_freq, dtype=jnp.int32)
    ).astype(jnp.float32)
    speeds = jnp.repeat(speed_top * jnp.exp(-decline * freq_ids), ND)
    angles = 2.0 * jnp.pi * jnp.arange(ND, dtype=jnp.float32) / ND
    cosines = jnp.tile(jnp.cos(angles), local_freq)
    sine_part = jnp.tile(jnp.sin(angles), local_freq)
    coef = jnp.stack([speeds * cosines, speeds * sine_part])
    turned = propagate(
        spectrum, depth_speed, sea_mask, turning, from_west, from_east, coef, n_spec
    )
    points = lax.all_to_all(turned, "spec", split_axis=0, concat_axis=0, tiled=True)
    return settle(points, drift, partners)


def solution(mesh):
    return jax.shard_map(
        shards,
        mesh=mesh,
        in_specs=(
            P("spec", None, "tile"),
            P(None, "tile"),
            P(None, "tile"),
            P(),
            P(),
            P(None, "tile", None),
            P(None, "tile"),
        ),
        out_specs=P(None, "spec", "tile"),
        check_vma=False,
    )
```

```python
import jax
import jax.numpy as jnp
from jax import lax
from jax.sharding import PartitionSpec as P
from jax.experimental import pallas as pl
from jax.experimental.pallas import tpu as pltpu

ND = 36
NF = 32
PAD_DIR = 40


speed_top = 0.6
decline = 0.0953102
dia_coeff = 0.25


def extended(cells, sides, width):
    for axis, dim in sides:
        count = lax.axis_size(axis)
        head = lax.slice_in_dim(cells, 0, width, axis=dim)
        tail = lax.slice_in_dim(cells, cells.shape[dim] - width, cells.shape[dim], axis=dim)
        cells = jnp.concatenate(
            [
                lax.ppermute(tail, axis, [(i, (i + 1) % count) for i in range(count)]),
                cells,
                lax.ppermute(head, axis, [((i + 1) % count, i) for i in range(count)]),
            ],
            axis=dim,
        )
    return cells


def edge_cells(sea_list, sea_total, sub_rows, grid_cols):
    slot_rank = jnp.arange(sea_list.shape[1], dtype=jnp.int32)
    is_live = slot_rank[None, :] < sea_total[:, None]
    rows = jnp.arange(sub_rows, dtype=jnp.int32)[:, None] * grid_cols
    cells = rows + jnp.array([0, grid_cols - 1], dtype=jnp.int32)[None, :]
    matches = (sea_list[:, None, None, :] == cells[None, :, :, None]) & is_live[:, None, None, :]
    return jnp.any(matches, axis=3).astype(jnp.float32).reshape(-1, 2)


def sea_cells(sea_list, sea_total, per_block):
    cell_ids = jnp.arange(per_block, dtype=jnp.int32)
    slot_rank = jnp.arange(sea_list.shape[1], dtype=jnp.int32)
    is_live = slot_rank[None, :] < sea_total[:, None]
    matches = (sea_list[:, :, None] == cell_ids[None, None, :]) & is_live[:, :, None]
    return jnp.any(matches, axis=1).astype(jnp.float32)


def advect_space(energy_ext, depth_ext, speeds, cosines, sine_part, sea_mask):
    east_rate = (speeds * cosines)[:, None, None] * depth_ext[None]
    north_rate = (speeds * sine_part)[:, None, None] * depth_ext[None, :, 1:-1]
    centre = energy_ext[:, :, 1:-1]
    east_mid = east_rate[:, :, 1:-1]
    inflow = (
        jnp.maximum(east_rate[:, :, :-2], 0.0) * energy_ext[:, :, :-2]
        + jnp.maximum(-east_rate[:, :, 2:], 0.0) * energy_ext[:, :, 2:]
    )
    empty_row = jnp.zeros_like(centre[:, :1])
    from_south = jnp.concatenate(
        [empty_row, (jnp.maximum(north_rate, 0.0) * centre)[:, :-1]], axis=1
    )
    from_north = jnp.concatenate(
        [(jnp.maximum(-north_rate, 0.0) * centre)[:, 1:], empty_row], axis=1
    )
    updated = (
        centre
        - (jnp.abs(east_mid) + jnp.abs(north_rate)) * centre
        + inflow
        + from_south
        + from_north
    )
    return updated * sea_mask


def advect_direction(energy, turning):
    turn_plus = jnp.maximum(turning, 0.0)
    behind = jnp.maximum(-turning, 0.0)
    return (
        energy
        - jnp.abs(turning) * energy
        + turn_plus * jnp.roll(energy, 1, axis=1)
        + behind * jnp.roll(energy, -1, axis=1)
    )


def advect_frequency(energy, drift, n_freq, n_dir):
    shaped = energy.reshape(n_freq, n_dir, -1)
    drift_rate = drift.reshape(n_freq, n_dir, 1)
    upward = jnp.maximum(drift_rate, 0.0) * shaped
    downward = jnp.maximum(-drift_rate, 0.0) * shaped
    empty_row = jnp.zeros_like(shaped[:1])
    from_below = jnp.concatenate([empty_row, upward[:-1]], axis=0)
    from_above = jnp.concatenate([downward[1:], empty_row], axis=0)
    return (shaped - jnp.abs(drift_rate) * shaped + from_below + from_above).reshape(energy.shape)


def shift_freq(x, s, up):
    if s == 0:
        return x
    n = x.shape[0]
    if up:
        return jnp.concatenate([x[s:], jnp.repeat(x[n - 1 :], s, axis=0)], axis=0)
    return jnp.concatenate([jnp.repeat(x[:1], s, axis=0), x[: n - s]], axis=0)


def pad_freq(x, s, up):
    if s == 0:
        return x
    n = x.shape[0]
    zeros = jnp.zeros_like(x[:s])
    if up:
        return jnp.concatenate([x[s:], zeros], axis=0)
    return jnp.concatenate([zeros, x[: n - s]], axis=0)


def pick_shift(choice, options):
    out = options[-1]
    for i in range(len(options) - 2, -1, -1):
        out = jnp.where(choice == i + 1, options[i], out)
    return out


def turn_rows(x, k):
    d = lax.broadcasted_iota(jnp.int32, x.shape, 0)
    ahead = pltpu.roll(x, PAD_DIR - k, 0)
    wrapped = pltpu.roll(x, ND - k, 0)
    return jnp.where(d + k < ND, ahead, wrapped)


def settle_kernel(
    table_ref, blocks_ref, drift_ref, out_ref, points_ref, shifted_ref, quartet_ref, *source_refs
):
    n_freq = blocks_ref.shape[0]
    sub_rows = blocks_ref.shape[1] // ND
    for r in range(sub_rows):
        start = r * ND // 8 * 8
        offset = r * ND - start

        def align(f, carry):
            block = blocks_ref[f, pl.ds(start, PAD_DIR), :]
            if offset:
                block = pltpu.roll(block, PAD_DIR - offset, 0)
            points_ref[f * sub_rows + r] = block
            return carry

        lax.fori_loop(0, n_freq, align, 0, unroll=True)

    for r in range(sub_rows):
        for f in range(n_freq):
            here = points_ref[f * sub_rows + r]
            rate = drift_ref[:, f : f + 1]
            shifted = here - jnp.abs(rate) * here
            if f > 0:
                below = points_ref[(f - 1) * sub_rows + r]
                shifted = shifted + jnp.maximum(drift_ref[:, f - 1 : f], 0.0) * below
            if f < n_freq - 1:
                above = points_ref[(f + 1) * sub_rows + r]
                shifted = shifted + jnp.maximum(-drift_ref[:, f + 1 : f + 2], 0.0) * above
            shifted_ref[f * sub_rows + r] = shifted
            for source_ref in source_refs:
                source_ref[f * sub_rows + r] = jnp.zeros_like(here)

    def interact(f, carry):
        up_freq = table_ref[0, f]
        down_freq = table_ref[1, f]
        up_turn = table_ref[2, f]
        down_turn = table_ref[3, f]
        for r in range(sub_rows):
            up_ref = source_refs[2 * r]
            down_ref = source_refs[2 * r + 1]
            here = shifted_ref[f * sub_rows + r]
            plus_values = turn_rows(shifted_ref[up_freq * sub_rows + r], up_turn)
            minus_values = turn_rows(shifted_ref[down_freq * sub_rows + r], ND - down_turn)
            quartet = (
                here * here * (plus_values + minus_values)
                - 2.0 * here * plus_values * minus_values
            )
            quartet_ref[f * sub_rows + r] = quartet
            up_at = up_freq * sub_rows + r
            down_at = down_freq * sub_rows + r
            up_ref[up_at] = up_ref[up_at] + turn_rows(quartet, ND - up_turn)
            down_ref[down_at] = down_ref[down_at] + turn_rows(quartet, down_turn)
        return carry

    lax.fori_loop(0, n_freq, interact, 0, unroll=True)

    def finish(f, carry):
        values = []
        for r in range(sub_rows):
            at = f * sub_rows + r
            source = source_refs[2 * r][at] + source_refs[2 * r + 1][at] - 2.0 * quartet_ref[at]
            values.append((shifted_ref[at] + dia_coeff * source)[:ND])
        out_ref[pl.ds(f * ND, ND), :, :] = jnp.stack(values, axis=1)
        return carry

    lax.fori_loop(0, n_freq, finish, 0, unroll=True)


def settle(points, drift, partners):
    _, block_rows, grid_cols = points.shape
    sub_rows = block_rows // ND
    up_ids = partners[0].reshape(NF, ND)[:, 0]
    down_ids = partners[1].reshape(NF, ND)[:, 0]
    table = jnp.stack([up_ids // ND, down_ids // ND, up_ids % ND, ND - down_ids % ND])
    rates = jnp.pad(drift.reshape(NF, ND).T, ((0, PAD_DIR - ND), (0, grid_cols - NF)))
    vmem = pl.BlockSpec(memory_space=pltpu.VMEM)
    block = pltpu.VMEM((NF * sub_rows, PAD_DIR, grid_cols), jnp.float32)
    out = pl.pallas_call(
        settle_kernel,
        out_shape=jax.ShapeDtypeStruct((NF * ND, sub_rows, grid_cols), jnp.float32),
        in_specs=[pl.BlockSpec(memory_space=pltpu.SMEM), vmem, vmem],
        out_specs=vmem,
        scratch_shapes=[block] * (3 + 2 * sub_rows),
    )(table, points, rates)
    return out


def neighbours(edges_first, edges_last):
    count = lax.axis_size("tile")
    from_west = lax.ppermute(edges_last, "tile", [(i, (i + 1) % count) for i in range(count)])
    from_east = lax.ppermute(edges_first, "tile", [((i + 1) % count, i) for i in range(count)])
    return from_west, from_east


def propagate_kernel(
    coef_ref, spec_ref, mask_ref, depth_ref, turn_ref, west_ref, east_ref, out_ref, spaced_ref, plane_ref
):
    channels, grid_rows, grid_cols = spec_ref.shape
    mask = mask_ref[...]
    depth = depth_ref[...]
    west = west_ref[...]
    east = east_ref[...]
    col = lax.broadcasted_iota(jnp.int32, (grid_rows, grid_cols), 1)
    row = lax.broadcasted_iota(jnp.int32, (grid_rows, grid_cols), 0)
    first_col = col == 0
    last_col = col == grid_cols - 1
    first_row = row == 0
    last_row = row == grid_rows - 1
    west_depth = jnp.where(first_col, west[:, channels : channels + 1], pltpu.roll(depth, 1, 1))
    east_depth = jnp.where(last_col, east[:, channels : channels + 1], pltpu.roll(depth, grid_cols - 1, 1))
    for d in range(channels):
        energy = spec_ref[d] * mask
        west_energy = jnp.where(first_col, west[:, d : d + 1], pltpu.roll(energy, 1, 1))
        east_energy = jnp.where(last_col, east[:, d : d + 1], pltpu.roll(energy, grid_cols - 1, 1))
        east_coef = coef_ref[0, d]
        north_coef = coef_ref[1, d]
        east_mid = east_coef * depth
        north_rate = north_coef * depth
        inflow = (
            jnp.maximum(east_coef * west_depth, 0.0) * west_energy
            + jnp.maximum(-(east_coef * east_depth), 0.0) * east_energy
        )
        south_flux = jnp.maximum(north_rate, 0.0) * energy
        north_flux = jnp.maximum(-north_rate, 0.0) * energy
        from_south = jnp.where(first_row, 0.0, pltpu.roll(south_flux, 1, 0))
        from_north = jnp.where(last_row, 0.0, pltpu.roll(north_flux, grid_rows - 1, 0))
        updated = (
            energy
            - (jnp.abs(east_mid) + jnp.abs(north_rate)) * energy
            + inflow
            + from_south
            + from_north
        )
        spaced_ref[d] = updated * mask
    blocks = out_ref.shape[0]
    sub_rows = out_ref.shape[1] // channels
    turning = turn_ref[...]
    turn_plus = jnp.maximum(turning, 0.0)
    behind = jnp.maximum(-turning, 0.0)
    turn_abs = jnp.abs(turning)
    for d in range(channels):
        here = spaced_ref[d]
        plane_ref[...] = (
            here
            - turn_abs * here
            + turn_plus * spaced_ref[(d - 1) % channels]
            + behind * spaced_ref[(d + 1) % channels]
        )
        for r in range(sub_rows):
            out_ref[:, r * channels + d, :] = plane_ref[pl.ds(r, blocks, stride=sub_rows), :]


def edges_kernel(spec_ref, mask_ref, depth_ref, first_ref, last_ref):
    channels, grid_rows, grid_cols = spec_ref.shape
    edge_mask = mask_ref[...]
    depth = depth_ref[...]
    lane = lax.broadcasted_iota(jnp.int32, (grid_rows, grid_cols), 1)
    first = jnp.where(lane == channels, depth[:, :1], 0.0)
    last = jnp.where(lane == channels, depth[:, grid_cols - 1 :], 0.0)
    for d in range(channels):
        plane = spec_ref[d]
        first = jnp.where(lane == d, plane[:, :1] * edge_mask[:, :1], first)
        last = jnp.where(lane == d, plane[:, grid_cols - 1 :] * edge_mask[:, 1:], last)
    first_ref[...] = first
    last_ref[...] = last


def edges(spectrum, edge_mask, depth):
    vmem = pl.BlockSpec(memory_space=pltpu.VMEM)
    plane = jax.ShapeDtypeStruct(depth.shape, jnp.float32)
    return pl.pallas_call(
        edges_kernel,
        out_shape=(plane, plane),
        in_specs=[vmem] * 3,
        out_specs=(vmem, vmem),
    )(spectrum, edge_mask, depth)


def propagate(spectrum, depth, sea_mask, turning, from_west, from_east, coef, blocks):
    channels, grid_rows, grid_cols = spectrum.shape
    vmem = pl.BlockSpec(memory_space=pltpu.VMEM)
    return pl.pallas_call(
        propagate_kernel,
        out_shape=jax.ShapeDtypeStruct((blocks, grid_rows // blocks * channels, grid_cols), jnp.float32),
        in_specs=[pl.BlockSpec(memory_space=pltpu.SMEM)] + [vmem] * 6,
        out_specs=vmem,
        scratch_shapes=[
            pltpu.VMEM(spectrum.shape, jnp.float32),
            pltpu.VMEM((grid_rows, grid_cols), jnp.float32),
        ],
    )(coef, spectrum, sea_mask, depth, turning, from_west, from_east)


def shards(spectrum, depth_speed, turning, drift, partners, sea_slots, sea_counts):
    channels, grid_rows, grid_cols = spectrum.shape
    n_spec = lax.axis_size("spec")
    sub_rows = grid_rows // n_spec
    per_block = sub_rows * grid_cols
    sea_list = sea_slots[:, 0, :]
    sea_mask = sea_cells(sea_list, sea_counts[:, 0], per_block).reshape(grid_rows, grid_cols)
    edge_mask = edge_cells(sea_list, sea_counts[:, 0], sub_rows, grid_cols)
    edges_first, edges_last = edges(spectrum, edge_mask, depth_speed)
    from_west, from_east = neighbours(edges_first, edges_last)
    local_freq = channels // ND
    freq_ids = (
        lax.axis_index("spec") * local_freq + jnp.arange(local_freq, dtype=jnp.int32)
    ).astype(jnp.float32)
    speeds = jnp.repeat(speed_top * jnp.exp(-decline * freq_ids), ND)
    angles = 2.0 * jnp.pi * jnp.arange(ND, dtype=jnp.float32) / ND
    cosines = jnp.tile(jnp.cos(angles), local_freq)
    sine_part = jnp.tile(jnp.sin(angles), local_freq)
    coef = jnp.stack([speeds * cosines, speeds * sine_part])
    turned = propagate(
        spectrum, depth_speed, sea_mask, turning, from_west, from_east, coef, n_spec
    )
    points = lax.all_to_all(turned, "spec", split_axis=0, concat_axis=0, tiled=True)
    return settle(points, drift, partners)


def solution(mesh):
    return jax.shard_map(
        shards,
        mesh=mesh,
        in_specs=(
            P("spec", None, "tile"),
            P(None, "tile"),
            P(None, "tile"),
            P(),
            P(),
            P(None, "tile", None),
            P(None, "tile"),
        ),
        out_specs=P(None, "spec", "tile"),
        check_vma=False,
    )
```

```python
import jax
import jax.numpy as jnp
from jax import lax
from jax.sharding import PartitionSpec as P
from jax.experimental import pallas as pl
from jax.experimental.pallas import tpu as pltpu

ND = 36
NF = 32
PAD_DIR = 40


speed_top = 0.6
decline = 0.0953102
dia_coeff = 0.25


def extended(cells, sides, width):
    for axis, dim in sides:
        count = lax.axis_size(axis)
        head = lax.slice_in_dim(cells, 0, width, axis=dim)
        tail = lax.slice_in_dim(cells, cells.shape[dim] - width, cells.shape[dim], axis=dim)
        cells = jnp.concatenate(
            [
                lax.ppermute(tail, axis, [(i, (i + 1) % count) for i in range(count)]),
                cells,
                lax.ppermute(head, axis, [((i + 1) % count, i) for i in range(count)]),
            ],
            axis=dim,
        )
    return cells


def edge_cells(sea_list, sea_total, sub_rows, grid_cols):
    slot_rank = jnp.arange(sea_list.shape[1], dtype=jnp.int32)
    is_live = slot_rank[None, :] < sea_total[:, None]
    rows = jnp.arange(sub_rows, dtype=jnp.int32)[:, None] * grid_cols
    cells = rows + jnp.array([0, grid_cols - 1], dtype=jnp.int32)[None, :]
    matches = (sea_list[:, None, None, :] == cells[None, :, :, None]) & is_live[:, None, None, :]
    return jnp.any(matches, axis=3).astype(jnp.float32).reshape(-1, 2)


def sea_cells(sea_list, sea_total, per_block):
    cell_ids = jnp.arange(per_block, dtype=jnp.int32)
    slot_rank = jnp.arange(sea_list.shape[1], dtype=jnp.int32)
    is_live = slot_rank[None, :] < sea_total[:, None]
    matches = (sea_list[:, :, None] == cell_ids[None, None, :]) & is_live[:, :, None]
    return jnp.any(matches, axis=1).astype(jnp.float32)


def advect_space(energy_ext, depth_ext, speeds, cosines, sine_part, sea_mask):
    east_rate = (speeds * cosines)[:, None, None] * depth_ext[None]
    north_rate = (speeds * sine_part)[:, None, None] * depth_ext[None, :, 1:-1]
    centre = energy_ext[:, :, 1:-1]
    east_mid = east_rate[:, :, 1:-1]
    inflow = (
        jnp.maximum(east_rate[:, :, :-2], 0.0) * energy_ext[:, :, :-2]
        + jnp.maximum(-east_rate[:, :, 2:], 0.0) * energy_ext[:, :, 2:]
    )
    empty_row = jnp.zeros_like(centre[:, :1])
    from_south = jnp.concatenate(
        [empty_row, (jnp.maximum(north_rate, 0.0) * centre)[:, :-1]], axis=1
    )
    from_north = jnp.concatenate(
        [(jnp.maximum(-north_rate, 0.0) * centre)[:, 1:], empty_row], axis=1
    )
    updated = (
        centre
        - (jnp.abs(east_mid) + jnp.abs(north_rate)) * centre
        + inflow
        + from_south
        + from_north
    )
    return updated * sea_mask


def advect_direction(energy, turning):
    turn_plus = jnp.maximum(turning, 0.0)
    behind = jnp.maximum(-turning, 0.0)
    return (
        energy
        - jnp.abs(turning) * energy
        + turn_plus * jnp.roll(energy, 1, axis=1)
        + behind * jnp.roll(energy, -1, axis=1)
    )


def advect_frequency(energy, drift, n_freq, n_dir):
    shaped = energy.reshape(n_freq, n_dir, -1)
    drift_rate = drift.reshape(n_freq, n_dir, 1)
    upward = jnp.maximum(drift_rate, 0.0) * shaped
    downward = jnp.maximum(-drift_rate, 0.0) * shaped
    empty_row = jnp.zeros_like(shaped[:1])
    from_below = jnp.concatenate([empty_row, upward[:-1]], axis=0)
    from_above = jnp.concatenate([downward[1:], empty_row], axis=0)
    return (shaped - jnp.abs(drift_rate) * shaped + from_below + from_above).reshape(energy.shape)


def shift_freq(x, s, up):
    if s == 0:
        return x
    n = x.shape[0]
    if up:
        return jnp.concatenate([x[s:], jnp.repeat(x[n - 1 :], s, axis=0)], axis=0)
    return jnp.concatenate([jnp.repeat(x[:1], s, axis=0), x[: n - s]], axis=0)


def pad_freq(x, s, up):
    if s == 0:
        return x
    n = x.shape[0]
    zeros = jnp.zeros_like(x[:s])
    if up:
        return jnp.concatenate([x[s:], zeros], axis=0)
    return jnp.concatenate([zeros, x[: n - s]], axis=0)


def pick_shift(choice, options):
    out = options[-1]
    for i in range(len(options) - 2, -1, -1):
        out = jnp.where(choice == i + 1, options[i], out)
    return out


def turn_rows(x, k):
    d = lax.broadcasted_iota(jnp.int32, x.shape, 0)
    ahead = pltpu.roll(x, PAD_DIR - k, 0)
    wrapped = pltpu.roll(x, ND - k, 0)
    return jnp.where(d + k < ND, ahead, wrapped)


def settle_kernel(
    table_ref, blocks_ref, drift_ref, out_ref, points_ref, shifted_ref, quartet_ref, source_ref
):
    n_freq = drift_ref.shape[0]
    sub_rows = blocks_ref.shape[1] // ND
    for r in range(sub_rows):
        start = r * ND // 8 * 8
        offset = r * ND - start

        def align(f, carry):
            block = blocks_ref[f, pl.ds(start, PAD_DIR), :]
            if offset:
                block = pltpu.roll(block, PAD_DIR - offset, 0)
            points_ref[f * sub_rows + r] = block
            return carry

        lax.fori_loop(0, n_freq, align, 0, unroll=True)

    for r in range(sub_rows):

        def advect(f, carry):
            here = points_ref[f * sub_rows + r]
            rate = drift_ref[f]
            below = jnp.maximum(f - 1, 0)
            above = jnp.minimum(f + 1, n_freq - 1)
            from_below = jnp.where(
                f > 0, jnp.maximum(drift_ref[below], 0.0) * points_ref[below * sub_rows + r], 0.0
            )
            from_above = jnp.where(
                f < n_freq - 1,
                jnp.maximum(-drift_ref[above], 0.0) * points_ref[above * sub_rows + r],
                0.0,
            )
            shifted_ref[f] = here - jnp.abs(rate) * here + from_below + from_above
            source_ref[f] = jnp.zeros_like(here)
            return carry

        lax.fori_loop(0, n_freq, advect, 0, unroll=True)

        def interact(f, carry):
            up_freq = table_ref[0, f]
            down_freq = table_ref[1, f]
            up_turn = table_ref[2, f]
            down_turn = table_ref[3, f]
            here = shifted_ref[f]
            plus_values = turn_rows(shifted_ref[up_freq], up_turn)
            minus_values = turn_rows(shifted_ref[down_freq], ND - down_turn)
            quartet = (
                here * here * (plus_values + minus_values)
                - 2.0 * here * plus_values * minus_values
            )
            quartet_ref[f] = quartet
            source_ref[up_freq] = source_ref[up_freq] + turn_rows(quartet, ND - up_turn)
            source_ref[down_freq] = source_ref[down_freq] + turn_rows(quartet, down_turn)
            return carry

        lax.fori_loop(0, n_freq, interact, 0, unroll=True)

        def finish(f, carry):
            source = source_ref[f] - 2.0 * quartet_ref[f]
            value = shifted_ref[f] + dia_coeff * source
            out_ref[pl.ds(f * ND, ND), r, :] = value[:ND]
            return carry

        lax.fori_loop(0, n_freq, finish, 0, unroll=True)


def settle(points, drift, partners):
    _, block_rows, grid_cols = points.shape
    sub_rows = block_rows // ND
    up_ids = partners[0].reshape(NF, ND)[:, 0]
    down_ids = partners[1].reshape(NF, ND)[:, 0]
    table = jnp.stack([up_ids // ND, down_ids // ND, up_ids % ND, ND - down_ids % ND])
    rates = jnp.pad(drift.reshape(NF, ND), ((0, 0), (0, PAD_DIR - ND)))
    rates = jnp.broadcast_to(rates[:, :, None], (NF, PAD_DIR, grid_cols))
    vmem = pl.BlockSpec(memory_space=pltpu.VMEM)
    block = pltpu.VMEM((NF, PAD_DIR, grid_cols), jnp.float32)
    out = pl.pallas_call(
        settle_kernel,
        out_shape=jax.ShapeDtypeStruct((NF * ND, sub_rows, grid_cols), jnp.float32),
        in_specs=[pl.BlockSpec(memory_space=pltpu.SMEM), vmem, vmem],
        out_specs=vmem,
        scratch_shapes=[pltpu.VMEM((NF * sub_rows, PAD_DIR, grid_cols), jnp.float32), block, block, block],
    )(table, points, rates)
    return out


def neighbours(edges_first, edges_last):
    count = lax.axis_size("tile")
    from_west = lax.ppermute(edges_last, "tile", [(i, (i + 1) % count) for i in range(count)])
    from_east = lax.ppermute(edges_first, "tile", [((i + 1) % count, i) for i in range(count)])
    return from_west, from_east


def propagate_kernel(
    coef_ref, spec_ref, mask_ref, depth_ref, turn_ref, west_ref, east_ref, out_ref, spaced_ref, plane_ref
):
    channels, grid_rows, grid_cols = spec_ref.shape
    mask = mask_ref[...]
    depth = depth_ref[...]
    west = west_ref[...]
    east = east_ref[...]
    col = lax.broadcasted_iota(jnp.int32, (grid_rows, grid_cols), 1)
    row = lax.broadcasted_iota(jnp.int32, (grid_rows, grid_cols), 0)
    first_col = col == 0
    last_col = col == grid_cols - 1
    first_row = row == 0
    last_row = row == grid_rows - 1
    west_depth = jnp.where(first_col, west[:, channels : channels + 1], pltpu.roll(depth, 1, 1))
    east_depth = jnp.where(last_col, east[:, channels : channels + 1], pltpu.roll(depth, grid_cols - 1, 1))
    for d in range(channels):
        energy = spec_ref[d] * mask
        west_energy = jnp.where(first_col, west[:, d : d + 1], pltpu.roll(energy, 1, 1))
        east_energy = jnp.where(last_col, east[:, d : d + 1], pltpu.roll(energy, grid_cols - 1, 1))
        east_coef = coef_ref[0, d]
        north_coef = coef_ref[1, d]
        east_mid = east_coef * depth
        north_rate = north_coef * depth
        inflow = (
            jnp.maximum(east_coef * west_depth, 0.0) * west_energy
            + jnp.maximum(-(east_coef * east_depth), 0.0) * east_energy
        )
        south_flux = jnp.maximum(north_rate, 0.0) * energy
        north_flux = jnp.maximum(-north_rate, 0.0) * energy
        from_south = jnp.where(first_row, 0.0, pltpu.roll(south_flux, 1, 0))
        from_north = jnp.where(last_row, 0.0, pltpu.roll(north_flux, grid_rows - 1, 0))
        updated = (
            energy
            - (jnp.abs(east_mid) + jnp.abs(north_rate)) * energy
            + inflow
            + from_south
            + from_north
        )
        spaced_ref[d] = updated * mask
    blocks = out_ref.shape[0]
    sub_rows = out_ref.shape[1] // channels
    turning = turn_ref[...]
    turn_plus = jnp.maximum(turning, 0.0)
    behind = jnp.maximum(-turning, 0.0)
    turn_abs = jnp.abs(turning)
    for d in range(channels):
        here = spaced_ref[d]
        plane_ref[...] = (
            here
            - turn_abs * here
            + turn_plus * spaced_ref[(d - 1) % channels]
            + behind * spaced_ref[(d + 1) % channels]
        )
        for r in range(sub_rows):
            out_ref[:, r * channels + d, :] = plane_ref[pl.ds(r, blocks, stride=sub_rows), :]


def edges_kernel(spec_ref, mask_ref, depth_ref, first_ref, last_ref):
    channels, grid_rows, grid_cols = spec_ref.shape
    edge_mask = mask_ref[...]
    depth = depth_ref[...]
    lane = lax.broadcasted_iota(jnp.int32, (grid_rows, grid_cols), 1)
    first = jnp.where(lane == channels, depth[:, :1], 0.0)
    last = jnp.where(lane == channels, depth[:, grid_cols - 1 :], 0.0)
    for d in range(channels):
        plane = spec_ref[d]
        first = jnp.where(lane == d, plane[:, :1] * edge_mask[:, :1], first)
        last = jnp.where(lane == d, plane[:, grid_cols - 1 :] * edge_mask[:, 1:], last)
    first_ref[...] = first
    last_ref[...] = last


def edges(spectrum, edge_mask, depth):
    vmem = pl.BlockSpec(memory_space=pltpu.VMEM)
    plane = jax.ShapeDtypeStruct(depth.shape, jnp.float32)
    return pl.pallas_call(
        edges_kernel,
        out_shape=(plane, plane),
        in_specs=[vmem] * 3,
        out_specs=(vmem, vmem),
    )(spectrum, edge_mask, depth)


def propagate(spectrum, depth, sea_mask, turning, from_west, from_east, coef, blocks):
    channels, grid_rows, grid_cols = spectrum.shape
    vmem = pl.BlockSpec(memory_space=pltpu.VMEM)
    return pl.pallas_call(
        propagate_kernel,
        out_shape=jax.ShapeDtypeStruct((blocks, grid_rows // blocks * channels, grid_cols), jnp.float32),
        in_specs=[pl.BlockSpec(memory_space=pltpu.SMEM)] + [vmem] * 6,
        out_specs=vmem,
        scratch_shapes=[
            pltpu.VMEM(spectrum.shape, jnp.float32),
            pltpu.VMEM((grid_rows, grid_cols), jnp.float32),
        ],
    )(coef, spectrum, sea_mask, depth, turning, from_west, from_east)


def shards(spectrum, depth_speed, turning, drift, partners, sea_slots, sea_counts):
    channels, grid_rows, grid_cols = spectrum.shape
    n_spec = lax.axis_size("spec")
    sub_rows = grid_rows // n_spec
    per_block = sub_rows * grid_cols
    sea_list = sea_slots[:, 0, :]
    edge_mask = edge_cells(sea_list, sea_counts[:, 0], sub_rows, grid_cols)
    edges_first, edges_last = edges(spectrum, edge_mask, depth_speed)
    from_west, from_east = neighbours(edges_first, edges_last)
    from_west, from_east, sea_list = lax.optimization_barrier((from_west, from_east, sea_list))
    sea_mask = sea_cells(sea_list, sea_counts[:, 0], per_block).reshape(grid_rows, grid_cols)
    local_freq = channels // ND
    freq_ids = (
        lax.axis_index("spec") * local_freq + jnp.arange(local_freq, dtype=jnp.int32)
    ).astype(jnp.float32)
    speeds = jnp.repeat(speed_top * jnp.exp(-decline * freq_ids), ND)
    angles = 2.0 * jnp.pi * jnp.arange(ND, dtype=jnp.float32) / ND
    cosines = jnp.tile(jnp.cos(angles), local_freq)
    sine_part = jnp.tile(jnp.sin(angles), local_freq)
    coef = jnp.stack([speeds * cosines, speeds * sine_part])
    turned = propagate(
        spectrum, depth_speed, sea_mask, turning, from_west, from_east, coef, n_spec
    )
    points = lax.all_to_all(turned, "spec", split_axis=0, concat_axis=0, tiled=True)
    return settle(points, drift, partners)


def solution(mesh):
    return jax.shard_map(
        shards,
        mesh=mesh,
        in_specs=(
            P("spec", None, "tile"),
            P(None, "tile"),
            P(None, "tile"),
            P(),
            P(),
            P(None, "tile", None),
            P(None, "tile"),
        ),
        out_specs=P(None, "spec", "tile"),
        check_vma=False,
    )
```

```python
import jax
import jax.numpy as jnp
from jax import lax
from jax.sharding import PartitionSpec as P
from jax.experimental import pallas as pl
from jax.experimental.pallas import tpu as pltpu

ND = 36
NF = 32
PAD_DIR = 40


speed_top = 0.6
decline = 0.0953102
dia_coeff = 0.25


def extended(cells, sides, width):
    for axis, dim in sides:
        count = lax.axis_size(axis)
        head = lax.slice_in_dim(cells, 0, width, axis=dim)
        tail = lax.slice_in_dim(cells, cells.shape[dim] - width, cells.shape[dim], axis=dim)
        cells = jnp.concatenate(
            [
                lax.ppermute(tail, axis, [(i, (i + 1) % count) for i in range(count)]),
                cells,
                lax.ppermute(head, axis, [((i + 1) % count, i) for i in range(count)]),
            ],
            axis=dim,
        )
    return cells


def edge_cells(sea_list, sea_total, sub_rows, grid_cols):
    slot_rank = jnp.arange(sea_list.shape[1], dtype=jnp.int32)
    is_live = slot_rank[None, :] < sea_total[:, None]
    rows = jnp.arange(sub_rows, dtype=jnp.int32)[:, None] * grid_cols
    cells = rows + jnp.array([0, grid_cols - 1], dtype=jnp.int32)[None, :]
    matches = (sea_list[:, None, None, :] == cells[None, :, :, None]) & is_live[:, None, None, :]
    return jnp.any(matches, axis=3).astype(jnp.float32).reshape(-1, 2)


def sea_rows(sea_list, sea_total, sub_rows, grid_cols):
    slot_rank = jnp.arange(sea_list.shape[1], dtype=jnp.int32)
    live = jnp.where(slot_rank[None, :] < sea_total[:, None], sea_list, -1)
    live = jnp.repeat(live, sub_rows, axis=0)
    row_start = (jnp.arange(live.shape[0], dtype=jnp.int32) % sub_rows) * grid_cols
    cols = jnp.arange(grid_cols, dtype=jnp.int32)
    matches = (live - row_start[:, None])[:, :, None] == cols[None, None, :]
    return jnp.any(matches & (live >= 0)[:, :, None], axis=1).astype(jnp.float32)


def sea_cells(sea_list, sea_total, per_block):
    cell_ids = jnp.arange(per_block, dtype=jnp.int32)
    slot_rank = jnp.arange(sea_list.shape[1], dtype=jnp.int32)
    is_live = slot_rank[None, :] < sea_total[:, None]
    matches = (sea_list[:, :, None] == cell_ids[None, None, :]) & is_live[:, :, None]
    return jnp.any(matches, axis=1).astype(jnp.float32)


def advect_space(energy_ext, depth_ext, speeds, cosines, sine_part, sea_mask):
    east_rate = (speeds * cosines)[:, None, None] * depth_ext[None]
    north_rate = (speeds * sine_part)[:, None, None] * depth_ext[None, :, 1:-1]
    centre = energy_ext[:, :, 1:-1]
    east_mid = east_rate[:, :, 1:-1]
    inflow = (
        jnp.maximum(east_rate[:, :, :-2], 0.0) * energy_ext[:, :, :-2]
        + jnp.maximum(-east_rate[:, :, 2:], 0.0) * energy_ext[:, :, 2:]
    )
    empty_row = jnp.zeros_like(centre[:, :1])
    from_south = jnp.concatenate(
        [empty_row, (jnp.maximum(north_rate, 0.0) * centre)[:, :-1]], axis=1
    )
    from_north = jnp.concatenate(
        [(jnp.maximum(-north_rate, 0.0) * centre)[:, 1:], empty_row], axis=1
    )
    updated = (
        centre
        - (jnp.abs(east_mid) + jnp.abs(north_rate)) * centre
        + inflow
        + from_south
        + from_north
    )
    return updated * sea_mask


def advect_direction(energy, turning):
    turn_plus = jnp.maximum(turning, 0.0)
    behind = jnp.maximum(-turning, 0.0)
    return (
        energy
        - jnp.abs(turning) * energy
        + turn_plus * jnp.roll(energy, 1, axis=1)
        + behind * jnp.roll(energy, -1, axis=1)
    )


def advect_frequency(energy, drift, n_freq, n_dir):
    shaped = energy.reshape(n_freq, n_dir, -1)
    drift_rate = drift.reshape(n_freq, n_dir, 1)
    upward = jnp.maximum(drift_rate, 0.0) * shaped
    downward = jnp.maximum(-drift_rate, 0.0) * shaped
    empty_row = jnp.zeros_like(shaped[:1])
    from_below = jnp.concatenate([empty_row, upward[:-1]], axis=0)
    from_above = jnp.concatenate([downward[1:], empty_row], axis=0)
    return (shaped - jnp.abs(drift_rate) * shaped + from_below + from_above).reshape(energy.shape)


def shift_freq(x, s, up):
    if s == 0:
        return x
    n = x.shape[0]
    if up:
        return jnp.concatenate([x[s:], jnp.repeat(x[n - 1 :], s, axis=0)], axis=0)
    return jnp.concatenate([jnp.repeat(x[:1], s, axis=0), x[: n - s]], axis=0)


def pad_freq(x, s, up):
    if s == 0:
        return x
    n = x.shape[0]
    zeros = jnp.zeros_like(x[:s])
    if up:
        return jnp.concatenate([x[s:], zeros], axis=0)
    return jnp.concatenate([zeros, x[: n - s]], axis=0)


def pick_shift(choice, options):
    out = options[-1]
    for i in range(len(options) - 2, -1, -1):
        out = jnp.where(choice == i + 1, options[i], out)
    return out


def turn_rows(x, k):
    d = lax.broadcasted_iota(jnp.int32, x.shape, 0)
    ahead = pltpu.roll(x, PAD_DIR - k, 0)
    wrapped = pltpu.roll(x, ND - k, 0)
    return jnp.where(d + k < ND, ahead, wrapped)


def settle_kernel(
    table_ref, blocks_ref, drift_ref, out_ref, points_ref, shifted_ref, quartet_ref, source_ref
):
    n_freq = drift_ref.shape[0]
    sub_rows = blocks_ref.shape[1] // ND
    for r in range(sub_rows):
        start = r * ND // 8 * 8
        offset = r * ND - start

        def align(f, carry):
            block = blocks_ref[f, pl.ds(start, PAD_DIR), :]
            if offset:
                block = pltpu.roll(block, PAD_DIR - offset, 0)
            points_ref[f * sub_rows + r] = block
            return carry

        lax.fori_loop(0, n_freq, align, 0, unroll=True)

    for r in range(sub_rows):

        def advect(f, carry):
            here = points_ref[f * sub_rows + r]
            rate = drift_ref[f]
            below = jnp.maximum(f - 1, 0)
            above = jnp.minimum(f + 1, n_freq - 1)
            from_below = jnp.where(
                f > 0, jnp.maximum(drift_ref[below], 0.0) * points_ref[below * sub_rows + r], 0.0
            )
            from_above = jnp.where(
                f < n_freq - 1,
                jnp.maximum(-drift_ref[above], 0.0) * points_ref[above * sub_rows + r],
                0.0,
            )
            shifted_ref[f] = here - jnp.abs(rate) * here + from_below + from_above
            source_ref[f] = jnp.zeros_like(here)
            return carry

        lax.fori_loop(0, n_freq, advect, 0, unroll=True)

        def interact(f, carry):
            up_freq = table_ref[0, f]
            down_freq = table_ref[1, f]
            up_turn = table_ref[2, f]
            down_turn = table_ref[3, f]
            here = shifted_ref[f]
            plus_values = turn_rows(shifted_ref[up_freq], up_turn)
            minus_values = turn_rows(shifted_ref[down_freq], ND - down_turn)
            quartet = (
                here * here * (plus_values + minus_values)
                - 2.0 * here * plus_values * minus_values
            )
            quartet_ref[f] = quartet
            source_ref[up_freq] = source_ref[up_freq] + turn_rows(quartet, ND - up_turn)
            source_ref[down_freq] = source_ref[down_freq] + turn_rows(quartet, down_turn)
            return carry

        lax.fori_loop(0, n_freq, interact, 0, unroll=True)

        def finish(f, carry):
            source = source_ref[f] - 2.0 * quartet_ref[f]
            value = shifted_ref[f] + dia_coeff * source
            out_ref[pl.ds(f * ND, ND), r, :] = value[:ND]
            return carry

        lax.fori_loop(0, n_freq, finish, 0, unroll=True)


def settle(points, drift, partners):
    _, block_rows, grid_cols = points.shape
    sub_rows = block_rows // ND
    up_ids = partners[0].reshape(NF, ND)[:, 0]
    down_ids = partners[1].reshape(NF, ND)[:, 0]
    table = jnp.stack([up_ids // ND, down_ids // ND, up_ids % ND, ND - down_ids % ND])
    rates = jnp.pad(drift.reshape(NF, ND), ((0, 0), (0, PAD_DIR - ND)))
    rates = jnp.broadcast_to(rates[:, :, None], (NF, PAD_DIR, grid_cols))
    vmem = pl.BlockSpec(memory_space=pltpu.VMEM)
    block = pltpu.VMEM((NF, PAD_DIR, grid_cols), jnp.float32)
    out = pl.pallas_call(
        settle_kernel,
        out_shape=jax.ShapeDtypeStruct((NF * ND, sub_rows, grid_cols), jnp.float32),
        in_specs=[pl.BlockSpec(memory_space=pltpu.SMEM), vmem, vmem],
        out_specs=vmem,
        scratch_shapes=[pltpu.VMEM((NF * sub_rows, PAD_DIR, grid_cols), jnp.float32), block, block, block],
    )(table, points, rates)
    return out


def neighbours(edges_first, edges_last):
    count = lax.axis_size("tile")
    from_west = lax.ppermute(edges_last, "tile", [(i, (i + 1) % count) for i in range(count)])
    from_east = lax.ppermute(edges_first, "tile", [((i + 1) % count, i) for i in range(count)])
    return from_west, from_east


def propagate_kernel(
    coef_ref, spec_ref, mask_ref, depth_ref, turn_ref, west_ref, east_ref, out_ref, spaced_ref, plane_ref
):
    channels, grid_rows, grid_cols = spec_ref.shape
    mask = mask_ref[...]
    depth = depth_ref[...]
    west = west_ref[...]
    east = east_ref[...]
    col = lax.broadcasted_iota(jnp.int32, (grid_rows, grid_cols), 1)
    row = lax.broadcasted_iota(jnp.int32, (grid_rows, grid_cols), 0)
    first_col = col == 0
    last_col = col == grid_cols - 1
    first_row = row == 0
    last_row = row == grid_rows - 1
    west_depth = jnp.where(first_col, west[:, channels : channels + 1], pltpu.roll(depth, 1, 1))
    east_depth = jnp.where(last_col, east[:, channels : channels + 1], pltpu.roll(depth, grid_cols - 1, 1))
    for d in range(channels):
        energy = spec_ref[d] * mask
        west_energy = jnp.where(first_col, west[:, d : d + 1], pltpu.roll(energy, 1, 1))
        east_energy = jnp.where(last_col, east[:, d : d + 1], pltpu.roll(energy, grid_cols - 1, 1))
        east_coef = coef_ref[0, d]
        north_coef = coef_ref[1, d]
        east_mid = east_coef * depth
        north_rate = north_coef * depth
        inflow = (
            jnp.maximum(east_coef * west_depth, 0.0) * west_energy
            + jnp.maximum(-(east_coef * east_depth), 0.0) * east_energy
        )
        south_flux = jnp.maximum(north_rate, 0.0) * energy
        north_flux = jnp.maximum(-north_rate, 0.0) * energy
        from_south = jnp.where(first_row, 0.0, pltpu.roll(south_flux, 1, 0))
        from_north = jnp.where(last_row, 0.0, pltpu.roll(north_flux, grid_rows - 1, 0))
        updated = (
            energy
            - (jnp.abs(east_mid) + jnp.abs(north_rate)) * energy
            + inflow
            + from_south
            + from_north
        )
        spaced_ref[d] = updated * mask
    blocks = out_ref.shape[0]
    sub_rows = out_ref.shape[1] // channels
    turning = turn_ref[...]
    turn_plus = jnp.maximum(turning, 0.0)
    behind = jnp.maximum(-turning, 0.0)
    turn_abs = jnp.abs(turning)
    for d in range(channels):
        here = spaced_ref[d]
        plane_ref[...] = (
            here
            - turn_abs * here
            + turn_plus * spaced_ref[(d - 1) % channels]
            + behind * spaced_ref[(d + 1) % channels]
        )
        for r in range(sub_rows):
            out_ref[:, r * channels + d, :] = plane_ref[pl.ds(r, blocks, stride=sub_rows), :]


def edges_kernel(spec_ref, mask_ref, depth_ref, first_ref, last_ref):
    channels, grid_rows, grid_cols = spec_ref.shape
    edge_mask = mask_ref[...]
    depth = depth_ref[...]
    lane = lax.broadcasted_iota(jnp.int32, (grid_rows, grid_cols), 1)
    first = jnp.where(lane == channels, depth[:, :1], 0.0)
    last = jnp.where(lane == channels, depth[:, grid_cols - 1 :], 0.0)
    for d in range(channels):
        plane = spec_ref[d]
        first = jnp.where(lane == d, plane[:, :1] * edge_mask[:, :1], first)
        last = jnp.where(lane == d, plane[:, grid_cols - 1 :] * edge_mask[:, 1:], last)
    first_ref[...] = first
    last_ref[...] = last


def edges(spectrum, edge_mask, depth):
    vmem = pl.BlockSpec(memory_space=pltpu.VMEM)
    plane = jax.ShapeDtypeStruct(depth.shape, jnp.float32)
    return pl.pallas_call(
        edges_kernel,
        out_shape=(plane, plane),
        in_specs=[vmem] * 3,
        out_specs=(vmem, vmem),
    )(spectrum, edge_mask, depth)


def propagate(spectrum, depth, sea_mask, turning, from_west, from_east, coef, blocks):
    channels, grid_rows, grid_cols = spectrum.shape
    vmem = pl.BlockSpec(memory_space=pltpu.VMEM)
    return pl.pallas_call(
        propagate_kernel,
        out_shape=jax.ShapeDtypeStruct((blocks, grid_rows // blocks * channels, grid_cols), jnp.float32),
        in_specs=[pl.BlockSpec(memory_space=pltpu.SMEM)] + [vmem] * 6,
        out_specs=vmem,
        scratch_shapes=[
            pltpu.VMEM(spectrum.shape, jnp.float32),
            pltpu.VMEM((grid_rows, grid_cols), jnp.float32),
        ],
    )(coef, spectrum, sea_mask, depth, turning, from_west, from_east)


def shards(spectrum, depth_speed, turning, drift, partners, sea_slots, sea_counts):
    channels, grid_rows, grid_cols = spectrum.shape
    n_spec = lax.axis_size("spec")
    sub_rows = grid_rows // n_spec
    per_block = sub_rows * grid_cols
    sea_list = sea_slots[:, 0, :]
    sea_mask = sea_rows(sea_list, sea_counts[:, 0], sub_rows, grid_cols)
    edge_mask = edge_cells(sea_list, sea_counts[:, 0], sub_rows, grid_cols)
    edges_first, edges_last = edges(spectrum, edge_mask, depth_speed)
    from_west, from_east = neighbours(edges_first, edges_last)
    local_freq = channels // ND
    freq_ids = (
        lax.axis_index("spec") * local_freq + jnp.arange(local_freq, dtype=jnp.int32)
    ).astype(jnp.float32)
    speeds = jnp.repeat(speed_top * jnp.exp(-decline * freq_ids), ND)
    angles = 2.0 * jnp.pi * jnp.arange(ND, dtype=jnp.float32) / ND
    cosines = jnp.tile(jnp.cos(angles), local_freq)
    sine_part = jnp.tile(jnp.sin(angles), local_freq)
    coef = jnp.stack([speeds * cosines, speeds * sine_part])
    turned = propagate(
        spectrum, depth_speed, sea_mask, turning, from_west, from_east, coef, n_spec
    )
    points = lax.all_to_all(turned, "spec", split_axis=0, concat_axis=0, tiled=True)
    return settle(points, drift, partners)


def solution(mesh):
    return jax.shard_map(
        shards,
        mesh=mesh,
        in_specs=(
            P("spec", None, "tile"),
            P(None, "tile"),
            P(None, "tile"),
            P(),
            P(),
            P(None, "tile", None),
            P(None, "tile"),
        ),
        out_specs=P(None, "spec", "tile"),
        check_vma=False,
    )
```

```python
import jax
import jax.numpy as jnp
from jax import lax
from jax.sharding import PartitionSpec as P
from jax.experimental import pallas as pl
from jax.experimental.pallas import tpu as pltpu

ND = 36
NF = 32
PAD_DIR = 40


speed_top = 0.6
decline = 0.0953102
dia_coeff = 0.25


def extended(cells, sides, width):
    for axis, dim in sides:
        count = lax.axis_size(axis)
        head = lax.slice_in_dim(cells, 0, width, axis=dim)
        tail = lax.slice_in_dim(cells, cells.shape[dim] - width, cells.shape[dim], axis=dim)
        cells = jnp.concatenate(
            [
                lax.ppermute(tail, axis, [(i, (i + 1) % count) for i in range(count)]),
                cells,
                lax.ppermute(head, axis, [((i + 1) % count, i) for i in range(count)]),
            ],
            axis=dim,
        )
    return cells


def edge_cells(sea_list, sea_total, sub_rows, grid_cols):
    slot_rank = jnp.arange(sea_list.shape[1], dtype=jnp.int32)
    is_live = slot_rank[None, :] < sea_total[:, None]
    rows = jnp.arange(sub_rows, dtype=jnp.int32)[:, None] * grid_cols
    cells = rows + jnp.array([0, grid_cols - 1], dtype=jnp.int32)[None, :]
    matches = (sea_list[:, None, None, :] == cells[None, :, :, None]) & is_live[:, None, None, :]
    return jnp.any(matches, axis=3).astype(jnp.float32).reshape(-1, 2)


def sea_cells(sea_list, sea_total, per_block):
    cell_ids = jnp.arange(per_block, dtype=jnp.int32)
    slot_rank = jnp.arange(sea_list.shape[1], dtype=jnp.int32)
    is_live = slot_rank[None, :] < sea_total[:, None]
    matches = (sea_list[:, :, None] == cell_ids[None, None, :]) & is_live[:, :, None]
    return jnp.any(matches, axis=1).astype(jnp.float32)


def advect_space(energy_ext, depth_ext, speeds, cosines, sine_part, sea_mask):
    east_rate = (speeds * cosines)[:, None, None] * depth_ext[None]
    north_rate = (speeds * sine_part)[:, None, None] * depth_ext[None, :, 1:-1]
    centre = energy_ext[:, :, 1:-1]
    east_mid = east_rate[:, :, 1:-1]
    inflow = (
        jnp.maximum(east_rate[:, :, :-2], 0.0) * energy_ext[:, :, :-2]
        + jnp.maximum(-east_rate[:, :, 2:], 0.0) * energy_ext[:, :, 2:]
    )
    empty_row = jnp.zeros_like(centre[:, :1])
    from_south = jnp.concatenate(
        [empty_row, (jnp.maximum(north_rate, 0.0) * centre)[:, :-1]], axis=1
    )
    from_north = jnp.concatenate(
        [(jnp.maximum(-north_rate, 0.0) * centre)[:, 1:], empty_row], axis=1
    )
    updated = (
        centre
        - (jnp.abs(east_mid) + jnp.abs(north_rate)) * centre
        + inflow
        + from_south
        + from_north
    )
    return updated * sea_mask


def advect_direction(energy, turning):
    turn_plus = jnp.maximum(turning, 0.0)
    behind = jnp.maximum(-turning, 0.0)
    return (
        energy
        - jnp.abs(turning) * energy
        + turn_plus * jnp.roll(energy, 1, axis=1)
        + behind * jnp.roll(energy, -1, axis=1)
    )


def advect_frequency(energy, drift, n_freq, n_dir):
    shaped = energy.reshape(n_freq, n_dir, -1)
    drift_rate = drift.reshape(n_freq, n_dir, 1)
    upward = jnp.maximum(drift_rate, 0.0) * shaped
    downward = jnp.maximum(-drift_rate, 0.0) * shaped
    empty_row = jnp.zeros_like(shaped[:1])
    from_below = jnp.concatenate([empty_row, upward[:-1]], axis=0)
    from_above = jnp.concatenate([downward[1:], empty_row], axis=0)
    return (shaped - jnp.abs(drift_rate) * shaped + from_below + from_above).reshape(energy.shape)


def shift_freq(x, s, up):
    if s == 0:
        return x
    n = x.shape[0]
    if up:
        return jnp.concatenate([x[s:], jnp.repeat(x[n - 1 :], s, axis=0)], axis=0)
    return jnp.concatenate([jnp.repeat(x[:1], s, axis=0), x[: n - s]], axis=0)


def pad_freq(x, s, up):
    if s == 0:
        return x
    n = x.shape[0]
    zeros = jnp.zeros_like(x[:s])
    if up:
        return jnp.concatenate([x[s:], zeros], axis=0)
    return jnp.concatenate([zeros, x[: n - s]], axis=0)


def pick_shift(choice, options):
    out = options[-1]
    for i in range(len(options) - 2, -1, -1):
        out = jnp.where(choice == i + 1, options[i], out)
    return out


def turn_rows(x, k, rows):
    ahead = pltpu.roll(x, PAD_DIR - k, 0)
    wrapped = pltpu.roll(x, ND - k, 0)
    return jnp.where(rows < ND - k, ahead, wrapped)


def settle_kernel(
    table_ref, blocks_ref, drift_ref, out_ref, points_ref, shifted_ref, quartet_ref, source_ref
):
    n_freq = drift_ref.shape[0]
    sub_rows = blocks_ref.shape[1] // ND
    rows = lax.broadcasted_iota(jnp.int32, (PAD_DIR, blocks_ref.shape[2]), 0)
    for r in range(sub_rows):
        start = r * ND // 8 * 8
        offset = r * ND - start

        def align(f, carry):
            block = blocks_ref[f, pl.ds(start, PAD_DIR), :]
            if offset:
                block = pltpu.roll(block, PAD_DIR - offset, 0)
            points_ref[f * sub_rows + r] = block
            return carry

        lax.fori_loop(0, n_freq, align, 0, unroll=True)

    for r in range(sub_rows):

        def advect(f, carry):
            here = points_ref[f * sub_rows + r]
            rate = drift_ref[f]
            below = jnp.maximum(f - 1, 0)
            above = jnp.minimum(f + 1, n_freq - 1)
            from_below = jnp.where(
                f > 0, jnp.maximum(drift_ref[below], 0.0) * points_ref[below * sub_rows + r], 0.0
            )
            from_above = jnp.where(
                f < n_freq - 1,
                jnp.maximum(-drift_ref[above], 0.0) * points_ref[above * sub_rows + r],
                0.0,
            )
            shifted_ref[f] = here - jnp.abs(rate) * here + from_below + from_above
            source_ref[f] = jnp.zeros_like(here)
            return carry

        lax.fori_loop(0, n_freq, advect, 0, unroll=True)

        def interact(f, carry):
            up_freq = table_ref[0, f]
            down_freq = table_ref[1, f]
            up_turn = table_ref[2, f]
            down_turn = table_ref[3, f]
            here = shifted_ref[f]
            plus_values = turn_rows(shifted_ref[up_freq], up_turn, rows)
            minus_values = turn_rows(shifted_ref[down_freq], ND - down_turn, rows)
            quartet = (
                here * here * (plus_values + minus_values)
                - 2.0 * here * plus_values * minus_values
            )
            quartet_ref[f] = quartet
            source_ref[up_freq] = source_ref[up_freq] + turn_rows(quartet, ND - up_turn, rows)
            source_ref[down_freq] = source_ref[down_freq] + turn_rows(quartet, down_turn, rows)
            return carry

        lax.fori_loop(0, n_freq, interact, 0, unroll=True)

        def finish(f, carry):
            source = source_ref[f] - 2.0 * quartet_ref[f]
            value = shifted_ref[f] + dia_coeff * source
            out_ref[pl.ds(f * ND, ND), r, :] = value[:ND]
            return carry

        lax.fori_loop(0, n_freq, finish, 0, unroll=True)


def settle(points, drift, partners):
    _, block_rows, grid_cols = points.shape
    sub_rows = block_rows // ND
    up_ids = partners[0].reshape(NF, ND)[:, 0]
    down_ids = partners[1].reshape(NF, ND)[:, 0]
    table = jnp.stack([up_ids // ND, down_ids // ND, up_ids % ND, ND - down_ids % ND])
    rates = jnp.pad(drift.reshape(NF, ND), ((0, 0), (0, PAD_DIR - ND)))
    rates = jnp.broadcast_to(rates[:, :, None], (NF, PAD_DIR, grid_cols))
    vmem = pl.BlockSpec(memory_space=pltpu.VMEM)
    block = pltpu.VMEM((NF, PAD_DIR, grid_cols), jnp.float32)
    out = pl.pallas_call(
        settle_kernel,
        out_shape=jax.ShapeDtypeStruct((NF * ND, sub_rows, grid_cols), jnp.float32),
        in_specs=[pl.BlockSpec(memory_space=pltpu.SMEM), vmem, vmem],
        out_specs=vmem,
        scratch_shapes=[pltpu.VMEM((NF * sub_rows, PAD_DIR, grid_cols), jnp.float32), block, block, block],
    )(table, points, rates)
    return out


def neighbours(edges_first, edges_last):
    count = lax.axis_size("tile")
    from_west = lax.ppermute(edges_last, "tile", [(i, (i + 1) % count) for i in range(count)])
    from_east = lax.ppermute(edges_first, "tile", [((i + 1) % count, i) for i in range(count)])
    return from_west, from_east


def propagate_kernel(
    coef_ref, spec_ref, mask_ref, depth_ref, turn_ref, west_ref, east_ref, out_ref, spaced_ref, plane_ref
):
    channels, grid_rows, grid_cols = spec_ref.shape
    mask = mask_ref[...]
    depth = depth_ref[...]
    west = west_ref[...]
    east = east_ref[...]
    col = lax.broadcasted_iota(jnp.int32, (grid_rows, grid_cols), 1)
    row = lax.broadcasted_iota(jnp.int32, (grid_rows, grid_cols), 0)
    first_col = col == 0
    last_col = col == grid_cols - 1
    first_row = row == 0
    last_row = row == grid_rows - 1
    west_depth = jnp.where(first_col, west[:, channels : channels + 1], pltpu.roll(depth, 1, 1))
    east_depth = jnp.where(last_col, east[:, channels : channels + 1], pltpu.roll(depth, grid_cols - 1, 1))
    for d in range(channels):
        energy = spec_ref[d] * mask
        west_energy = jnp.where(first_col, west[:, d : d + 1], pltpu.roll(energy, 1, 1))
        east_energy = jnp.where(last_col, east[:, d : d + 1], pltpu.roll(energy, grid_cols - 1, 1))
        east_coef = coef_ref[0, d]
        north_coef = coef_ref[1, d]
        east_mid = east_coef * depth
        north_rate = north_coef * depth
        inflow = (
            jnp.maximum(east_coef * west_depth, 0.0) * west_energy
            + jnp.maximum(-(east_coef * east_depth), 0.0) * east_energy
        )
        south_flux = jnp.maximum(north_rate, 0.0) * energy
        north_flux = jnp.maximum(-north_rate, 0.0) * energy
        from_south = jnp.where(first_row, 0.0, pltpu.roll(south_flux, 1, 0))
        from_north = jnp.where(last_row, 0.0, pltpu.roll(north_flux, grid_rows - 1, 0))
        updated = (
            energy
            - (jnp.abs(east_mid) + jnp.abs(north_rate)) * energy
            + inflow
            + from_south
            + from_north
        )
        spaced_ref[d] = updated * mask
    blocks = out_ref.shape[0]
    sub_rows = out_ref.shape[1] // channels
    turning = turn_ref[...]
    turn_plus = jnp.maximum(turning, 0.0)
    behind = jnp.maximum(-turning, 0.0)
    turn_abs = jnp.abs(turning)
    for d in range(channels):
        here = spaced_ref[d]
        plane_ref[...] = (
            here
            - turn_abs * here
            + turn_plus * spaced_ref[(d - 1) % channels]
            + behind * spaced_ref[(d + 1) % channels]
        )
        for r in range(sub_rows):
            out_ref[:, r * channels + d, :] = plane_ref[pl.ds(r, blocks, stride=sub_rows), :]


def edges_kernel(spec_ref, mask_ref, depth_ref, first_ref, last_ref):
    channels, grid_rows, grid_cols = spec_ref.shape
    edge_mask = mask_ref[...]
    depth = depth_ref[...]
    lane = lax.broadcasted_iota(jnp.int32, (grid_rows, grid_cols), 1)
    first = jnp.where(lane == channels, depth[:, :1], 0.0)
    last = jnp.where(lane == channels, depth[:, grid_cols - 1 :], 0.0)
    for d in range(channels):
        plane = spec_ref[d]
        first = jnp.where(lane == d, plane[:, :1] * edge_mask[:, :1], first)
        last = jnp.where(lane == d, plane[:, grid_cols - 1 :] * edge_mask[:, 1:], last)
    first_ref[...] = first
    last_ref[...] = last


def edges(spectrum, edge_mask, depth):
    vmem = pl.BlockSpec(memory_space=pltpu.VMEM)
    plane = jax.ShapeDtypeStruct(depth.shape, jnp.float32)
    return pl.pallas_call(
        edges_kernel,
        out_shape=(plane, plane),
        in_specs=[vmem] * 3,
        out_specs=(vmem, vmem),
    )(spectrum, edge_mask, depth)


def propagate(spectrum, depth, sea_mask, turning, from_west, from_east, coef, blocks):
    channels, grid_rows, grid_cols = spectrum.shape
    vmem = pl.BlockSpec(memory_space=pltpu.VMEM)
    return pl.pallas_call(
        propagate_kernel,
        out_shape=jax.ShapeDtypeStruct((blocks, grid_rows // blocks * channels, grid_cols), jnp.float32),
        in_specs=[pl.BlockSpec(memory_space=pltpu.SMEM)] + [vmem] * 6,
        out_specs=vmem,
        scratch_shapes=[
            pltpu.VMEM(spectrum.shape, jnp.float32),
            pltpu.VMEM((grid_rows, grid_cols), jnp.float32),
        ],
    )(coef, spectrum, sea_mask, depth, turning, from_west, from_east)


def shards(spectrum, depth_speed, turning, drift, partners, sea_slots, sea_counts):
    channels, grid_rows, grid_cols = spectrum.shape
    n_spec = lax.axis_size("spec")
    sub_rows = grid_rows // n_spec
    per_block = sub_rows * grid_cols
    sea_list = sea_slots[:, 0, :]
    sea_mask = sea_cells(sea_list, sea_counts[:, 0], per_block).reshape(grid_rows, grid_cols)
    edge_mask = edge_cells(sea_list, sea_counts[:, 0], sub_rows, grid_cols)
    edges_first, edges_last = edges(spectrum, edge_mask, depth_speed)
    from_west, from_east = neighbours(edges_first, edges_last)
    local_freq = channels // ND
    freq_ids = (
        lax.axis_index("spec") * local_freq + jnp.arange(local_freq, dtype=jnp.int32)
    ).astype(jnp.float32)
    speeds = jnp.repeat(speed_top * jnp.exp(-decline * freq_ids), ND)
    angles = 2.0 * jnp.pi * jnp.arange(ND, dtype=jnp.float32) / ND
    cosines = jnp.tile(jnp.cos(angles), local_freq)
    sine_part = jnp.tile(jnp.sin(angles), local_freq)
    coef = jnp.stack([speeds * cosines, speeds * sine_part])
    turned = propagate(
        spectrum, depth_speed, sea_mask, turning, from_west, from_east, coef, n_spec
    )
    points = lax.all_to_all(turned, "spec", split_axis=0, concat_axis=0, tiled=True)
    return settle(points, drift, partners)


def solution(mesh):
    return jax.shard_map(
        shards,
        mesh=mesh,
        in_specs=(
            P("spec", None, "tile"),
            P(None, "tile"),
            P(None, "tile"),
            P(),
            P(),
            P(None, "tile", None),
            P(None, "tile"),
        ),
        out_specs=P(None, "spec", "tile"),
        check_vma=False,
    )
```
